32 devices in a mesh: axial: 8 (over y, x, core), radial: 4 (over z).
Axes of the slice: x: 2, y: 2, z: 4, core: 2. Of those that a mesh axis runs over, the one named last changes fastest.
Arguments:
- composition_deviations: float32 [38, 1024, 512], P(None, 'axial', 'radial'), may hold values from -6 to 6
- flow_speed_vector: float32 [2, 1024, 512], P(None, 'axial', 'radial'), may hold values from -1 to 1
- thermal_field: float32 [1024, 512], P('axial', 'radial'), may hold values from 0.4 to 4
- linearized_kinetics_operator: float32 [38, 38], replicated, may hold values from -0.5 to 0.5
- frozen_jacobian_inverse_addend: float32 [38, 38], replicated, may hold values from -0.25 to 0.25
- rigid_block_indicator: int32 [512, 4], P('axial', 'radial'), may hold values from 0 to 1, as said below
- molar_absorptivity_table: float32 [4, 38], replicated, may hold values from -1 to 1
- spokewise_sightline_length: float32 [512], P('radial'), may hold values from 0.3 to 3
- sightline_lengthwise_index: int32 [4, 32768], replicated, may hold values from 0 to 1023
- observed_absorbance_traces: float32 [4, 32768], P(None, ('axial', 'radial')), may hold values from -6 to 6
Outputs:
- species_out: float32 [38, 1024, 512], P(None, 'axial', 'radial')
- misfit: float32 [4, 32768], P(None, ('axial', 'radial'))
The draws below stay inside these ranges and needn't reach their ends.
Inputs may be any that keep to these rules, and one draw needn't show every extreme that they name: `rigid_block_indicator`: in each radial column of tiles, the tiles of 2 cyclically consecutive axial devices are all stiff and every other axial device holds exactly 8 stiff tiles, so the column holds 176 stiff tiles.
All inputs are finite; a program needn't handle non-finite values.
Results may differ from the reference program's by a relative error of at most 0.0001.
Values sent between devices are 32-bit elements; how exact they have to be, the bound alone decides.
No kernel may reach another device: no remote copies, remote signals or barrier semaphores. Data moves between devices by JAX's collectives and lax.ppermute only.
A program may use at most 192 MiB of HBM per device.

```python
import math
import jax
import jax.numpy as jnp
from jax import lax

NS = 38
LASERS = 4
CR = 128
TILE_ROWS = 2
ITERS = 3
TILES_DEV = 64
LENGTHWISE_BINS = 1024
SPOKEWISE_BINS = 512
NSAMP = 32768
N_AXIAL = 8
N_RADIAL = 4


def draw_rigid_block_indicator(key, part):
    band_key = jax.random.fold_in(key, 11)
    score_key = jax.random.fold_in(key, 23)
    band_start = jax.random.randint(band_key, (1, N_RADIAL, 1), 0, N_AXIAL)
    members = jnp.arange(N_AXIAL, dtype=jnp.int32).reshape(N_AXIAL, 1, 1)
    in_band = (members - band_start) % N_AXIAL < N_AXIAL // 4
    scores = jax.random.randint(score_key, (N_AXIAL, N_RADIAL, TILES_DEV), 0, 1 << 20) * TILES_DEV + jnp.arange(TILES_DEV, dtype=jnp.int32)
    tile_ranks = jnp.argsort(jnp.argsort(scores, axis=2), axis=2)
    stiff_tiles = in_band | (tile_ranks < TILES_DEV // 8)
    return jnp.transpose(stiff_tiles.astype(jnp.int32), (0, 2, 1)).reshape(N_AXIAL * TILES_DEV, N_RADIAL)


def set_ends(array, rng, low, high):
    longest = array.shape.index(max(array.shape))
    spots = []
    for shift in (0, 1):
        where = [jax.random.randint(jax.random.fold_in(rng, axis), (), 0, length) for axis, length in enumerate(array.shape)]
        where[longest] = (where[longest] + shift) % array.shape[longest]
        spots.append(tuple(where))
    return array.at[spots[0]].set(low).at[spots[1]].set(high)


def levels(rng, shape, pieces, smallest, top_value):
    factor_of, own = 1.0, jax.random.fold_in(rng, 6)
    for dim, shards_of in pieces:
        steps = jnp.exp(jax.random.uniform(jax.random.fold_in(own, dim), (shards_of,), jnp.float32, smallest / len(pieces), top_value / len(pieces)))
        factor_of = factor_of * jnp.repeat(steps, shape[dim] // shards_of).reshape([-1 if axis == dim else 1 for axis in range(len(shape))])
    return factor_of


def noise(key, extent, width, reach, split=(), held_as=jnp.bfloat16):
    values = width * jax.random.normal(key, extent, jnp.float32)
    if split:
        values = values * levels(key, extent, split, -0.22, 0.18)
    return jnp.clip(values, -reach, reach).astype(held_as)


def setup_inputs(seed: int = 0) -> dict:
    seeds = jax.random.split(jax.random.key(seed), 11)
    composition_deviations = noise(seeds[0], (NS, LENGTHWISE_BINS, SPOKEWISE_BINS), 1.0, 6.0, ((1, 8), (2, 4)), jnp.float32)
    flow_speed_vector = jnp.clip(jax.random.uniform(seeds[1], (2, LENGTHWISE_BINS, SPOKEWISE_BINS), jnp.float32, -1.0, 1.0) * levels(seeds[1], (2, LENGTHWISE_BINS, SPOKEWISE_BINS), ((1, 8), (2, 4)), -0.4, 0.0), -1.0, 1.0)
    thermal_field = jnp.clip(jnp.exp(math.log(4.0) - 2.3025851 * jax.random.uniform(seeds[2], (LENGTHWISE_BINS, SPOKEWISE_BINS), jnp.float32) ** levels(seeds[2], (LENGTHWISE_BINS, SPOKEWISE_BINS), ((0, 8), (1, 4)), -0.2, 0.2)), 0.4, 4.0)
    linearized_kinetics_operator = noise(seeds[3], (NS, NS), (4 * NS) ** -0.5, 0.5, (), jnp.float32)
    frozen_jacobian_inverse_addend = noise(seeds[4], (NS, NS), (16 * NS) ** -0.5, 0.25, (), jnp.float32)
    rigid_block_indicator = draw_rigid_block_indicator(jax.random.fold_in(seeds[10], 71), 0)
    molar_absorptivity_table = noise(seeds[6], (LASERS, NS), NS ** -0.5, 1.0, (), jnp.float32)
    spokewise_sightline_length = jnp.clip(jnp.exp(math.log(3.0) - 2.3025851 * jax.random.uniform(seeds[7], (SPOKEWISE_BINS,), jnp.float32) ** levels(seeds[7], (SPOKEWISE_BINS,), ((0, 4),), -0.2, 0.2)), 0.3, 3.0)
    sightline_lengthwise_index = set_ends(jax.random.randint(seeds[8], (LASERS, NSAMP), 0, LENGTHWISE_BINS), jax.random.fold_in(seeds[8], 1), 0, LENGTHWISE_BINS - 1).astype(jnp.int32)
    observed_absorbance_traces = noise(seeds[9], (LASERS, NSAMP), 1.0, 6.0, ((1, 32),), jnp.float32)
    return {"composition_deviations": composition_deviations, "flow_speed_vector": flow_speed_vector, "thermal_field": thermal_field, "linearized_kinetics_operator": linearized_kinetics_operator, "frozen_jacobian_inverse_addend": frozen_jacobian_inverse_addend, "rigid_block_indicator": rigid_block_indicator, "molar_absorptivity_table": molar_absorptivity_table, "spokewise_sightline_length": spokewise_sightline_length, "sightline_lengthwise_index": sightline_lengthwise_index, "observed_absorbance_traces": observed_absorbance_traces}


TIME_STEP = 0.4
CHEM_STEP = 0.5
ARRHENIUS_BARRIER = 1.0
WENO_EPS = 1e-06
HIGHEST = lax.Precision.HIGHEST

def weno_side(minus_two, minus_one, centre, plus_one, plus_two):
    beta_zero = 13.0 / 12.0 * (minus_two - 2.0 * minus_one + centre) ** 2 + 0.25 * (minus_two - 4.0 * minus_one + 3.0 * centre) ** 2
    beta_one = 13.0 / 12.0 * (minus_one - 2.0 * centre + plus_one) ** 2 + 0.25 * (minus_one - plus_one) ** 2
    beta_two = 13.0 / 12.0 * (centre - 2.0 * plus_one + plus_two) ** 2 + 0.25 * (3.0 * centre - 4.0 * plus_one + plus_two) ** 2
    weight_zero = 0.1 / (WENO_EPS + beta_zero) ** 2
    weight_one = 0.6 / (WENO_EPS + beta_one) ** 2
    weight_two = 0.3 / (WENO_EPS + beta_two) ** 2
    weight_total = weight_zero + weight_one + weight_two
    blended = weight_zero * (2.0 * minus_two - 7.0 * minus_one + 11.0 * centre)
    blended = blended + weight_one * (-minus_one + 5.0 * centre + 2.0 * plus_one)
    blended = blended + weight_two * (2.0 * centre + 5.0 * plus_one - plus_two)
    return blended / (6.0 * weight_total)

def face_difference(field, speed, along, length):
    face_count = length + 1

    def cut_part(offset):
        return lax.slice_in_dim(field, offset, offset + face_count, axis=along)
    left_value = weno_side(cut_part(0), cut_part(1), cut_part(2), cut_part(3), cut_part(4))
    right_value = weno_side(cut_part(5), cut_part(4), cut_part(3), cut_part(2), cut_part(1))
    face_speed = 0.5 * (lax.slice_in_dim(speed, 2, 2 + face_count, axis=along) + lax.slice_in_dim(speed, 3, 3 + face_count, axis=along))
    face_flux = jnp.maximum(face_speed, 0.0) * left_value + jnp.minimum(face_speed, 0.0) * right_value
    return lax.slice_in_dim(face_flux, 1, face_count, axis=along) - lax.slice_in_dim(face_flux, 0, face_count - 1, axis=along)

def transport(field_pad, speed_pad):
    row_count = field_pad.shape[1] - 6
    col_count = field_pad.shape[2] - 6
    along_axial = face_difference(field_pad[:, :, 3:-3], speed_pad[0:1, :, 3:-3], 1, row_count)
    along_radial = face_difference(field_pad[:, 3:-3, :], speed_pad[1:2, 3:-3, :], 2, col_count)
    return field_pad[:, 3:-3, 3:-3] - TIME_STEP * (along_axial + along_radial)

def kinetics_advance(starting_composition_field, thermal_field, linearized_kinetics_operator, frozen_jacobian_inverse_addend):
    acceleration_factor = jnp.exp(-ARRHENIUS_BARRIER / thermal_field)
    current = starting_composition_field
    for newton_step in range(ITERS):
        source = jnp.tensordot(linearized_kinetics_operator, current, axes=(1, 0), precision=HIGHEST) - jnp.tanh(current)
        defect = current - starting_composition_field - CHEM_STEP * acceleration_factor * source
        current = current - defect - jnp.tensordot(frozen_jacobian_inverse_addend, defect, axes=(1, 0), precision=HIGHEST)
    return current

def absorbance_profile(field, molar_absorptivity_table, spokewise_sightline_length):
    mixed = jnp.tensordot(molar_absorptivity_table, field, axes=(1, 0), precision=HIGHEST)
    return jnp.dot(mixed, spokewise_sightline_length, precision=HIGHEST)

def reference(composition_deviations, flow_speed_vector, thermal_field, linearized_kinetics_operator, frozen_jacobian_inverse_addend, rigid_block_indicator, molar_absorptivity_table, spokewise_sightline_length, sightline_lengthwise_index, observed_absorbance_traces):
    speed_pad = jnp.pad(flow_speed_vector, ((0, 0), (3, 3), (3, 3)))

    def advect_one(one_field):
        return transport(jnp.pad(one_field[None], ((0, 0), (3, 3), (3, 3))), speed_pad)[0]
    advected_composition_field = lax.map(advect_one, composition_deviations)
    combusted_composition_field = kinetics_advance(advected_composition_field, thermal_field, linearized_kinetics_operator, frozen_jacobian_inverse_addend)
    flag_cells = jnp.repeat(jnp.repeat(rigid_block_indicator, TILE_ROWS, axis=0), CR, axis=1)
    species_out = jnp.where(flag_cells[None] > 0, combusted_composition_field, advected_composition_field)
    path_scale = 1.0 / math.sqrt(SPOKEWISE_BINS)
    profile = absorbance_profile(species_out, molar_absorptivity_table, spokewise_sightline_length) * path_scale
    values = jnp.take_along_axis(profile, sightline_lengthwise_index, axis=1)
    return (species_out, values - observed_absorbance_traces)
```

```python
import math

import jax
import jax.numpy as jnp
from jax import lax
from jax.sharding import PartitionSpec as P

TILE_ROWS = 2
ITERS = 3


TIME_STEP = 0.4
CHEM_STEP = 0.5
ARRHENIUS_BARRIER = 1.0
WENO_EPS = 1e-06
HIGHEST = lax.Precision.HIGHEST


def extended(shard, sides, width):
    for axis, dim in sides:
        peers, length = (lax.axis_size(axis), shard.shape[dim])
        up = [(i, (i + 1) % peers) for i in range(peers - 1)]
        down = [(j, i) for i, j in up]
        last = lax.slice_in_dim(shard, length - width, length, axis=dim)
        initial = lax.slice_in_dim(shard, 0, width, axis=dim)
        before = lax.ppermute(last, axis, up)
        after = lax.ppermute(initial, axis, down)
        shard = jnp.concatenate([before, shard, after], axis=dim)
    return shard


def weno_side(minus_two, minus_one, centre, plus_one, plus_two):
    beta_zero = (
        13.0 / 12.0 * (minus_two - 2.0 * minus_one + centre) ** 2
        + 0.25 * (minus_two - 4.0 * minus_one + 3.0 * centre) ** 2
    )
    beta_one = (
        13.0 / 12.0 * (minus_one - 2.0 * centre + plus_one) ** 2
        + 0.25 * (minus_one - plus_one) ** 2
    )
    beta_two = (
        13.0 / 12.0 * (centre - 2.0 * plus_one + plus_two) ** 2
        + 0.25 * (3.0 * centre - 4.0 * plus_one + plus_two) ** 2
    )
    weight_zero = 0.1 / (WENO_EPS + beta_zero) ** 2
    weight_one = 0.6 / (WENO_EPS + beta_one) ** 2
    weight_two = 0.3 / (WENO_EPS + beta_two) ** 2
    weight_total = weight_zero + weight_one + weight_two
    blended = weight_zero * (2.0 * minus_two - 7.0 * minus_one + 11.0 * centre)
    blended = blended + weight_one * (-minus_one + 5.0 * centre + 2.0 * plus_one)
    blended = blended + weight_two * (2.0 * centre + 5.0 * plus_one - plus_two)
    return blended / (6.0 * weight_total)


def face_difference(field, speed, along, length):
    face_count = length + 1

    def cut_part(offset):
        return lax.slice_in_dim(field, offset, offset + face_count, axis=along)

    left_value = weno_side(cut_part(0), cut_part(1), cut_part(2), cut_part(3), cut_part(4))
    right_value = weno_side(cut_part(5), cut_part(4), cut_part(3), cut_part(2), cut_part(1))
    face_speed = 0.5 * (
        lax.slice_in_dim(speed, 2, 2 + face_count, axis=along)
        + lax.slice_in_dim(speed, 3, 3 + face_count, axis=along)
    )
    face_flux = (
        jnp.maximum(face_speed, 0.0) * left_value + jnp.minimum(face_speed, 0.0) * right_value
    )
    return lax.slice_in_dim(face_flux, 1, face_count, axis=along) - lax.slice_in_dim(
        face_flux, 0, face_count - 1, axis=along
    )


def transport(field_pad, speed_pad):
    row_count = field_pad.shape[1] - 6
    col_count = field_pad.shape[2] - 6
    along_axial = face_difference(field_pad[:, :, 3:-3], speed_pad[0:1, :, 3:-3], 1, row_count)
    along_radial = face_difference(field_pad[:, 3:-3, :], speed_pad[1:2, 3:-3, :], 2, col_count)
    return field_pad[:, 3:-3, 3:-3] - TIME_STEP * (along_axial + along_radial)


def kinetics_advance(
    starting_composition_field,
    thermal_field,
    linearized_kinetics_operator,
    frozen_jacobian_inverse_addend,
):
    acceleration_factor = jnp.exp(-ARRHENIUS_BARRIER / thermal_field)
    current = starting_composition_field
    for newton_step in range(ITERS):
        source = jnp.tensordot(
            linearized_kinetics_operator, current, axes=(1, 0), precision=HIGHEST
        ) - jnp.tanh(current)
        defect = current - starting_composition_field - CHEM_STEP * acceleration_factor * source
        current = (
            current
            - defect
            - jnp.tensordot(frozen_jacobian_inverse_addend, defect, axes=(1, 0), precision=HIGHEST)
        )
    return current


def absorbance_profile(field, molar_absorptivity_table, spokewise_sightline_length):
    mixed = jnp.tensordot(molar_absorptivity_table, field, axes=(1, 0), precision=HIGHEST)
    return jnp.dot(mixed, spokewise_sightline_length, precision=HIGHEST)


def local(
    composition_deviations,
    flow_speed_vector,
    thermal_field,
    linearized_kinetics_operator,
    frozen_jacobian_inverse_addend,
    rigid_block_indicator,
    molar_absorptivity_table,
    spokewise_sightline_length,
    sightline_lengthwise_index,
    observed_absorbance_traces,
):
    species_count = composition_deviations.shape[0]
    stacked = jnp.concatenate([composition_deviations, flow_speed_vector], axis=0)
    padded = extended(stacked, (("axial", 1), ("radial", 2)), 3)
    advected_composition_field = transport(padded[:species_count], padded[species_count:])
    combusted_composition_field = kinetics_advance(
        advected_composition_field,
        thermal_field,
        linearized_kinetics_operator,
        frozen_jacobian_inverse_addend,
    )
    flag_cells = jnp.repeat(
        jnp.repeat(rigid_block_indicator, TILE_ROWS, axis=0),
        advected_composition_field.shape[2],
        axis=1,
    )
    species_out = jnp.where(
        flag_cells[None] > 0, combusted_composition_field, advected_composition_field
    )
    path_scale = 1.0 / math.sqrt(advected_composition_field.shape[2] * lax.axis_size("radial"))
    profile = (
        absorbance_profile(species_out, molar_absorptivity_table, spokewise_sightline_length)
        * path_scale
    )
    axial_count, radial_count = (lax.axis_size("axial"), lax.axis_size("radial"))
    parts = lax.all_gather(profile, ("axial", "radial"), axis=0)
    parts = parts.reshape((axial_count, radial_count) + profile.shape).sum(axis=1)
    whole_profile = jnp.transpose(parts, (1, 0, 2)).reshape(profile.shape[0], -1)
    device = lax.axis_index(("axial", "radial"))
    sample_count = observed_absorbance_traces.shape[1]
    own_rows = lax.dynamic_slice_in_dim(
        sightline_lengthwise_index, device * sample_count, sample_count, 1
    )
    cells = lax.broadcasted_iota(jnp.int32, (1, whole_profile.shape[1], 1), 1)
    values = jnp.sum(
        jnp.where(own_rows[:, None, :] == cells, whole_profile[:, :, None], 0.0), axis=1
    )
    return (species_out, values - observed_absorbance_traces)


def solution(mesh):
    in_specs = (
        P(None, "axial", "radial"),
        P(None, "axial", "radial"),
        P("axial", "radial"),
        P(),
        P(),
        P("axial", "radial"),
        P(),
        P("radial"),
        P(),
        P(None, ("axial", "radial")),
    )
    out_specs = (P(None, "axial", "radial"), P(None, ("axial", "radial")))
    return jax.shard_map(local, mesh=mesh, in_specs=in_specs, out_specs=out_specs, check_vma=False)
```

```python
import math

import jax
import jax.numpy as jnp
from jax import lax
from jax.sharding import PartitionSpec as P

TILE_ROWS = 2
ITERS = 3


TIME_STEP = 0.4
CHEM_STEP = 0.5
ARRHENIUS_BARRIER = 1.0
WENO_EPS = 1e-06
HIGHEST = lax.Precision.HIGHEST


def extended(shard, sides, width):
    for axis, dim in sides:
        peers, length = (lax.axis_size(axis), shard.shape[dim])
        up = [(i, (i + 1) % peers) for i in range(peers - 1)]
        down = [(j, i) for i, j in up]
        last = lax.slice_in_dim(shard, length - width, length, axis=dim)
        initial = lax.slice_in_dim(shard, 0, width, axis=dim)
        before = lax.ppermute(last, axis, up)
        after = lax.ppermute(initial, axis, down)
        shard = jnp.concatenate([before, shard, after], axis=dim)
    return shard


def weno_side(minus_two, minus_one, centre, plus_one, plus_two):
    curve_zero = minus_two - 2.0 * minus_one + centre
    curve_one = minus_one - 2.0 * centre + plus_one
    curve_two = centre - 2.0 * plus_one + plus_two
    slope_zero = minus_two - 4.0 * minus_one + 3.0 * centre
    slope_one = minus_one - plus_one
    slope_two = 3.0 * centre - 4.0 * plus_one + plus_two
    beta_zero = 13.0 / 12.0 * curve_zero * curve_zero + 0.25 * slope_zero * slope_zero
    beta_one = 13.0 / 12.0 * curve_one * curve_one + 0.25 * slope_one * slope_one
    beta_two = 13.0 / 12.0 * curve_two * curve_two + 0.25 * slope_two * slope_two
    guard_zero = WENO_EPS + beta_zero
    guard_one = WENO_EPS + beta_one
    guard_two = WENO_EPS + beta_two
    guard_zero = guard_zero * guard_zero
    guard_one = guard_one * guard_one
    guard_two = guard_two * guard_two
    cross_zero = guard_one * guard_two
    cross_one = 6.0 * (guard_zero * guard_two)
    cross_two = 3.0 * (guard_zero * guard_one)
    blended = cross_zero * (2.0 * minus_two - 7.0 * minus_one + 11.0 * centre)
    blended = blended + cross_one * (-minus_one + 5.0 * centre + 2.0 * plus_one)
    blended = blended + cross_two * (2.0 * centre + 5.0 * plus_one - plus_two)
    return blended / (6.0 * (cross_zero + cross_one + cross_two))


def face_difference(field, speed, along, length):
    face_count = length + 1

    def cut_part(offset):
        return lax.slice_in_dim(field, offset, offset + face_count, axis=along)

    face_speed = 0.5 * (
        lax.slice_in_dim(speed, 2, 2 + face_count, axis=along)
        + lax.slice_in_dim(speed, 3, 3 + face_count, axis=along)
    )
    forward = face_speed >= 0.0
    stencil = [
        jnp.where(forward, cut_part(low), cut_part(high))
        for low, high in ((0, 5), (1, 4), (2, 3), (3, 2), (4, 1))
    ]
    face_flux = face_speed * weno_side(*stencil)
    return lax.slice_in_dim(face_flux, 1, face_count, axis=along) - lax.slice_in_dim(
        face_flux, 0, face_count - 1, axis=along
    )


def transport(field_pad, speed_pad):
    row_count = field_pad.shape[1] - 6
    col_count = field_pad.shape[2] - 6
    along_axial = face_difference(field_pad[:, :, 3:-3], speed_pad[0:1, :, 3:-3], 1, row_count)
    along_radial = face_difference(field_pad[:, 3:-3, :], speed_pad[1:2, 3:-3, :], 2, col_count)
    return field_pad[:, 3:-3, 3:-3] - TIME_STEP * (along_axial + along_radial)


def kinetics_advance(
    starting_composition_field,
    thermal_field,
    linearized_kinetics_operator,
    frozen_jacobian_inverse_addend,
):
    acceleration_factor = jnp.exp(-ARRHENIUS_BARRIER / thermal_field)
    current = starting_composition_field
    for newton_step in range(ITERS):
        source = jnp.tensordot(
            linearized_kinetics_operator, current, axes=(1, 0), precision=HIGHEST
        ) - jnp.tanh(current)
        defect = current - starting_composition_field - CHEM_STEP * acceleration_factor * source
        current = (
            current
            - defect
            - jnp.tensordot(frozen_jacobian_inverse_addend, defect, axes=(1, 0), precision=HIGHEST)
        )
    return current


def absorbance_profile(field, molar_absorptivity_table, spokewise_sightline_length):
    mixed = jnp.tensordot(molar_absorptivity_table, field, axes=(1, 0), precision=HIGHEST)
    return jnp.dot(mixed, spokewise_sightline_length, precision=HIGHEST)


def butterfly_sum(part, axis):
    peers, stride = (lax.axis_size(axis), 1)
    if peers & (peers - 1):
        return lax.psum(part, axis)
    while stride < peers:
        pairs = [(j, j ^ stride) for j in range(peers)]
        part = part + lax.ppermute(part, axis, pairs)
        stride *= 2
    return part


def doubling_gather(part, axis):
    peers, stride = (lax.axis_size(axis), 1)
    if peers & (peers - 1):
        return lax.all_gather(part, axis, axis=1, tiled=True)
    position = lax.axis_index(axis)
    blocks = part[None]
    while stride < peers:
        pairs = [(j, j ^ stride) for j in range(peers)]
        other = lax.ppermute(blocks, axis, pairs)
        upper = (position // stride) % 2 == 1
        blocks = jnp.where(
            upper, jnp.concatenate([other, blocks], 0), jnp.concatenate([blocks, other], 0)
        )
        stride *= 2
    return jnp.transpose(blocks, (1, 0, 2)).reshape(part.shape[0], -1)


def gathered_profile(profile):
    return doubling_gather(butterfly_sum(profile, "radial"), "axial")


def local(
    composition_deviations,
    flow_speed_vector,
    thermal_field,
    linearized_kinetics_operator,
    frozen_jacobian_inverse_addend,
    rigid_block_indicator,
    molar_absorptivity_table,
    spokewise_sightline_length,
    sightline_lengthwise_index,
    observed_absorbance_traces,
):
    species_count = composition_deviations.shape[0]
    stacked = jnp.concatenate([composition_deviations, flow_speed_vector], axis=0)
    padded = extended(stacked, (("axial", 1), ("radial", 2)), 3)
    advected_composition_field = transport(padded[:species_count], padded[species_count:])
    combusted_composition_field = kinetics_advance(
        advected_composition_field,
        thermal_field,
        linearized_kinetics_operator,
        frozen_jacobian_inverse_addend,
    )
    flag_cells = jnp.repeat(
        jnp.repeat(rigid_block_indicator, TILE_ROWS, axis=0),
        advected_composition_field.shape[2],
        axis=1,
    )
    species_out = jnp.where(
        flag_cells[None] > 0, combusted_composition_field, advected_composition_field
    )
    path_scale = 1.0 / math.sqrt(advected_composition_field.shape[2] * lax.axis_size("radial"))
    profile = (
        absorbance_profile(species_out, molar_absorptivity_table, spokewise_sightline_length)
        * path_scale
    )
    whole_profile = gathered_profile(profile)
    device = lax.axis_index(("axial", "radial"))
    sample_count = observed_absorbance_traces.shape[1]
    own_rows = lax.dynamic_slice_in_dim(
        sightline_lengthwise_index, device * sample_count, sample_count, 1
    )
    cells = lax.broadcasted_iota(jnp.int32, (1, whole_profile.shape[1], 1), 1)
    values = jnp.sum(
        jnp.where(own_rows[:, None, :] == cells, whole_profile[:, :, None], 0.0), axis=1
    )
    return (species_out, values - observed_absorbance_traces)


def solution(mesh):
    in_specs = (
        P(None, "axial", "radial"),
        P(None, "axial", "radial"),
        P("axial", "radial"),
        P(),
        P(),
        P("axial", "radial"),
        P(),
        P("radial"),
        P(),
        P(None, ("axial", "radial")),
    )
    out_specs = (P(None, "axial", "radial"), P(None, ("axial", "radial")))
    return jax.shard_map(local, mesh=mesh, in_specs=in_specs, out_specs=out_specs, check_vma=False)
```

```python
import math

import jax
import jax.numpy as jnp
from jax import lax
from jax.sharding import PartitionSpec as P

TILE_ROWS = 2
ITERS = 3


TIME_STEP = 0.4
CHEM_STEP = 0.5
ARRHENIUS_BARRIER = 1.0
WENO_EPS = 1e-06
HIGHEST = lax.Precision.HIGHEST


def edge_layers(shard, axis, dim, width):
    peers, length = (lax.axis_size(axis), shard.shape[dim])
    up = [(i, i + 1) for i in range(peers - 1)]
    down = [(j, i) for i, j in up]
    last = lax.slice_in_dim(shard, length - width, length, axis=dim)
    initial = lax.slice_in_dim(shard, 0, width, axis=dim)
    return lax.ppermute(last, axis, up), lax.ppermute(initial, axis, down)


def weno_side(minus_two, minus_one, centre, plus_one, plus_two):
    curve_zero = minus_two - 2.0 * minus_one + centre
    curve_one = minus_one - 2.0 * centre + plus_one
    curve_two = centre - 2.0 * plus_one + plus_two
    slope_zero = minus_two - 4.0 * minus_one + 3.0 * centre
    slope_one = minus_one - plus_one
    slope_two = 3.0 * centre - 4.0 * plus_one + plus_two
    beta_zero = 13.0 / 12.0 * curve_zero * curve_zero + 0.25 * slope_zero * slope_zero
    beta_one = 13.0 / 12.0 * curve_one * curve_one + 0.25 * slope_one * slope_one
    beta_two = 13.0 / 12.0 * curve_two * curve_two + 0.25 * slope_two * slope_two
    guard_zero = WENO_EPS + beta_zero
    guard_one = WENO_EPS + beta_one
    guard_two = WENO_EPS + beta_two
    guard_zero = guard_zero * guard_zero
    guard_one = guard_one * guard_one
    guard_two = guard_two * guard_two
    cross_zero = guard_one * guard_two
    cross_one = 6.0 * (guard_zero * guard_two)
    cross_two = 3.0 * (guard_zero * guard_one)
    blended = cross_zero * (2.0 * minus_two - 7.0 * minus_one + 11.0 * centre)
    blended = blended + cross_one * (-minus_one + 5.0 * centre + 2.0 * plus_one)
    blended = blended + cross_two * (2.0 * centre + 5.0 * plus_one - plus_two)
    return blended / (6.0 * (cross_zero + cross_one + cross_two))


def face_difference(field, speed, along, length):
    face_count = length + 1

    def cut_part(offset):
        return lax.slice_in_dim(field, offset, offset + face_count, axis=along)

    face_speed = 0.5 * (
        lax.slice_in_dim(speed, 2, 2 + face_count, axis=along)
        + lax.slice_in_dim(speed, 3, 3 + face_count, axis=along)
    )
    forward = face_speed >= 0.0
    stencil = [
        jnp.where(forward, cut_part(low), cut_part(high))
        for low, high in ((0, 5), (1, 4), (2, 3), (3, 2), (4, 1))
    ]
    face_flux = face_speed * weno_side(*stencil)
    return lax.slice_in_dim(face_flux, 1, face_count, axis=along) - lax.slice_in_dim(
        face_flux, 0, face_count - 1, axis=along
    )


def transport(species, speed, width=3):
    species_count = species.shape[0]
    along = []
    for component, (axis, dim) in enumerate((("axial", 1), ("radial", 2))):
        edges = jnp.concatenate([species, speed[component : component + 1]], axis=0)
        before, after = edge_layers(edges, axis, dim, width)
        field = jnp.concatenate([before[:species_count], species, after[:species_count]], axis=dim)
        velocity = jnp.concatenate(
            [before[species_count:], speed[component : component + 1], after[species_count:]],
            axis=dim,
        )
        along.append(face_difference(field, velocity, dim, species.shape[dim]))
    return species - TIME_STEP * (along[0] + along[1])


def kinetics_advance(
    starting_composition_field,
    thermal_field,
    linearized_kinetics_operator,
    frozen_jacobian_inverse_addend,
):
    acceleration_factor = jnp.exp(-ARRHENIUS_BARRIER / thermal_field)
    current = starting_composition_field
    for newton_step in range(ITERS):
        source = jnp.tensordot(
            linearized_kinetics_operator, current, axes=(1, 0), precision=HIGHEST
        ) - jnp.tanh(current)
        defect = current - starting_composition_field - CHEM_STEP * acceleration_factor * source
        current = (
            current
            - defect
            - jnp.tensordot(frozen_jacobian_inverse_addend, defect, axes=(1, 0), precision=HIGHEST)
        )
    return current


def absorbance_profile(field, molar_absorptivity_table, spokewise_sightline_length):
    mixed = jnp.tensordot(molar_absorptivity_table, field, axes=(1, 0), precision=HIGHEST)
    return jnp.dot(mixed, spokewise_sightline_length, precision=HIGHEST)


def butterfly_sum(part, axis):
    peers, stride = (lax.axis_size(axis), 1)
    if peers & (peers - 1):
        return lax.psum(part, axis)
    while stride < peers:
        pairs = [(j, j ^ stride) for j in range(peers)]
        part = part + lax.ppermute(part, axis, pairs)
        stride *= 2
    return part


def doubling_gather(part, axis):
    peers, stride = (lax.axis_size(axis), 1)
    if peers & (peers - 1):
        return lax.all_gather(part, axis, axis=1, tiled=True)
    position = lax.axis_index(axis)
    blocks = part[None]
    while stride < peers:
        pairs = [(j, j ^ stride) for j in range(peers)]
        other = lax.ppermute(blocks, axis, pairs)
        upper = (position // stride) % 2 == 1
        blocks = jnp.where(
            upper, jnp.concatenate([other, blocks], 0), jnp.concatenate([blocks, other], 0)
        )
        stride *= 2
    return jnp.transpose(blocks, (1, 0, 2)).reshape(part.shape[0], -1)


def gathered_profile(profile):
    return doubling_gather(butterfly_sum(profile, "radial"), "axial")


def local(
    composition_deviations,
    flow_speed_vector,
    thermal_field,
    linearized_kinetics_operator,
    frozen_jacobian_inverse_addend,
    rigid_block_indicator,
    molar_absorptivity_table,
    spokewise_sightline_length,
    sightline_lengthwise_index,
    observed_absorbance_traces,
):
    advected_composition_field = transport(composition_deviations, flow_speed_vector)
    combusted_composition_field = kinetics_advance(
        advected_composition_field,
        thermal_field,
        linearized_kinetics_operator,
        frozen_jacobian_inverse_addend,
    )
    flag_cells = jnp.repeat(
        jnp.repeat(rigid_block_indicator, TILE_ROWS, axis=0),
        advected_composition_field.shape[2],
        axis=1,
    )
    species_out = jnp.where(
        flag_cells[None] > 0, combusted_composition_field, advected_composition_field
    )
    path_scale = 1.0 / math.sqrt(advected_composition_field.shape[2] * lax.axis_size("radial"))
    profile = (
        absorbance_profile(species_out, molar_absorptivity_table, spokewise_sightline_length)
        * path_scale
    )
    whole_profile = gathered_profile(profile)
    device = lax.axis_index(("axial", "radial"))
    sample_count = observed_absorbance_traces.shape[1]
    own_rows = lax.dynamic_slice_in_dim(
        sightline_lengthwise_index, device * sample_count, sample_count, 1
    )
    cells = lax.broadcasted_iota(jnp.int32, (1, whole_profile.shape[1], 1), 1)
    values = jnp.sum(
        jnp.where(own_rows[:, None, :] == cells, whole_profile[:, :, None], 0.0), axis=1
    )
    return (species_out, values - observed_absorbance_traces)


def solution(mesh):
    in_specs = (
        P(None, "axial", "radial"),
        P(None, "axial", "radial"),
        P("axial", "radial"),
        P(),
        P(),
        P("axial", "radial"),
        P(),
        P("radial"),
        P(),
        P(None, ("axial", "radial")),
    )
    out_specs = (P(None, "axial", "radial"), P(None, ("axial", "radial")))
    return jax.shard_map(local, mesh=mesh, in_specs=in_specs, out_specs=out_specs, check_vma=False)
```

```python
import math

import jax
import jax.numpy as jnp
from jax import lax
from jax.sharding import PartitionSpec as P

TILE_ROWS = 2
ITERS = 3


TIME_STEP = 0.4
CHEM_STEP = 0.5
ARRHENIUS_BARRIER = 1.0
WENO_EPS = 1e-06
HIGHEST = lax.Precision.HIGHEST
CHEMISTRY_PRECISION = lax.Precision.HIGH


def edge_layers(shard, axis, dim, width):
    peers, length = (lax.axis_size(axis), shard.shape[dim])
    up = [(i, i + 1) for i in range(peers - 1)]
    down = [(j, i) for i, j in up]
    last = lax.slice_in_dim(shard, length - width, length, axis=dim)
    initial = lax.slice_in_dim(shard, 0, width, axis=dim)
    return lax.ppermute(last, axis, up), lax.ppermute(initial, axis, down)


def weno_side(minus_two, minus_one, centre, plus_one, plus_two):
    curve_zero = minus_two - 2.0 * minus_one + centre
    curve_one = minus_one - 2.0 * centre + plus_one
    curve_two = centre - 2.0 * plus_one + plus_two
    slope_zero = minus_two - 4.0 * minus_one + 3.0 * centre
    slope_one = minus_one - plus_one
    slope_two = 3.0 * centre - 4.0 * plus_one + plus_two
    beta_zero = 13.0 / 12.0 * curve_zero * curve_zero + 0.25 * slope_zero * slope_zero
    beta_one = 13.0 / 12.0 * curve_one * curve_one + 0.25 * slope_one * slope_one
    beta_two = 13.0 / 12.0 * curve_two * curve_two + 0.25 * slope_two * slope_two
    guard_zero = WENO_EPS + beta_zero
    guard_one = WENO_EPS + beta_one
    guard_two = WENO_EPS + beta_two
    guard_zero = guard_zero * guard_zero
    guard_one = guard_one * guard_one
    guard_two = guard_two * guard_two
    cross_zero = guard_one * guard_two
    cross_one = 6.0 * (guard_zero * guard_two)
    cross_two = 3.0 * (guard_zero * guard_one)
    blended = cross_zero * (2.0 * minus_two - 7.0 * minus_one + 11.0 * centre)
    blended = blended + cross_one * (-minus_one + 5.0 * centre + 2.0 * plus_one)
    blended = blended + cross_two * (2.0 * centre + 5.0 * plus_one - plus_two)
    return blended / (6.0 * (cross_zero + cross_one + cross_two))


def face_difference(field, speed, along, length):
    face_count = length + 1

    def cut_part(offset):
        return lax.slice_in_dim(field, offset, offset + face_count, axis=along)

    face_speed = 0.5 * (
        lax.slice_in_dim(speed, 2, 2 + face_count, axis=along)
        + lax.slice_in_dim(speed, 3, 3 + face_count, axis=along)
    )
    forward = face_speed >= 0.0
    stencil = [
        jnp.where(forward, cut_part(low), cut_part(high))
        for low, high in ((0, 5), (1, 4), (2, 3), (3, 2), (4, 1))
    ]
    face_flux = face_speed * weno_side(*stencil)
    return lax.slice_in_dim(face_flux, 1, face_count, axis=along) - lax.slice_in_dim(
        face_flux, 0, face_count - 1, axis=along
    )


def transport(species, speed, width=3):
    species_count = species.shape[0]
    along = []
    for component, (axis, dim) in enumerate((("axial", 1), ("radial", 2))):
        edges = jnp.concatenate([species, speed[component : component + 1]], axis=0)
        before, after = edge_layers(edges, axis, dim, width)
        field = jnp.concatenate([before[:species_count], species, after[:species_count]], axis=dim)
        velocity = jnp.concatenate(
            [before[species_count:], speed[component : component + 1], after[species_count:]],
            axis=dim,
        )
        along.append(face_difference(field, velocity, dim, species.shape[dim]))
    return species - TIME_STEP * (along[0] + along[1])


def kinetics_advance(
    starting_composition_field,
    thermal_field,
    linearized_kinetics_operator,
    frozen_jacobian_inverse_addend,
):
    acceleration_factor = jnp.exp(-ARRHENIUS_BARRIER / thermal_field)
    current = starting_composition_field
    for newton_step in range(ITERS):
        source = jnp.tensordot(
            linearized_kinetics_operator, current, axes=(1, 0), precision=CHEMISTRY_PRECISION
        ) - jnp.tanh(current)
        defect = current - starting_composition_field - CHEM_STEP * acceleration_factor * source
        current = (
            current
            - defect
            - jnp.tensordot(frozen_jacobian_inverse_addend, defect, axes=(1, 0), precision=CHEMISTRY_PRECISION)
        )
    return current


def absorbance_profile(field, molar_absorptivity_table, spokewise_sightline_length):
    mixed = jnp.tensordot(molar_absorptivity_table, field, axes=(1, 0), precision=HIGHEST)
    return jnp.dot(mixed, spokewise_sightline_length, precision=HIGHEST)


def butterfly_sum(part, axis):
    peers, stride = (lax.axis_size(axis), 1)
    if peers & (peers - 1):
        return lax.psum(part, axis)
    while stride < peers:
        pairs = [(j, j ^ stride) for j in range(peers)]
        part = part + lax.ppermute(part, axis, pairs)
        stride *= 2
    return part


def doubling_gather(part, axis):
    peers, stride = (lax.axis_size(axis), 1)
    if peers & (peers - 1):
        return lax.all_gather(part, axis, axis=1, tiled=True)
    position = lax.axis_index(axis)
    blocks = part[None]
    while stride < peers:
        pairs = [(j, j ^ stride) for j in range(peers)]
        other = lax.ppermute(blocks, axis, pairs)
        upper = (position // stride) % 2 == 1
        blocks = jnp.where(
            upper, jnp.concatenate([other, blocks], 0), jnp.concatenate([blocks, other], 0)
        )
        stride *= 2
    return jnp.transpose(blocks, (1, 0, 2)).reshape(part.shape[0], -1)


def gathered_profile(profile):
    return doubling_gather(butterfly_sum(profile, "radial"), "axial")


def local(
    composition_deviations,
    flow_speed_vector,
    thermal_field,
    linearized_kinetics_operator,
    frozen_jacobian_inverse_addend,
    rigid_block_indicator,
    molar_absorptivity_table,
    spokewise_sightline_length,
    sightline_lengthwise_index,
    observed_absorbance_traces,
):
    advected_composition_field = transport(composition_deviations, flow_speed_vector)
    combusted_composition_field = kinetics_advance(
        advected_composition_field,
        thermal_field,
        linearized_kinetics_operator,
        frozen_jacobian_inverse_addend,
    )
    flag_cells = jnp.repeat(
        jnp.repeat(rigid_block_indicator, TILE_ROWS, axis=0),
        advected_composition_field.shape[2],
        axis=1,
    )
    species_out = jnp.where(
        flag_cells[None] > 0, combusted_composition_field, advected_composition_field
    )
    path_scale = 1.0 / math.sqrt(advected_composition_field.shape[2] * lax.axis_size("radial"))
    profile = (
        absorbance_profile(species_out, molar_absorptivity_table, spokewise_sightline_length)
        * path_scale
    )
    whole_profile = gathered_profile(profile)
    device = lax.axis_index(("axial", "radial"))
    sample_count = observed_absorbance_traces.shape[1]
    own_rows = lax.dynamic_slice_in_dim(
        sightline_lengthwise_index, device * sample_count, sample_count, 1
    )
    cells = lax.broadcasted_iota(jnp.int32, (1, whole_profile.shape[1], 1), 1)
    values = jnp.sum(
        jnp.where(own_rows[:, None, :] == cells, whole_profile[:, :, None], 0.0), axis=1
    )
    return (species_out, values - observed_absorbance_traces)


def solution(mesh):
    in_specs = (
        P(None, "axial", "radial"),
        P(None, "axial", "radial"),
        P("axial", "radial"),
        P(),
        P(),
        P("axial", "radial"),
        P(),
        P("radial"),
        P(),
        P(None, ("axial", "radial")),
    )
    out_specs = (P(None, "axial", "radial"), P(None, ("axial", "radial")))
    return jax.shard_map(local, mesh=mesh, in_specs=in_specs, out_specs=out_specs, check_vma=False)
```

```python
import math

import jax
import jax.numpy as jnp
from jax import lax
from jax.sharding import PartitionSpec as P
from jax.experimental import pallas as pl
from jax.experimental.pallas import tpu as pltpu

TILE_ROWS = 2
ITERS = 3


TIME_STEP = 0.4
CHEM_STEP = 0.5
ARRHENIUS_BARRIER = 1.0
WENO_EPS = 1e-06
HIGHEST = lax.Precision.HIGHEST
CHEMISTRY_PRECISION = lax.Precision.HIGH


def edge_layers(shard, axis, dim, width):
    peers, length = (lax.axis_size(axis), shard.shape[dim])
    up = [(i, i + 1) for i in range(peers - 1)]
    down = [(j, i) for i, j in up]
    last = lax.slice_in_dim(shard, length - width, length, axis=dim)
    initial = lax.slice_in_dim(shard, 0, width, axis=dim)
    return lax.ppermute(last, axis, up), lax.ppermute(initial, axis, down)


def weno_side(minus_two, minus_one, centre, plus_one, plus_two):
    curve_zero = minus_two - 2.0 * minus_one + centre
    curve_one = minus_one - 2.0 * centre + plus_one
    curve_two = centre - 2.0 * plus_one + plus_two
    slope_zero = minus_two - 4.0 * minus_one + 3.0 * centre
    slope_one = minus_one - plus_one
    slope_two = 3.0 * centre - 4.0 * plus_one + plus_two
    beta_zero = 13.0 / 12.0 * curve_zero * curve_zero + 0.25 * slope_zero * slope_zero
    beta_one = 13.0 / 12.0 * curve_one * curve_one + 0.25 * slope_one * slope_one
    beta_two = 13.0 / 12.0 * curve_two * curve_two + 0.25 * slope_two * slope_two
    guard_zero = WENO_EPS + beta_zero
    guard_one = WENO_EPS + beta_one
    guard_two = WENO_EPS + beta_two
    guard_zero = guard_zero * guard_zero
    guard_one = guard_one * guard_one
    guard_two = guard_two * guard_two
    cross_zero = guard_one * guard_two
    cross_one = 6.0 * (guard_zero * guard_two)
    cross_two = 3.0 * (guard_zero * guard_one)
    blended = cross_zero * (2.0 * minus_two - 7.0 * minus_one + 11.0 * centre)
    blended = blended + cross_one * (-minus_one + 5.0 * centre + 2.0 * plus_one)
    blended = blended + cross_two * (2.0 * centre + 5.0 * plus_one - plus_two)
    return blended / (6.0 * (cross_zero + cross_one + cross_two))


HALO = 8
CHUNK = 8


def upwind_divergence(ext_ref, vel_ref, flux_ref, rows):
    faces = flux_ref.shape[0]
    for low in range(0, faces, CHUNK):

        def cut(offset):
            return ext_ref[pl.ds(HALO - 3 + offset + low, CHUNK), :]

        face_speed = 0.5 * (
            vel_ref[pl.ds(HALO - 1 + low, CHUNK), :] + vel_ref[pl.ds(HALO + low, CHUNK), :]
        )
        forward = face_speed >= 0.0
        stencil = [
            jnp.where(forward, cut(lower), cut(upper))
            for lower, upper in ((0, 5), (1, 4), (2, 3), (3, 2), (4, 1))
        ]
        flux_ref[pl.ds(low, CHUNK), :] = face_speed * weno_side(*stencil)
    return flux_ref[pl.ds(1, rows), :] - flux_ref[pl.ds(0, rows), :]


def transport_kernel(
    field_ref, speed_ref, top_ref, top_speed_ref, bottom_ref, bottom_speed_ref,
    left_ref, left_speed_ref, right_ref, right_speed_ref, out_ref,
    ext_ref, vel_ref, flux_ref,
):
    rows, cols = field_ref.shape[1], field_ref.shape[2]
    span = ext_ref.shape[0]
    tail = span - HALO - rows
    zeros = jnp.zeros((tail - HALO, cols), jnp.float32)
    field = field_ref[0]

    ext_ref[pl.ds(0, HALO), :] = top_ref[0]
    ext_ref[pl.ds(HALO, rows), :] = field
    ext_ref[pl.ds(HALO + rows, HALO), :] = bottom_ref[0]
    ext_ref[pl.ds(2 * HALO + rows, tail - HALO), :] = zeros
    vel_ref[pl.ds(0, HALO), :] = top_speed_ref[0]
    vel_ref[pl.ds(HALO, rows), :] = speed_ref[0]
    vel_ref[pl.ds(HALO + rows, HALO), :] = bottom_speed_ref[0]
    vel_ref[pl.ds(2 * HALO + rows, tail - HALO), :] = zeros
    along_axial = upwind_divergence(ext_ref, vel_ref, flux_ref, rows)

    ext_ref[pl.ds(0, HALO), :] = left_ref[0]
    ext_ref[pl.ds(HALO, cols), :] = field.T
    ext_ref[pl.ds(HALO + cols, HALO), :] = right_ref[0]
    vel_ref[pl.ds(0, HALO), :] = left_speed_ref[0]
    vel_ref[pl.ds(HALO, cols), :] = speed_ref[1].T
    vel_ref[pl.ds(HALO + cols, HALO), :] = right_speed_ref[0]
    along_radial = upwind_divergence(ext_ref, vel_ref, flux_ref, cols).T

    out_ref[0] = field - TIME_STEP * (along_axial + along_radial)


def transport(species, speed, width=3):
    species_count, rows, cols = species.shape
    assert rows == cols and rows % CHUNK == 0
    axial_edges = jnp.concatenate([species, speed[0:1]], axis=0)
    top, bottom = edge_layers(axial_edges, "axial", 1, width)
    radial_edges = jnp.swapaxes(jnp.concatenate([species, speed[1:2]], axis=0), 1, 2)
    left, right = edge_layers(radial_edges, "radial", 1, width)
    before = ((0, 0), (HALO - width, 0), (0, 0))
    after = ((0, 0), (0, HALO - width), (0, 0))
    top, left = (jnp.pad(top, before), jnp.pad(left, before))
    bottom, right = (jnp.pad(bottom, after), jnp.pad(right, after))
    faces = rows + CHUNK
    span = HALO + faces + HALO
    plane = pl.BlockSpec((1, rows, cols), lambda s: (s, 0, 0))
    speeds = pl.BlockSpec((2, rows, cols), lambda s: (0, 0, 0))
    edge = pl.BlockSpec((1, HALO, cols), lambda s: (s, 0, 0))
    edge_speed = pl.BlockSpec((1, HALO, cols), lambda s: (species_count, 0, 0))
    return pl.pallas_call(
        transport_kernel,
        grid=(species_count,),
        in_specs=[plane, speeds] + [edge, edge_speed] * 4,
        out_specs=plane,
        out_shape=jax.ShapeDtypeStruct(species.shape, jnp.float32),
        scratch_shapes=[
            pltpu.VMEM((span, cols), jnp.float32),
            pltpu.VMEM((span, cols), jnp.float32),
            pltpu.VMEM((faces, cols), jnp.float32),
        ],
    )(species, speed, top, top, bottom, bottom, left, left, right, right)


def kinetics_advance(
    starting_composition_field,
    thermal_field,
    linearized_kinetics_operator,
    frozen_jacobian_inverse_addend,
):
    acceleration_factor = jnp.exp(-ARRHENIUS_BARRIER / thermal_field)
    current = starting_composition_field
    for newton_step in range(ITERS):
        source = jnp.tensordot(
            linearized_kinetics_operator, current, axes=(1, 0), precision=CHEMISTRY_PRECISION
        ) - jnp.tanh(current)
        defect = current - starting_composition_field - CHEM_STEP * acceleration_factor * source
        current = (
            current
            - defect
            - jnp.tensordot(frozen_jacobian_inverse_addend, defect, axes=(1, 0), precision=CHEMISTRY_PRECISION)
        )
    return current


def absorbance_profile(field, molar_absorptivity_table, spokewise_sightline_length):
    mixed = jnp.tensordot(molar_absorptivity_table, field, axes=(1, 0), precision=HIGHEST)
    return jnp.dot(mixed, spokewise_sightline_length, precision=HIGHEST)


def butterfly_sum(part, axis):
    peers, stride = (lax.axis_size(axis), 1)
    if peers & (peers - 1):
        return lax.psum(part, axis)
    while stride < peers:
        pairs = [(j, j ^ stride) for j in range(peers)]
        part = part + lax.ppermute(part, axis, pairs)
        stride *= 2
    return part


def doubling_gather(part, axis):
    peers, stride = (lax.axis_size(axis), 1)
    if peers & (peers - 1):
        return lax.all_gather(part, axis, axis=1, tiled=True)
    position = lax.axis_index(axis)
    blocks = part[None]
    while stride < peers:
        pairs = [(j, j ^ stride) for j in range(peers)]
        other = lax.ppermute(blocks, axis, pairs)
        upper = (position // stride) % 2 == 1
        blocks = jnp.where(
            upper, jnp.concatenate([other, blocks], 0), jnp.concatenate([blocks, other], 0)
        )
        stride *= 2
    return jnp.transpose(blocks, (1, 0, 2)).reshape(part.shape[0], -1)


def gathered_profile(profile):
    return doubling_gather(butterfly_sum(profile, "radial"), "axial")


def local(
    composition_deviations,
    flow_speed_vector,
    thermal_field,
    linearized_kinetics_operator,
    frozen_jacobian_inverse_addend,
    rigid_block_indicator,
    molar_absorptivity_table,
    spokewise_sightline_length,
    sightline_lengthwise_index,
    observed_absorbance_traces,
):
    advected_composition_field = transport(composition_deviations, flow_speed_vector)
    combusted_composition_field = kinetics_advance(
        advected_composition_field,
        thermal_field,
        linearized_kinetics_operator,
        frozen_jacobian_inverse_addend,
    )
    flag_cells = jnp.repeat(
        jnp.repeat(rigid_block_indicator, TILE_ROWS, axis=0),
        advected_composition_field.shape[2],
        axis=1,
    )
    species_out = jnp.where(
        flag_cells[None] > 0, combusted_composition_field, advected_composition_field
    )
    path_scale = 1.0 / math.sqrt(advected_composition_field.shape[2] * lax.axis_size("radial"))
    profile = (
        absorbance_profile(species_out, molar_absorptivity_table, spokewise_sightline_length)
        * path_scale
    )
    whole_profile = gathered_profile(profile)
    device = lax.axis_index(("axial", "radial"))
    sample_count = observed_absorbance_traces.shape[1]
    own_rows = lax.dynamic_slice_in_dim(
        sightline_lengthwise_index, device * sample_count, sample_count, 1
    )
    cells = lax.broadcasted_iota(jnp.int32, (1, whole_profile.shape[1], 1), 1)
    values = jnp.sum(
        jnp.where(own_rows[:, None, :] == cells, whole_profile[:, :, None], 0.0), axis=1
    )
    return (species_out, values - observed_absorbance_traces)


def solution(mesh):
    in_specs = (
        P(None, "axial", "radial"),
        P(None, "axial", "radial"),
        P("axial", "radial"),
        P(),
        P(),
        P("axial", "radial"),
        P(),
        P("radial"),
        P(),
        P(None, ("axial", "radial")),
    )
    out_specs = (P(None, "axial", "radial"), P(None, ("axial", "radial")))
    return jax.shard_map(local, mesh=mesh, in_specs=in_specs, out_specs=out_specs, check_vma=False)
```

```python
import math

import jax
import jax.numpy as jnp
from jax import lax
from jax.sharding import PartitionSpec as P
from jax.experimental import pallas as pl
from jax.experimental.pallas import tpu as pltpu

TILE_ROWS = 2
ITERS = 3


TIME_STEP = 0.4
CHEM_STEP = 0.5
ARRHENIUS_BARRIER = 1.0
WENO_EPS = 1e-06
HIGHEST = lax.Precision.HIGHEST
CHEMISTRY_PRECISION = lax.Precision.HIGH


def edge_layers(shard, axis, dim, width):
    peers, length = (lax.axis_size(axis), shard.shape[dim])
    up = [(i, i + 1) for i in range(peers - 1)]
    down = [(j, i) for i, j in up]
    last = lax.slice_in_dim(shard, length - width, length, axis=dim)
    initial = lax.slice_in_dim(shard, 0, width, axis=dim)
    return lax.ppermute(last, axis, up), lax.ppermute(initial, axis, down)


def weno_side(minus_two, minus_one, centre, plus_one, plus_two):
    curve_zero = minus_two - 2.0 * minus_one + centre
    curve_one = minus_one - 2.0 * centre + plus_one
    curve_two = centre - 2.0 * plus_one + plus_two
    slope_zero = minus_two - 4.0 * minus_one + 3.0 * centre
    slope_one = minus_one - plus_one
    slope_two = 3.0 * centre - 4.0 * plus_one + plus_two
    beta_zero = 13.0 / 12.0 * curve_zero * curve_zero + 0.25 * slope_zero * slope_zero
    beta_one = 13.0 / 12.0 * curve_one * curve_one + 0.25 * slope_one * slope_one
    beta_two = 13.0 / 12.0 * curve_two * curve_two + 0.25 * slope_two * slope_two
    guard_zero = WENO_EPS + beta_zero
    guard_one = WENO_EPS + beta_one
    guard_two = WENO_EPS + beta_two
    guard_zero = guard_zero * guard_zero
    guard_one = guard_one * guard_one
    guard_two = guard_two * guard_two
    cross_zero = guard_one * guard_two
    cross_one = 6.0 * (guard_zero * guard_two)
    cross_two = 3.0 * (guard_zero * guard_one)
    blended = cross_zero * (2.0 * minus_two - 7.0 * minus_one + 11.0 * centre)
    blended = blended + cross_one * (-minus_one + 5.0 * centre + 2.0 * plus_one)
    blended = blended + cross_two * (2.0 * centre + 5.0 * plus_one - plus_two)
    return blended / (6.0 * (cross_zero + cross_one + cross_two))


HALO = 8
CHUNK = 8


def upwind_divergence(ext_ref, vel_ref, flux_ref, rows):
    faces = flux_ref.shape[0]
    for low in range(0, faces, CHUNK):

        def cut(offset):
            return ext_ref[pl.ds(HALO - 3 + offset + low, CHUNK), :]

        face_speed = 0.5 * (
            vel_ref[pl.ds(HALO - 1 + low, CHUNK), :] + vel_ref[pl.ds(HALO + low, CHUNK), :]
        )
        forward = face_speed >= 0.0
        stencil = [
            jnp.where(forward, cut(lower), cut(upper))
            for lower, upper in ((0, 5), (1, 4), (2, 3), (3, 2), (4, 1))
        ]
        flux_ref[pl.ds(low, CHUNK), :] = face_speed * weno_side(*stencil)
    return flux_ref[pl.ds(1, rows), :] - flux_ref[pl.ds(0, rows), :]


def transport_kernel(
    field_ref, speed_ref, top_ref, top_speed_ref, bottom_ref, bottom_speed_ref,
    left_ref, left_speed_ref, right_ref, right_speed_ref, out_ref,
    ext_ref, vel_ref, flux_ref,
):
    rows, cols = field_ref.shape[1], field_ref.shape[2]
    span = ext_ref.shape[0]
    tail = span - HALO - rows
    zeros = jnp.zeros((tail - HALO, cols), jnp.float32)
    field = field_ref[0]

    ext_ref[pl.ds(0, HALO), :] = top_ref[0]
    ext_ref[pl.ds(HALO, rows), :] = field
    ext_ref[pl.ds(HALO + rows, HALO), :] = bottom_ref[0]
    ext_ref[pl.ds(2 * HALO + rows, tail - HALO), :] = zeros
    vel_ref[pl.ds(0, HALO), :] = top_speed_ref[0]
    vel_ref[pl.ds(HALO, rows), :] = speed_ref[0]
    vel_ref[pl.ds(HALO + rows, HALO), :] = bottom_speed_ref[0]
    vel_ref[pl.ds(2 * HALO + rows, tail - HALO), :] = zeros
    along_axial = upwind_divergence(ext_ref, vel_ref, flux_ref, rows)

    ext_ref[pl.ds(0, HALO), :] = left_ref[0]
    ext_ref[pl.ds(HALO, cols), :] = field.T
    ext_ref[pl.ds(HALO + cols, HALO), :] = right_ref[0]
    vel_ref[pl.ds(0, HALO), :] = left_speed_ref[0]
    vel_ref[pl.ds(HALO, cols), :] = speed_ref[1].T
    vel_ref[pl.ds(HALO + cols, HALO), :] = right_speed_ref[0]
    along_radial = upwind_divergence(ext_ref, vel_ref, flux_ref, cols).T

    out_ref[0] = field - TIME_STEP * (along_axial + along_radial)


def transport(species, speed, width=3):
    species_count, rows, cols = species.shape
    assert rows == cols and rows % CHUNK == 0
    axial_edges = jnp.concatenate([species, speed[0:1]], axis=0)
    top, bottom = edge_layers(axial_edges, "axial", 1, width)
    radial_edges = jnp.swapaxes(jnp.concatenate([species, speed[1:2]], axis=0), 1, 2)
    left, right = edge_layers(radial_edges, "radial", 1, width)
    before = ((0, 0), (HALO - width, 0), (0, 0))
    after = ((0, 0), (0, HALO - width), (0, 0))
    top, left = (jnp.pad(top, before), jnp.pad(left, before))
    bottom, right = (jnp.pad(bottom, after), jnp.pad(right, after))
    faces = rows + CHUNK
    span = HALO + faces + HALO
    plane = pl.BlockSpec((1, rows, cols), lambda s: (s, 0, 0))
    speeds = pl.BlockSpec((2, rows, cols), lambda s: (0, 0, 0))
    edge = pl.BlockSpec((1, HALO, cols), lambda s: (s, 0, 0))
    edge_speed = pl.BlockSpec((1, HALO, cols), lambda s: (species_count, 0, 0))
    return pl.pallas_call(
        transport_kernel,
        grid=(species_count,),
        in_specs=[plane, speeds] + [edge, edge_speed] * 4,
        out_specs=plane,
        out_shape=jax.ShapeDtypeStruct(species.shape, jnp.float32),
        scratch_shapes=[
            pltpu.VMEM((span, cols), jnp.float32),
            pltpu.VMEM((span, cols), jnp.float32),
            pltpu.VMEM((faces, cols), jnp.float32),
        ],
    )(species, speed, top, top, bottom, bottom, left, left, right, right)


def split_bf16(value):
    high = value.astype(jnp.bfloat16)
    return high, (value - high.astype(jnp.float32)).astype(jnp.bfloat16)


def three_pass_dot(matrix_parts, value):
    value_high, value_low = split_bf16(value)
    matrix_high, matrix_low = matrix_parts
    product = partial_dot(matrix_high, value_high)
    product = product + partial_dot(matrix_high, value_low)
    return product + partial_dot(matrix_low, value_high)


def partial_dot(left, right):
    return jnp.dot(left, right, preferred_element_type=jnp.float32)


def chemistry_kernel(
    moved_ref, thermal_ref, flag_ref, path_ref, kinetics_ref, jacobian_ref, table_ref,
    out_ref, mixed_ref,
):
    moved = moved_ref[...]
    acceleration_factor = jnp.exp(-ARRHENIUS_BARRIER / thermal_ref[...])
    kinetics = split_bf16(kinetics_ref[...])
    jacobian = split_bf16(jacobian_ref[...])
    current = moved
    for newton_step in range(ITERS):
        source = three_pass_dot(kinetics, current) - jnp.tanh(current)
        defect = current - moved - CHEM_STEP * acceleration_factor * source
        current = current - defect - three_pass_dot(jacobian, defect)
    species_out = jnp.where(flag_ref[...] > 0, current, moved)
    out_ref[...] = species_out
    mixed = jnp.dot(
        table_ref[...], species_out, precision=HIGHEST, preferred_element_type=jnp.float32
    )
    mixed_ref[...] = mixed * path_ref[...]


def chemistry_and_profile(
    moved, thermal_field, rigid_block_indicator, spokewise_sightline_length,
    linearized_kinetics_operator, frozen_jacobian_inverse_addend, molar_absorptivity_table,
    block=2048,
):
    species_count, rows, cols = moved.shape
    cells = rows * cols
    block = min(block, cells)
    lasers = molar_absorptivity_table.shape[0]
    row_flags = jnp.repeat(rigid_block_indicator[:, 0], TILE_ROWS)
    flags = jnp.broadcast_to(row_flags[:, None], (rows, cols)).reshape(1, cells)
    path = jnp.broadcast_to(spokewise_sightline_length[None, :], (rows, cols)).reshape(1, cells)
    column = pl.BlockSpec((species_count, block), lambda c: (0, c))
    single = pl.BlockSpec((1, block), lambda c: (0, c))

    def whole(array):
        return pl.BlockSpec(array.shape, lambda c: (0, 0))

    species_out, mixed = pl.pallas_call(
        chemistry_kernel,
        grid=(cells // block,),
        in_specs=[
            column, single, single, single,
            whole(linearized_kinetics_operator), whole(frozen_jacobian_inverse_addend),
            whole(molar_absorptivity_table),
        ],
        out_specs=[column, pl.BlockSpec((lasers, block), lambda c: (0, c))],
        out_shape=[
            jax.ShapeDtypeStruct((species_count, cells), jnp.float32),
            jax.ShapeDtypeStruct((lasers, cells), jnp.float32),
        ],
    )(
        moved.reshape(species_count, cells), thermal_field.reshape(1, cells), flags, path,
        linearized_kinetics_operator, frozen_jacobian_inverse_addend, molar_absorptivity_table,
    )
    profile = mixed.reshape(lasers, rows, cols).sum(axis=2)
    return species_out.reshape(moved.shape), profile


def butterfly_sum(part, axis):
    peers, stride = (lax.axis_size(axis), 1)
    if peers & (peers - 1):
        return lax.psum(part, axis)
    while stride < peers:
        pairs = [(j, j ^ stride) for j in range(peers)]
        part = part + lax.ppermute(part, axis, pairs)
        stride *= 2
    return part


def doubling_gather(part, axis):
    peers, stride = (lax.axis_size(axis), 1)
    if peers & (peers - 1):
        return lax.all_gather(part, axis, axis=1, tiled=True)
    position = lax.axis_index(axis)
    blocks = part[None]
    while stride < peers:
        pairs = [(j, j ^ stride) for j in range(peers)]
        other = lax.ppermute(blocks, axis, pairs)
        upper = (position // stride) % 2 == 1
        blocks = jnp.where(
            upper, jnp.concatenate([other, blocks], 0), jnp.concatenate([blocks, other], 0)
        )
        stride *= 2
    return jnp.transpose(blocks, (1, 0, 2)).reshape(part.shape[0], -1)


def gathered_profile(profile):
    return doubling_gather(butterfly_sum(profile, "radial"), "axial")


def local(
    composition_deviations,
    flow_speed_vector,
    thermal_field,
    linearized_kinetics_operator,
    frozen_jacobian_inverse_addend,
    rigid_block_indicator,
    molar_absorptivity_table,
    spokewise_sightline_length,
    sightline_lengthwise_index,
    observed_absorbance_traces,
):
    advected_composition_field = transport(composition_deviations, flow_speed_vector)
    species_out, profile = chemistry_and_profile(
        advected_composition_field,
        thermal_field,
        rigid_block_indicator,
        spokewise_sightline_length,
        linearized_kinetics_operator,
        frozen_jacobian_inverse_addend,
        molar_absorptivity_table,
    )
    path_scale = 1.0 / math.sqrt(advected_composition_field.shape[2] * lax.axis_size("radial"))
    profile = profile * path_scale
    whole_profile = gathered_profile(profile)
    device = lax.axis_index(("axial", "radial"))
    sample_count = observed_absorbance_traces.shape[1]
    own_rows = lax.dynamic_slice_in_dim(
        sightline_lengthwise_index, device * sample_count, sample_count, 1
    )
    cells = lax.broadcasted_iota(jnp.int32, (1, whole_profile.shape[1], 1), 1)
    values = jnp.sum(
        jnp.where(own_rows[:, None, :] == cells, whole_profile[:, :, None], 0.0), axis=1
    )
    return (species_out, values - observed_absorbance_traces)


def solution(mesh):
    in_specs = (
        P(None, "axial", "radial"),
        P(None, "axial", "radial"),
        P("axial", "radial"),
        P(),
        P(),
        P("axial", "radial"),
        P(),
        P("radial"),
        P(),
        P(None, ("axial", "radial")),
    )
    out_specs = (P(None, "axial", "radial"), P(None, ("axial", "radial")))
    return jax.shard_map(local, mesh=mesh, in_specs=in_specs, out_specs=out_specs, check_vma=False)
```

```python
import math

import jax
import jax.numpy as jnp
from jax import lax
from jax.sharding import PartitionSpec as P
from jax.experimental import pallas as pl
from jax.experimental.pallas import tpu as pltpu

TILE_ROWS = 2
ITERS = 3


TIME_STEP = 0.4
CHEM_STEP = 0.5
ARRHENIUS_BARRIER = 1.0
WENO_EPS = 1e-06
HIGHEST = lax.Precision.HIGHEST
CHEMISTRY_PRECISION = lax.Precision.HIGH


def edge_layers(shard, axis, dim, width):
    peers, length = (lax.axis_size(axis), shard.shape[dim])
    up = [(i, i + 1) for i in range(peers - 1)]
    down = [(j, i) for i, j in up]
    last = lax.slice_in_dim(shard, length - width, length, axis=dim)
    initial = lax.slice_in_dim(shard, 0, width, axis=dim)
    return lax.ppermute(last, axis, up), lax.ppermute(initial, axis, down)


def weno_side(minus_two, minus_one, centre, plus_one, plus_two):
    curve_zero = minus_two - 2.0 * minus_one + centre
    curve_one = minus_one - 2.0 * centre + plus_one
    curve_two = centre - 2.0 * plus_one + plus_two
    slope_zero = minus_two - 4.0 * minus_one + 3.0 * centre
    slope_one = minus_one - plus_one
    slope_two = 3.0 * centre - 4.0 * plus_one + plus_two
    beta_zero = 13.0 / 12.0 * curve_zero * curve_zero + 0.25 * slope_zero * slope_zero
    beta_one = 13.0 / 12.0 * curve_one * curve_one + 0.25 * slope_one * slope_one
    beta_two = 13.0 / 12.0 * curve_two * curve_two + 0.25 * slope_two * slope_two
    guard_zero = WENO_EPS + beta_zero
    guard_one = WENO_EPS + beta_one
    guard_two = WENO_EPS + beta_two
    guard_zero = guard_zero * guard_zero
    guard_one = guard_one * guard_one
    guard_two = guard_two * guard_two
    cross_zero = guard_one * guard_two
    cross_one = 6.0 * (guard_zero * guard_two)
    cross_two = 3.0 * (guard_zero * guard_one)
    blended = cross_zero * (2.0 * minus_two - 7.0 * minus_one + 11.0 * centre)
    blended = blended + cross_one * (-minus_one + 5.0 * centre + 2.0 * plus_one)
    blended = blended + cross_two * (2.0 * centre + 5.0 * plus_one - plus_two)
    return blended / (6.0 * (cross_zero + cross_one + cross_two))


HALO = 8
CHUNK = 8


def upwind_divergence(ext_ref, vel_ref, flux_ref, rows):
    faces = flux_ref.shape[0]
    for low in range(0, faces, CHUNK):

        def cut(offset):
            return ext_ref[pl.ds(HALO - 3 + offset + low, CHUNK), :]

        face_speed = 0.5 * (
            vel_ref[pl.ds(HALO - 1 + low, CHUNK), :] + vel_ref[pl.ds(HALO + low, CHUNK), :]
        )
        forward = face_speed >= 0.0
        stencil = [
            jnp.where(forward, cut(lower), cut(upper))
            for lower, upper in ((0, 5), (1, 4), (2, 3), (3, 2), (4, 1))
        ]
        flux_ref[pl.ds(low, CHUNK), :] = face_speed * weno_side(*stencil)
    return flux_ref[pl.ds(1, rows), :] - flux_ref[pl.ds(0, rows), :]


def transport_kernel(
    field_ref, speed_ref, top_ref, top_speed_ref, bottom_ref, bottom_speed_ref,
    left_ref, left_speed_ref, right_ref, right_speed_ref, out_ref,
    ext_ref, vel_ref, flux_ref,
):
    rows, cols = field_ref.shape[1], field_ref.shape[2]
    span = ext_ref.shape[0]
    tail = span - HALO - rows
    zeros = jnp.zeros((tail - HALO, cols), jnp.float32)
    field = field_ref[0]

    ext_ref[pl.ds(0, HALO), :] = top_ref[0]
    ext_ref[pl.ds(HALO, rows), :] = field
    ext_ref[pl.ds(HALO + rows, HALO), :] = bottom_ref[0]
    ext_ref[pl.ds(2 * HALO + rows, tail - HALO), :] = zeros
    vel_ref[pl.ds(0, HALO), :] = top_speed_ref[0]
    vel_ref[pl.ds(HALO, rows), :] = speed_ref[0]
    vel_ref[pl.ds(HALO + rows, HALO), :] = bottom_speed_ref[0]
    vel_ref[pl.ds(2 * HALO + rows, tail - HALO), :] = zeros
    along_axial = upwind_divergence(ext_ref, vel_ref, flux_ref, rows)

    ext_ref[pl.ds(0, HALO), :] = left_ref[0]
    ext_ref[pl.ds(HALO, cols), :] = field.T
    ext_ref[pl.ds(HALO + cols, HALO), :] = right_ref[0]
    vel_ref[pl.ds(0, HALO), :] = left_speed_ref[0]
    vel_ref[pl.ds(HALO, cols), :] = speed_ref[1].T
    vel_ref[pl.ds(HALO + cols, HALO), :] = right_speed_ref[0]
    along_radial = upwind_divergence(ext_ref, vel_ref, flux_ref, cols).T

    moved = field - TIME_STEP * (along_axial + along_radial)
    out_ref[:, pl.ds(pl.program_id(0), 1), :] = moved[:, None, :]


def transport(species, speed, width=3):
    species_count, rows, cols = species.shape
    assert rows == cols and rows % CHUNK == 0
    axial_edges = jnp.concatenate([species, speed[0:1]], axis=0)
    top, bottom = edge_layers(axial_edges, "axial", 1, width)
    radial_edges = jnp.swapaxes(jnp.concatenate([species, speed[1:2]], axis=0), 1, 2)
    left, right = edge_layers(radial_edges, "radial", 1, width)
    before = ((0, 0), (HALO - width, 0), (0, 0))
    after = ((0, 0), (0, HALO - width), (0, 0))
    top, left = (jnp.pad(top, before), jnp.pad(left, before))
    bottom, right = (jnp.pad(bottom, after), jnp.pad(right, after))
    faces = rows + CHUNK
    span = HALO + faces + HALO
    plane = pl.BlockSpec((1, rows, cols), lambda s: (s, 0, 0))
    speeds = pl.BlockSpec((2, rows, cols), lambda s: (0, 0, 0))
    edge = pl.BlockSpec((1, HALO, cols), lambda s: (s, 0, 0))
    edge_speed = pl.BlockSpec((1, HALO, cols), lambda s: (species_count, 0, 0))
    moved_rows = pl.pallas_call(
        transport_kernel,
        grid=(species_count,),
        in_specs=[plane, speeds] + [edge, edge_speed] * 4,
        out_specs=pl.BlockSpec((rows, species_count, cols), lambda s: (0, 0, 0)),
        out_shape=jax.ShapeDtypeStruct((rows, species_count, cols), jnp.float32),
        scratch_shapes=[
            pltpu.VMEM((span, cols), jnp.float32),
            pltpu.VMEM((span, cols), jnp.float32),
            pltpu.VMEM((faces, cols), jnp.float32),
        ],
    )(species, speed, top, top, bottom, bottom, left, left, right, right)
    return jnp.transpose(moved_rows, (1, 0, 2))


def kinetics_advance(
    starting_composition_field,
    thermal_field,
    linearized_kinetics_operator,
    frozen_jacobian_inverse_addend,
):
    acceleration_factor = jnp.exp(-ARRHENIUS_BARRIER / thermal_field)
    current = starting_composition_field
    for newton_step in range(ITERS):
        source = jnp.tensordot(
            linearized_kinetics_operator, current, axes=(1, 0), precision=CHEMISTRY_PRECISION
        ) - jnp.tanh(current)
        defect = current - starting_composition_field - CHEM_STEP * acceleration_factor * source
        current = (
            current
            - defect
            - jnp.tensordot(frozen_jacobian_inverse_addend, defect, axes=(1, 0), precision=CHEMISTRY_PRECISION)
        )
    return current


def absorbance_profile(field, molar_absorptivity_table, spokewise_sightline_length):
    mixed = jnp.tensordot(molar_absorptivity_table, field, axes=(1, 0), precision=HIGHEST)
    return jnp.dot(mixed, spokewise_sightline_length, precision=HIGHEST)


def butterfly_sum(part, axis):
    peers, stride = (lax.axis_size(axis), 1)
    if peers & (peers - 1):
        return lax.psum(part, axis)
    while stride < peers:
        pairs = [(j, j ^ stride) for j in range(peers)]
        part = part + lax.ppermute(part, axis, pairs)
        stride *= 2
    return part


def doubling_gather(part, axis):
    peers, stride = (lax.axis_size(axis), 1)
    if peers & (peers - 1):
        return lax.all_gather(part, axis, axis=1, tiled=True)
    position = lax.axis_index(axis)
    blocks = part[None]
    while stride < peers:
        pairs = [(j, j ^ stride) for j in range(peers)]
        other = lax.ppermute(blocks, axis, pairs)
        upper = (position // stride) % 2 == 1
        blocks = jnp.where(
            upper, jnp.concatenate([other, blocks], 0), jnp.concatenate([blocks, other], 0)
        )
        stride *= 2
    return jnp.transpose(blocks, (1, 0, 2)).reshape(part.shape[0], -1)


def gathered_profile(profile):
    return doubling_gather(butterfly_sum(profile, "radial"), "axial")


def local(
    composition_deviations,
    flow_speed_vector,
    thermal_field,
    linearized_kinetics_operator,
    frozen_jacobian_inverse_addend,
    rigid_block_indicator,
    molar_absorptivity_table,
    spokewise_sightline_length,
    sightline_lengthwise_index,
    observed_absorbance_traces,
):
    advected_composition_field = transport(composition_deviations, flow_speed_vector)
    combusted_composition_field = kinetics_advance(
        advected_composition_field,
        thermal_field,
        linearized_kinetics_operator,
        frozen_jacobian_inverse_addend,
    )
    flag_cells = jnp.repeat(
        jnp.repeat(rigid_block_indicator, TILE_ROWS, axis=0),
        advected_composition_field.shape[2],
        axis=1,
    )
    species_out = jnp.where(
        flag_cells[None] > 0, combusted_composition_field, advected_composition_field
    )
    path_scale = 1.0 / math.sqrt(advected_composition_field.shape[2] * lax.axis_size("radial"))
    profile = (
        absorbance_profile(species_out, molar_absorptivity_table, spokewise_sightline_length)
        * path_scale
    )
    whole_profile = gathered_profile(profile)
    device = lax.axis_index(("axial", "radial"))
    sample_count = observed_absorbance_traces.shape[1]
    own_rows = lax.dynamic_slice_in_dim(
        sightline_lengthwise_index, device * sample_count, sample_count, 1
    )
    cells = lax.broadcasted_iota(jnp.int32, (1, whole_profile.shape[1], 1), 1)
    values = jnp.sum(
        jnp.where(own_rows[:, None, :] == cells, whole_profile[:, :, None], 0.0), axis=1
    )
    return (species_out, values - observed_absorbance_traces)


def solution(mesh):
    in_specs = (
        P(None, "axial", "radial"),
        P(None, "axial", "radial"),
        P("axial", "radial"),
        P(),
        P(),
        P("axial", "radial"),
        P(),
        P("radial"),
        P(),
        P(None, ("axial", "radial")),
    )
    out_specs = (P(None, "axial", "radial"), P(None, ("axial", "radial")))
    return jax.shard_map(local, mesh=mesh, in_specs=in_specs, out_specs=out_specs, check_vma=False)
```

```python
import math

import jax
import jax.numpy as jnp
from jax import lax
from jax.sharding import PartitionSpec as P
from jax.experimental import pallas as pl
from jax.experimental.pallas import tpu as pltpu

TILE_ROWS = 2
ITERS = 3


TIME_STEP = 0.4
CHEM_STEP = 0.5
ARRHENIUS_BARRIER = 1.0
WENO_EPS = 1e-06
HIGHEST = lax.Precision.HIGHEST
CHEMISTRY_PRECISION = lax.Precision.HIGH


def edge_layers(shard, axis, dim, width):
    peers, length = (lax.axis_size(axis), shard.shape[dim])
    up = [(i, i + 1) for i in range(peers - 1)]
    down = [(j, i) for i, j in up]
    last = lax.slice_in_dim(shard, length - width, length, axis=dim)
    initial = lax.slice_in_dim(shard, 0, width, axis=dim)
    return lax.ppermute(last, axis, up), lax.ppermute(initial, axis, down)


def weno_side(minus_two, minus_one, centre, plus_one, plus_two):
    curve_zero = minus_two - 2.0 * minus_one + centre
    curve_one = minus_one - 2.0 * centre + plus_one
    curve_two = centre - 2.0 * plus_one + plus_two
    slope_zero = minus_two - 4.0 * minus_one + 3.0 * centre
    slope_one = minus_one - plus_one
    slope_two = 3.0 * centre - 4.0 * plus_one + plus_two
    beta_zero = 13.0 / 12.0 * curve_zero * curve_zero + 0.25 * slope_zero * slope_zero
    beta_one = 13.0 / 12.0 * curve_one * curve_one + 0.25 * slope_one * slope_one
    beta_two = 13.0 / 12.0 * curve_two * curve_two + 0.25 * slope_two * slope_two
    guard_zero = WENO_EPS + beta_zero
    guard_one = WENO_EPS + beta_one
    guard_two = WENO_EPS + beta_two
    guard_zero = guard_zero * guard_zero
    guard_one = guard_one * guard_one
    guard_two = guard_two * guard_two
    cross_zero = guard_one * guard_two
    cross_one = 6.0 * (guard_zero * guard_two)
    cross_two = 3.0 * (guard_zero * guard_one)
    blended = cross_zero * (2.0 * minus_two - 7.0 * minus_one + 11.0 * centre)
    blended = blended + cross_one * (-minus_one + 5.0 * centre + 2.0 * plus_one)
    blended = blended + cross_two * (2.0 * centre + 5.0 * plus_one - plus_two)
    return blended / (6.0 * (cross_zero + cross_one + cross_two))


HALO = 8
CHUNK = 8


def upwind_divergence(ext_ref, speed_ref, flux_ref, rows):
    faces = flux_ref.shape[0]
    for low in range(0, faces, CHUNK):

        def cut(offset):
            return ext_ref[pl.ds(HALO - 3 + offset + low, CHUNK), :]

        face_speed = speed_ref[pl.ds(low, CHUNK), :]
        forward = face_speed >= 0.0
        stencil = [
            jnp.where(forward, cut(lower), cut(upper))
            for lower, upper in ((0, 5), (1, 4), (2, 3), (3, 2), (4, 1))
        ]
        flux_ref[pl.ds(low, CHUNK), :] = face_speed * weno_side(*stencil)
    return flux_ref[pl.ds(1, rows), :] - flux_ref[pl.ds(0, rows), :]


def transport_kernel(
    field_ref, axial_speed_ref, radial_speed_ref, top_ref, bottom_ref, left_ref, right_ref,
    out_ref, ext_ref, flux_ref,
):
    rows, cols = field_ref.shape[1], field_ref.shape[2]
    span = ext_ref.shape[0]
    tail = span - HALO - rows
    field = field_ref[0]

    ext_ref[pl.ds(0, HALO), :] = top_ref[0]
    ext_ref[pl.ds(HALO, rows), :] = field
    ext_ref[pl.ds(HALO + rows, HALO), :] = bottom_ref[0]
    ext_ref[pl.ds(2 * HALO + rows, tail - HALO), :] = jnp.zeros((tail - HALO, cols), jnp.float32)
    along_axial = upwind_divergence(ext_ref, axial_speed_ref, flux_ref, rows)

    ext_ref[pl.ds(0, HALO), :] = left_ref[0]
    ext_ref[pl.ds(HALO, cols), :] = field.T
    ext_ref[pl.ds(HALO + cols, HALO), :] = right_ref[0]
    along_radial = upwind_divergence(ext_ref, radial_speed_ref, flux_ref, cols).T

    moved = field - TIME_STEP * (along_axial + along_radial)
    out_ref[:, pl.ds(pl.program_id(0), 1), :] = moved[:, None, :]


def face_speeds(edges_before, speed, edges_after, faces):
    extended = jnp.concatenate([edges_before[-1:], speed, edges_after[:1]], axis=0)
    extended = jnp.pad(extended, ((0, faces + 1 - extended.shape[0]), (0, 0)))
    return 0.5 * (extended[:-1] + extended[1:])


def transport(species, speed, width=3):
    species_count, rows, cols = species.shape
    assert rows == cols and rows % CHUNK == 0
    axial_edges = jnp.concatenate([species, speed[0:1]], axis=0)
    top, bottom = edge_layers(axial_edges, "axial", 1, width)
    radial_edges = jnp.swapaxes(jnp.concatenate([species, speed[1:2]], axis=0), 1, 2)
    left, right = edge_layers(radial_edges, "radial", 1, width)
    faces = rows + CHUNK
    axial_speed = face_speeds(top[species_count], speed[0], bottom[species_count], faces)
    radial_speed = face_speeds(left[species_count], speed[1].T, right[species_count], faces)
    before = ((0, 0), (HALO - width, 0), (0, 0))
    after = ((0, 0), (0, HALO - width), (0, 0))
    top, left = (jnp.pad(top[:species_count], before), jnp.pad(left[:species_count], before))
    bottom, right = (jnp.pad(bottom[:species_count], after), jnp.pad(right[:species_count], after))
    span = HALO + faces + HALO
    plane = pl.BlockSpec((1, rows, cols), lambda s: (s, 0, 0))
    face_plane = pl.BlockSpec((faces, cols), lambda s: (0, 0))
    edge = pl.BlockSpec((1, HALO, cols), lambda s: (s, 0, 0))
    moved_rows = pl.pallas_call(
        transport_kernel,
        grid=(species_count,),
        in_specs=[plane, face_plane, face_plane] + [edge] * 4,
        out_specs=pl.BlockSpec((rows, species_count, cols), lambda s: (0, 0, 0)),
        out_shape=jax.ShapeDtypeStruct((rows, species_count, cols), jnp.float32),
        scratch_shapes=[
            pltpu.VMEM((span, cols), jnp.float32),
            pltpu.VMEM((faces, cols), jnp.float32),
        ],
    )(species, axial_speed, radial_speed, top, bottom, left, right)
    return jnp.transpose(moved_rows, (1, 0, 2))


def kinetics_advance(
    starting_composition_field,
    thermal_field,
    linearized_kinetics_operator,
    frozen_jacobian_inverse_addend,
):
    acceleration_factor = jnp.exp(-ARRHENIUS_BARRIER / thermal_field)
    current = starting_composition_field
    for newton_step in range(ITERS):
        source = jnp.tensordot(
            linearized_kinetics_operator, current, axes=(1, 0), precision=CHEMISTRY_PRECISION
        ) - jnp.tanh(current)
        defect = current - starting_composition_field - CHEM_STEP * acceleration_factor * source
        current = (
            current
            - defect
            - jnp.tensordot(frozen_jacobian_inverse_addend, defect, axes=(1, 0), precision=CHEMISTRY_PRECISION)
        )
    return current


def absorbance_profile(field, molar_absorptivity_table, spokewise_sightline_length):
    mixed = jnp.tensordot(molar_absorptivity_table, field, axes=(1, 0), precision=HIGHEST)
    return jnp.dot(mixed, spokewise_sightline_length, precision=HIGHEST)


def butterfly_sum(part, axis):
    peers, stride = (lax.axis_size(axis), 1)
    if peers & (peers - 1):
        return lax.psum(part, axis)
    while stride < peers:
        pairs = [(j, j ^ stride) for j in range(peers)]
        part = part + lax.ppermute(part, axis, pairs)
        stride *= 2
    return part


def doubling_gather(part, axis):
    peers, stride = (lax.axis_size(axis), 1)
    if peers & (peers - 1):
        return lax.all_gather(part, axis, axis=1, tiled=True)
    position = lax.axis_index(axis)
    blocks = part[None]
    while stride < peers:
        pairs = [(j, j ^ stride) for j in range(peers)]
        other = lax.ppermute(blocks, axis, pairs)
        upper = (position // stride) % 2 == 1
        blocks = jnp.where(
            upper, jnp.concatenate([other, blocks], 0), jnp.concatenate([blocks, other], 0)
        )
        stride *= 2
    return jnp.transpose(blocks, (1, 0, 2)).reshape(part.shape[0], -1)


def gathered_profile(profile):
    return doubling_gather(butterfly_sum(profile, "radial"), "axial")


def local(
    composition_deviations,
    flow_speed_vector,
    thermal_field,
    linearized_kinetics_operator,
    frozen_jacobian_inverse_addend,
    rigid_block_indicator,
    molar_absorptivity_table,
    spokewise_sightline_length,
    sightline_lengthwise_index,
    observed_absorbance_traces,
):
    advected_composition_field = transport(composition_deviations, flow_speed_vector)
    combusted_composition_field = kinetics_advance(
        advected_composition_field,
        thermal_field,
        linearized_kinetics_operator,
        frozen_jacobian_inverse_addend,
    )
    flag_cells = jnp.repeat(
        jnp.repeat(rigid_block_indicator, TILE_ROWS, axis=0),
        advected_composition_field.shape[2],
        axis=1,
    )
    species_out = jnp.where(
        flag_cells[None] > 0, combusted_composition_field, advected_composition_field
    )
    path_scale = 1.0 / math.sqrt(advected_composition_field.shape[2] * lax.axis_size("radial"))
    profile = (
        absorbance_profile(species_out, molar_absorptivity_table, spokewise_sightline_length)
        * path_scale
    )
    whole_profile = gathered_profile(profile)
    device = lax.axis_index(("axial", "radial"))
    sample_count = observed_absorbance_traces.shape[1]
    own_rows = lax.dynamic_slice_in_dim(
        sightline_lengthwise_index, device * sample_count, sample_count, 1
    )
    cells = lax.broadcasted_iota(jnp.int32, (1, whole_profile.shape[1], 1), 1)
    values = jnp.sum(
        jnp.where(own_rows[:, None, :] == cells, whole_profile[:, :, None], 0.0), axis=1
    )
    return (species_out, values - observed_absorbance_traces)


def solution(mesh):
    in_specs = (
        P(None, "axial", "radial"),
        P(None, "axial", "radial"),
        P("axial", "radial"),
        P(),
        P(),
        P("axial", "radial"),
        P(),
        P("radial"),
        P(),
        P(None, ("axial", "radial")),
    )
    out_specs = (P(None, "axial", "radial"), P(None, ("axial", "radial")))
    return jax.shard_map(local, mesh=mesh, in_specs=in_specs, out_specs=out_specs, check_vma=False)
```

```python
import math

import jax
import jax.numpy as jnp
from jax import lax
from jax.sharding import PartitionSpec as P
from jax.experimental import pallas as pl
from jax.experimental.pallas import tpu as pltpu

TILE_ROWS = 2
ITERS = 3


TIME_STEP = 0.4
CHEM_STEP = 0.5
ARRHENIUS_BARRIER = 1.0
WENO_EPS = 1e-06
HIGHEST = lax.Precision.HIGHEST
CHEMISTRY_PRECISION = lax.Precision.HIGH


def edge_layers(shard, axis, dim, width, arrange=lambda layers: layers):
    peers, length = (lax.axis_size(axis), shard.shape[dim])
    up = [(i, i + 1) for i in range(peers - 1)]
    down = [(j, i) for i, j in up]
    last = arrange(lax.slice_in_dim(shard, length - width, length, axis=dim))
    initial = arrange(lax.slice_in_dim(shard, 0, width, axis=dim))
    return lax.ppermute(last, axis, up), lax.ppermute(initial, axis, down)


def weno_side(minus_two, minus_one, centre, plus_one, plus_two):
    curve_zero = minus_two - 2.0 * minus_one + centre
    curve_one = minus_one - 2.0 * centre + plus_one
    curve_two = centre - 2.0 * plus_one + plus_two
    slope_zero = minus_two - 4.0 * minus_one + 3.0 * centre
    slope_one = minus_one - plus_one
    slope_two = 3.0 * centre - 4.0 * plus_one + plus_two
    beta_zero = 13.0 / 12.0 * curve_zero * curve_zero + 0.25 * slope_zero * slope_zero
    beta_one = 13.0 / 12.0 * curve_one * curve_one + 0.25 * slope_one * slope_one
    beta_two = 13.0 / 12.0 * curve_two * curve_two + 0.25 * slope_two * slope_two
    guard_zero = WENO_EPS + beta_zero
    guard_one = WENO_EPS + beta_one
    guard_two = WENO_EPS + beta_two
    guard_zero = guard_zero * guard_zero
    guard_one = guard_one * guard_one
    guard_two = guard_two * guard_two
    cross_zero = guard_one * guard_two
    cross_one = 6.0 * (guard_zero * guard_two)
    cross_two = 3.0 * (guard_zero * guard_one)
    blended = cross_zero * (2.0 * minus_two - 7.0 * minus_one + 11.0 * centre)
    blended = blended + cross_one * (-minus_one + 5.0 * centre + 2.0 * plus_one)
    blended = blended + cross_two * (2.0 * centre + 5.0 * plus_one - plus_two)
    return blended / (6.0 * (cross_zero + cross_one + cross_two))


HALO = 8
CHUNK = 8


def upwind_divergence(ext_ref, vel_ref, flux_ref, rows):
    faces = flux_ref.shape[0]
    for low in range(0, faces, CHUNK):

        def cut(offset):
            return ext_ref[pl.ds(HALO - 3 + offset + low, CHUNK), :]

        face_speed = 0.5 * (
            vel_ref[pl.ds(HALO - 1 + low, CHUNK), :] + vel_ref[pl.ds(HALO + low, CHUNK), :]
        )
        forward = face_speed >= 0.0
        stencil = [
            jnp.where(forward, cut(lower), cut(upper))
            for lower, upper in ((0, 5), (1, 4), (2, 3), (3, 2), (4, 1))
        ]
        flux_ref[pl.ds(low, CHUNK), :] = face_speed * weno_side(*stencil)
    return flux_ref[pl.ds(1, rows), :] - flux_ref[pl.ds(0, rows), :]


def transport_kernel(
    field_ref, speed_ref, top_ref, top_speed_ref, bottom_ref, bottom_speed_ref,
    left_ref, left_speed_ref, right_ref, right_speed_ref, out_ref,
    ext_ref, vel_ref, flux_ref,
):
    rows, cols = field_ref.shape[1], field_ref.shape[2]
    span = ext_ref.shape[0]
    tail = span - HALO - rows
    zeros = jnp.zeros((tail - HALO, cols), jnp.float32)
    field = field_ref[0]

    ext_ref[pl.ds(0, HALO), :] = top_ref[0]
    ext_ref[pl.ds(HALO, rows), :] = field
    ext_ref[pl.ds(HALO + rows, HALO), :] = bottom_ref[0]
    ext_ref[pl.ds(2 * HALO + rows, tail - HALO), :] = zeros
    vel_ref[pl.ds(0, HALO), :] = top_speed_ref[0]
    vel_ref[pl.ds(HALO, rows), :] = speed_ref[0]
    vel_ref[pl.ds(HALO + rows, HALO), :] = bottom_speed_ref[0]
    vel_ref[pl.ds(2 * HALO + rows, tail - HALO), :] = zeros
    along_axial = upwind_divergence(ext_ref, vel_ref, flux_ref, rows)

    ext_ref[pl.ds(0, HALO), :] = left_ref[0]
    ext_ref[pl.ds(HALO, cols), :] = field.T
    ext_ref[pl.ds(HALO + cols, HALO), :] = right_ref[0]
    vel_ref[pl.ds(0, HALO), :] = left_speed_ref[0]
    vel_ref[pl.ds(HALO, cols), :] = speed_ref[1].T
    vel_ref[pl.ds(HALO + cols, HALO), :] = right_speed_ref[0]
    along_radial = upwind_divergence(ext_ref, vel_ref, flux_ref, cols).T

    moved = field - TIME_STEP * (along_axial + along_radial)
    out_ref[:, pl.ds(pl.program_id(0), 1), :] = moved[:, None, :]


def transport(species, speed, width=3):
    species_count, rows, cols = species.shape
    assert rows == cols and rows % CHUNK == 0
    axial_edges = jnp.concatenate([species, speed[0:1]], axis=0)
    top, bottom = edge_layers(axial_edges, "axial", 1, width)
    radial_edges = jnp.concatenate([species, speed[1:2]], axis=0)
    left, right = edge_layers(
        radial_edges, "radial", 2, width, lambda layers: layers.reshape(layers.shape[0], -1)
    )
    left, right = (
        jnp.swapaxes(layers.reshape(species_count + 1, rows, width), 1, 2)
        for layers in (left, right)
    )
    before = ((0, 0), (HALO - width, 0), (0, 0))
    after = ((0, 0), (0, HALO - width), (0, 0))
    top, left = (jnp.pad(top, before), jnp.pad(left, before))
    bottom, right = (jnp.pad(bottom, after), jnp.pad(right, after))
    faces = rows + CHUNK
    span = HALO + faces + HALO
    plane = pl.BlockSpec((1, rows, cols), lambda s: (s, 0, 0))
    speeds = pl.BlockSpec((2, rows, cols), lambda s: (0, 0, 0))
    edge = pl.BlockSpec((1, HALO, cols), lambda s: (s, 0, 0))
    edge_speed = pl.BlockSpec((1, HALO, cols), lambda s: (species_count, 0, 0))
    moved_rows = pl.pallas_call(
        transport_kernel,
        grid=(species_count,),
        in_specs=[plane, speeds] + [edge, edge_speed] * 4,
        out_specs=pl.BlockSpec((rows, species_count, cols), lambda s: (0, 0, 0)),
        out_shape=jax.ShapeDtypeStruct((rows, species_count, cols), jnp.float32),
        scratch_shapes=[
            pltpu.VMEM((span, cols), jnp.float32),
            pltpu.VMEM((span, cols), jnp.float32),
            pltpu.VMEM((faces, cols), jnp.float32),
        ],
    )(species, speed, top, top, bottom, bottom, left, left, right, right)
    return jnp.transpose(moved_rows, (1, 0, 2))


def kinetics_advance(
    starting_composition_field,
    thermal_field,
    linearized_kinetics_operator,
    frozen_jacobian_inverse_addend,
):
    acceleration_factor = jnp.exp(-ARRHENIUS_BARRIER / thermal_field)
    current = starting_composition_field
    for newton_step in range(ITERS):
        source = jnp.tensordot(
            linearized_kinetics_operator, current, axes=(1, 0), precision=CHEMISTRY_PRECISION
        ) - jnp.tanh(current)
        defect = current - starting_composition_field - CHEM_STEP * acceleration_factor * source
        current = (
            current
            - defect
            - jnp.tensordot(frozen_jacobian_inverse_addend, defect, axes=(1, 0), precision=CHEMISTRY_PRECISION)
        )
    return current


def absorbance_profile(field, molar_absorptivity_table, spokewise_sightline_length):
    mixed = jnp.tensordot(molar_absorptivity_table, field, axes=(1, 0), precision=HIGHEST)
    return jnp.dot(mixed, spokewise_sightline_length, precision=HIGHEST)


def butterfly_sum(part, axis):
    peers, stride = (lax.axis_size(axis), 1)
    if peers & (peers - 1):
        return lax.psum(part, axis)
    while stride < peers:
        pairs = [(j, j ^ stride) for j in range(peers)]
        part = part + lax.ppermute(part, axis, pairs)
        stride *= 2
    return part


def doubling_gather(part, axis):
    peers, stride = (lax.axis_size(axis), 1)
    if peers & (peers - 1):
        return lax.all_gather(part, axis, axis=1, tiled=True)
    position = lax.axis_index(axis)
    blocks = part[None]
    while stride < peers:
        pairs = [(j, j ^ stride) for j in range(peers)]
        other = lax.ppermute(blocks, axis, pairs)
        upper = (position // stride) % 2 == 1
        blocks = jnp.where(
            upper, jnp.concatenate([other, blocks], 0), jnp.concatenate([blocks, other], 0)
        )
        stride *= 2
    return jnp.transpose(blocks, (1, 0, 2)).reshape(part.shape[0], -1)


def gathered_profile(profile):
    return doubling_gather(butterfly_sum(profile, "radial"), "axial")


def local(
    composition_deviations,
    flow_speed_vector,
    thermal_field,
    linearized_kinetics_operator,
    frozen_jacobian_inverse_addend,
    rigid_block_indicator,
    molar_absorptivity_table,
    spokewise_sightline_length,
    sightline_lengthwise_index,
    observed_absorbance_traces,
):
    advected_composition_field = transport(composition_deviations, flow_speed_vector)
    combusted_composition_field = kinetics_advance(
        advected_composition_field,
        thermal_field,
        linearized_kinetics_operator,
        frozen_jacobian_inverse_addend,
    )
    flag_cells = jnp.repeat(
        jnp.repeat(rigid_block_indicator, TILE_ROWS, axis=0),
        advected_composition_field.shape[2],
        axis=1,
    )
    species_out = jnp.where(
        flag_cells[None] > 0, combusted_composition_field, advected_composition_field
    )
    path_scale = 1.0 / math.sqrt(advected_composition_field.shape[2] * lax.axis_size("radial"))
    profile = (
        absorbance_profile(species_out, molar_absorptivity_table, spokewise_sightline_length)
        * path_scale
    )
    whole_profile = gathered_profile(profile)
    device = lax.axis_index(("axial", "radial"))
    sample_count = observed_absorbance_traces.shape[1]
    own_rows = lax.dynamic_slice_in_dim(
        sightline_lengthwise_index, device * sample_count, sample_count, 1
    )
    cells = lax.broadcasted_iota(jnp.int32, (1, whole_profile.shape[1], 1), 1)
    values = jnp.sum(
        jnp.where(own_rows[:, None, :] == cells, whole_profile[:, :, None], 0.0), axis=1
    )
    return (species_out, values - observed_absorbance_traces)


def solution(mesh):
    in_specs = (
        P(None, "axial", "radial"),
        P(None, "axial", "radial"),
        P("axial", "radial"),
        P(),
        P(),
        P("axial", "radial"),
        P(),
        P("radial"),
        P(),
        P(None, ("axial", "radial")),
    )
    out_specs = (P(None, "axial", "radial"), P(None, ("axial", "radial")))
    return jax.shard_map(local, mesh=mesh, in_specs=in_specs, out_specs=out_specs, check_vma=False)
```

```python
import math

import jax
import jax.numpy as jnp
from jax import lax
from jax.sharding import PartitionSpec as P
from jax.experimental import pallas as pl
from jax.experimental.pallas import tpu as pltpu

TILE_ROWS = 2
ITERS = 3


TIME_STEP = 0.4
CHEM_STEP = 0.5
ARRHENIUS_BARRIER = 1.0
WENO_EPS = 1e-06
HIGHEST = lax.Precision.HIGHEST
CHEMISTRY_PRECISION = lax.Precision.HIGH


def weno_side(minus_two, minus_one, centre, plus_one, plus_two):
    curve_zero = minus_two - 2.0 * minus_one + centre
    curve_one = minus_one - 2.0 * centre + plus_one
    curve_two = centre - 2.0 * plus_one + plus_two
    slope_zero = minus_two - 4.0 * minus_one + 3.0 * centre
    slope_one = minus_one - plus_one
    slope_two = 3.0 * centre - 4.0 * plus_one + plus_two
    beta_zero = 13.0 / 12.0 * curve_zero * curve_zero + 0.25 * slope_zero * slope_zero
    beta_one = 13.0 / 12.0 * curve_one * curve_one + 0.25 * slope_one * slope_one
    beta_two = 13.0 / 12.0 * curve_two * curve_two + 0.25 * slope_two * slope_two
    guard_zero = WENO_EPS + beta_zero
    guard_one = WENO_EPS + beta_one
    guard_two = WENO_EPS + beta_two
    guard_zero = guard_zero * guard_zero
    guard_one = guard_one * guard_one
    guard_two = guard_two * guard_two
    cross_zero = guard_one * guard_two
    cross_one = 6.0 * (guard_zero * guard_two)
    cross_two = 3.0 * (guard_zero * guard_one)
    blended = cross_zero * (2.0 * minus_two - 7.0 * minus_one + 11.0 * centre)
    blended = blended + cross_one * (-minus_one + 5.0 * centre + 2.0 * plus_one)
    blended = blended + cross_two * (2.0 * centre + 5.0 * plus_one - plus_two)
    return blended / (6.0 * (cross_zero + cross_one + cross_two))


HALO = 8
CHUNK = 8


def upwind_divergence(ext_ref, vel_ref, flux_ref, rows):
    faces = flux_ref.shape[0]
    for low in range(0, faces, CHUNK):

        def cut(offset):
            return ext_ref[pl.ds(HALO - 3 + offset + low, CHUNK), :]

        face_speed = 0.5 * (
            vel_ref[pl.ds(HALO - 1 + low, CHUNK), :] + vel_ref[pl.ds(HALO + low, CHUNK), :]
        )
        forward = face_speed >= 0.0
        stencil = [
            jnp.where(forward, cut(lower), cut(upper))
            for lower, upper in ((0, 5), (1, 4), (2, 3), (3, 2), (4, 1))
        ]
        flux_ref[pl.ds(low, CHUNK), :] = face_speed * weno_side(*stencil)
    return flux_ref[pl.ds(1, rows), :] - flux_ref[pl.ds(0, rows), :]


def transport_kernel(
    field_ref, speed_ref, top_ref, top_speed_ref, bottom_ref, bottom_speed_ref,
    left_ref, left_speed_ref, right_ref, right_speed_ref, out_ref,
    ext_ref, vel_ref, flux_ref,
):
    rows, cols = field_ref.shape[1], field_ref.shape[2]
    span = ext_ref.shape[0]
    tail = span - HALO - rows
    zeros = jnp.zeros((tail - HALO, cols), jnp.float32)
    field = field_ref[0]

    ext_ref[pl.ds(0, HALO), :] = top_ref[0]
    ext_ref[pl.ds(HALO, rows), :] = field
    ext_ref[pl.ds(HALO + rows, HALO), :] = bottom_ref[0]
    ext_ref[pl.ds(2 * HALO + rows, tail - HALO), :] = zeros
    vel_ref[pl.ds(0, HALO), :] = top_speed_ref[0]
    vel_ref[pl.ds(HALO, rows), :] = speed_ref[0]
    vel_ref[pl.ds(HALO + rows, HALO), :] = bottom_speed_ref[0]
    vel_ref[pl.ds(2 * HALO + rows, tail - HALO), :] = zeros
    along_axial = upwind_divergence(ext_ref, vel_ref, flux_ref, rows)

    ext_ref[pl.ds(0, HALO), :] = left_ref[0]
    ext_ref[pl.ds(HALO, cols), :] = field.T
    ext_ref[pl.ds(HALO + cols, HALO), :] = right_ref[0]
    vel_ref[pl.ds(0, HALO), :] = left_speed_ref[0]
    vel_ref[pl.ds(HALO, cols), :] = speed_ref[1].T
    vel_ref[pl.ds(HALO + cols, HALO), :] = right_speed_ref[0]
    along_radial = upwind_divergence(ext_ref, vel_ref, flux_ref, cols).T

    moved = field - TIME_STEP * (along_axial + along_radial)
    out_ref[:, pl.ds(pl.program_id(0), 1), :] = moved[:, None, :]


def edge_columns_kernel(field_ref, high_ref, low_ref):
    flipped = field_ref[0].T
    high_ref[0] = flipped[flipped.shape[0] - HALO :]
    low_ref[0] = flipped[:HALO]


def edge_columns(species):
    species_count, rows, cols = species.shape
    edge = pl.BlockSpec((1, HALO, rows), lambda s: (s, 0, 0))
    return pl.pallas_call(
        edge_columns_kernel,
        grid=(species_count,),
        in_specs=[pl.BlockSpec((1, rows, cols), lambda s: (s, 0, 0))],
        out_specs=[edge, edge],
        out_shape=[jax.ShapeDtypeStruct((species_count, HALO, rows), jnp.float32)] * 2,
    )(species)


def neighbour_layers(high, low, axis):
    peers = lax.axis_size(axis)
    up = [(i, i + 1) for i in range(peers - 1)]
    down = [(j, i) for i, j in up]
    return lax.ppermute(high, axis, up), lax.ppermute(low, axis, down)


def transport(species, speed):
    species_count, rows, cols = species.shape
    assert rows == cols and rows % CHUNK == 0 and rows >= HALO
    top, bottom = neighbour_layers(
        jnp.concatenate([species[:, rows - HALO :], speed[0:1, rows - HALO :]], axis=0),
        jnp.concatenate([species[:, :HALO], speed[0:1, :HALO]], axis=0),
        "axial",
    )
    high_columns, low_columns = edge_columns(species)
    radial_speed = speed[1].T
    left, right = neighbour_layers(
        jnp.concatenate([high_columns, radial_speed[None, cols - HALO :]], axis=0),
        jnp.concatenate([low_columns, radial_speed[None, :HALO]], axis=0),
        "radial",
    )
    faces = rows + CHUNK
    span = HALO + faces + HALO
    plane = pl.BlockSpec((1, rows, cols), lambda s: (s, 0, 0))
    speeds = pl.BlockSpec((2, rows, cols), lambda s: (0, 0, 0))
    edge = pl.BlockSpec((1, HALO, cols), lambda s: (s, 0, 0))
    edge_speed = pl.BlockSpec((1, HALO, cols), lambda s: (species_count, 0, 0))
    moved_rows = pl.pallas_call(
        transport_kernel,
        grid=(species_count,),
        in_specs=[plane, speeds] + [edge, edge_speed] * 4,
        out_specs=pl.BlockSpec((rows, species_count, cols), lambda s: (0, 0, 0)),
        out_shape=jax.ShapeDtypeStruct((rows, species_count, cols), jnp.float32),
        scratch_shapes=[
            pltpu.VMEM((span, cols), jnp.float32),
            pltpu.VMEM((span, cols), jnp.float32),
            pltpu.VMEM((faces, cols), jnp.float32),
        ],
    )(species, speed, top, top, bottom, bottom, left, left, right, right)
    return jnp.transpose(moved_rows, (1, 0, 2))


def kinetics_advance(
    starting_composition_field,
    thermal_field,
    linearized_kinetics_operator,
    frozen_jacobian_inverse_addend,
):
    acceleration_factor = jnp.exp(-ARRHENIUS_BARRIER / thermal_field)
    current = starting_composition_field
    for newton_step in range(ITERS):
        source = jnp.tensordot(
            linearized_kinetics_operator, current, axes=(1, 0), precision=CHEMISTRY_PRECISION
        ) - jnp.tanh(current)
        defect = current - starting_composition_field - CHEM_STEP * acceleration_factor * source
        current = (
            current
            - defect
            - jnp.tensordot(frozen_jacobian_inverse_addend, defect, axes=(1, 0), precision=CHEMISTRY_PRECISION)
        )
    return current


def absorbance_profile(field, molar_absorptivity_table, spokewise_sightline_length):
    mixed = jnp.tensordot(molar_absorptivity_table, field, axes=(1, 0), precision=HIGHEST)
    return jnp.dot(mixed, spokewise_sightline_length, precision=HIGHEST)


def butterfly_sum(part, axis):
    peers, stride = (lax.axis_size(axis), 1)
    if peers & (peers - 1):
        return lax.psum(part, axis)
    while stride < peers:
        pairs = [(j, j ^ stride) for j in range(peers)]
        part = part + lax.ppermute(part, axis, pairs)
        stride *= 2
    return part


def doubling_gather(part, axis):
    peers, stride = (lax.axis_size(axis), 1)
    if peers & (peers - 1):
        return lax.all_gather(part, axis, axis=1, tiled=True)
    position = lax.axis_index(axis)
    blocks = part[None]
    while stride < peers:
        pairs = [(j, j ^ stride) for j in range(peers)]
        other = lax.ppermute(blocks, axis, pairs)
        upper = (position // stride) % 2 == 1
        blocks = jnp.where(
            upper, jnp.concatenate([other, blocks], 0), jnp.concatenate([blocks, other], 0)
        )
        stride *= 2
    return jnp.transpose(blocks, (1, 0, 2)).reshape(part.shape[0], -1)


def gathered_profile(profile):
    return doubling_gather(butterfly_sum(profile, "radial"), "axial")


def local(
    composition_deviations,
    flow_speed_vector,
    thermal_field,
    linearized_kinetics_operator,
    frozen_jacobian_inverse_addend,
    rigid_block_indicator,
    molar_absorptivity_table,
    spokewise_sightline_length,
    sightline_lengthwise_index,
    observed_absorbance_traces,
):
    advected_composition_field = transport(composition_deviations, flow_speed_vector)
    combusted_composition_field = kinetics_advance(
        advected_composition_field,
        thermal_field,
        linearized_kinetics_operator,
        frozen_jacobian_inverse_addend,
    )
    flag_cells = jnp.repeat(
        jnp.repeat(rigid_block_indicator, TILE_ROWS, axis=0),
        advected_composition_field.shape[2],
        axis=1,
    )
    species_out = jnp.where(
        flag_cells[None] > 0, combusted_composition_field, advected_composition_field
    )
    path_scale = 1.0 / math.sqrt(advected_composition_field.shape[2] * lax.axis_size("radial"))
    profile = (
        absorbance_profile(species_out, molar_absorptivity_table, spokewise_sightline_length)
        * path_scale
    )
    whole_profile = gathered_profile(profile)
    device = lax.axis_index(("axial", "radial"))
    sample_count = observed_absorbance_traces.shape[1]
    own_rows = lax.dynamic_slice_in_dim(
        sightline_lengthwise_index, device * sample_count, sample_count, 1
    )
    cells = lax.broadcasted_iota(jnp.int32, (1, whole_profile.shape[1], 1), 1)
    values = jnp.sum(
        jnp.where(own_rows[:, None, :] == cells, whole_profile[:, :, None], 0.0), axis=1
    )
    return (species_out, values - observed_absorbance_traces)


def solution(mesh):
    in_specs = (
        P(None, "axial", "radial"),
        P(None, "axial", "radial"),
        P("axial", "radial"),
        P(),
        P(),
        P("axial", "radial"),
        P(),
        P("radial"),
        P(),
        P(None, ("axial", "radial")),
    )
    out_specs = (P(None, "axial", "radial"), P(None, ("axial", "radial")))
    return jax.shard_map(local, mesh=mesh, in_specs=in_specs, out_specs=out_specs, check_vma=False)
```

```python
import math

import jax
import jax.numpy as jnp
from jax import lax
from jax.sharding import PartitionSpec as P
from jax.experimental import pallas as pl
from jax.experimental.pallas import tpu as pltpu

TILE_ROWS = 2
ITERS = 3


TIME_STEP = 0.4
CHEM_STEP = 0.5
ARRHENIUS_BARRIER = 1.0
WENO_EPS = 1e-06
HIGHEST = lax.Precision.HIGHEST
CHEMISTRY_PRECISION = lax.Precision.HIGH


def edge_layers(shard, axis, dim, width):
    peers, length = (lax.axis_size(axis), shard.shape[dim])
    up = [(i, i + 1) for i in range(peers - 1)]
    down = [(j, i) for i, j in up]
    last = lax.slice_in_dim(shard, length - width, length, axis=dim)
    initial = lax.slice_in_dim(shard, 0, width, axis=dim)
    return lax.ppermute(last, axis, up), lax.ppermute(initial, axis, down)


SCALED_EPS = WENO_EPS * 12.0 / 13.0
SLOPE_WEIGHT = 3.0 / 13.0


def weno_side(minus_two, minus_one, centre, plus_one, plus_two):
    curve_zero = (minus_two + centre) - (minus_one + minus_one)
    curve_one = (minus_one + plus_one) - (centre + centre)
    curve_two = (centre + plus_two) - (plus_one + plus_one)
    slope_zero = curve_zero + 2.0 * (centre - minus_one)
    slope_one = minus_one - plus_one
    slope_two = curve_two + 2.0 * (centre - plus_one)
    guard_zero = (SCALED_EPS + curve_zero * curve_zero) + SLOPE_WEIGHT * (slope_zero * slope_zero)
    guard_one = (SCALED_EPS + curve_one * curve_one) + SLOPE_WEIGHT * (slope_one * slope_one)
    guard_two = (SCALED_EPS + curve_two * curve_two) + SLOPE_WEIGHT * (slope_two * slope_two)
    guard_zero = guard_zero * guard_zero
    guard_one = guard_one * guard_one
    guard_two = guard_two * guard_two
    cross_zero = guard_one * guard_two
    cross_one = 6.0 * (guard_zero * guard_two)
    cross_two = 3.0 * (guard_zero * guard_one)
    blended = cross_zero * (curve_zero + 3.0 * slope_zero)
    blended = blended + cross_one * (curve_one - 3.0 * slope_one)
    blended = blended + cross_two * (curve_two - 3.0 * slope_two)
    return centre + blended / (12.0 * (cross_zero + cross_one + cross_two))


HALO = 8
CHUNK = 8


def upwind_divergence(ext_ref, vel_ref, flux_ref, rows):
    faces = flux_ref.shape[0]
    for low in range(0, faces, CHUNK):

        def cut(offset):
            return ext_ref[pl.ds(HALO - 3 + offset + low, CHUNK), :]

        face_speed = 0.5 * (
            vel_ref[pl.ds(HALO - 1 + low, CHUNK), :] + vel_ref[pl.ds(HALO + low, CHUNK), :]
        )
        forward = face_speed >= 0.0
        stencil = [
            jnp.where(forward, cut(lower), cut(upper))
            for lower, upper in ((0, 5), (1, 4), (2, 3), (3, 2), (4, 1))
        ]
        flux_ref[pl.ds(low, CHUNK), :] = face_speed * weno_side(*stencil)
    return flux_ref[pl.ds(1, rows), :] - flux_ref[pl.ds(0, rows), :]


def transport_kernel(
    field_ref, speed_ref, top_ref, top_speed_ref, bottom_ref, bottom_speed_ref,
    left_ref, left_speed_ref, right_ref, right_speed_ref, out_ref,
    ext_ref, vel_ref, flux_ref,
):
    rows, cols = field_ref.shape[1], field_ref.shape[2]
    span = ext_ref.shape[0]
    tail = span - HALO - rows
    zeros = jnp.zeros((tail - HALO, cols), jnp.float32)
    field = field_ref[0]

    ext_ref[pl.ds(0, HALO), :] = top_ref[0]
    ext_ref[pl.ds(HALO, rows), :] = field
    ext_ref[pl.ds(HALO + rows, HALO), :] = bottom_ref[0]
    ext_ref[pl.ds(2 * HALO + rows, tail - HALO), :] = zeros
    vel_ref[pl.ds(0, HALO), :] = top_speed_ref[0]
    vel_ref[pl.ds(HALO, rows), :] = speed_ref[0]
    vel_ref[pl.ds(HALO + rows, HALO), :] = bottom_speed_ref[0]
    vel_ref[pl.ds(2 * HALO + rows, tail - HALO), :] = zeros
    along_axial = upwind_divergence(ext_ref, vel_ref, flux_ref, rows)

    ext_ref[pl.ds(0, HALO), :] = left_ref[0]
    ext_ref[pl.ds(HALO, cols), :] = field.T
    ext_ref[pl.ds(HALO + cols, HALO), :] = right_ref[0]
    vel_ref[pl.ds(0, HALO), :] = left_speed_ref[0]
    vel_ref[pl.ds(HALO, cols), :] = speed_ref[1].T
    vel_ref[pl.ds(HALO + cols, HALO), :] = right_speed_ref[0]
    along_radial = upwind_divergence(ext_ref, vel_ref, flux_ref, cols).T

    moved = field - TIME_STEP * (along_axial + along_radial)
    out_ref[:, pl.ds(pl.program_id(0), 1), :] = moved[:, None, :]


def transport(species, speed, width=3):
    species_count, rows, cols = species.shape
    assert rows == cols and rows % CHUNK == 0
    axial_edges = jnp.concatenate([species, speed[0:1]], axis=0)
    top, bottom = edge_layers(axial_edges, "axial", 1, width)
    radial_edges = jnp.swapaxes(jnp.concatenate([species, speed[1:2]], axis=0), 1, 2)
    left, right = edge_layers(radial_edges, "radial", 1, width)
    before = ((0, 0), (HALO - width, 0), (0, 0))
    after = ((0, 0), (0, HALO - width), (0, 0))
    top, left = (jnp.pad(top, before), jnp.pad(left, before))
    bottom, right = (jnp.pad(bottom, after), jnp.pad(right, after))
    faces = rows + CHUNK
    span = HALO + faces + HALO
    plane = pl.BlockSpec((1, rows, cols), lambda s: (s, 0, 0))
    speeds = pl.BlockSpec((2, rows, cols), lambda s: (0, 0, 0))
    edge = pl.BlockSpec((1, HALO, cols), lambda s: (s, 0, 0))
    edge_speed = pl.BlockSpec((1, HALO, cols), lambda s: (species_count, 0, 0))
    moved_rows = pl.pallas_call(
        transport_kernel,
        grid=(species_count,),
        in_specs=[plane, speeds] + [edge, edge_speed] * 4,
        out_specs=pl.BlockSpec((rows, species_count, cols), lambda s: (0, 0, 0)),
        out_shape=jax.ShapeDtypeStruct((rows, species_count, cols), jnp.float32),
        scratch_shapes=[
            pltpu.VMEM((span, cols), jnp.float32),
            pltpu.VMEM((span, cols), jnp.float32),
            pltpu.VMEM((faces, cols), jnp.float32),
        ],
    )(species, speed, top, top, bottom, bottom, left, left, right, right)
    return jnp.transpose(moved_rows, (1, 0, 2))


def kinetics_advance(
    starting_composition_field,
    thermal_field,
    linearized_kinetics_operator,
    frozen_jacobian_inverse_addend,
):
    acceleration_factor = jnp.exp(-ARRHENIUS_BARRIER / thermal_field)
    current = starting_composition_field
    for newton_step in range(ITERS):
        source = jnp.tensordot(
            linearized_kinetics_operator, current, axes=(1, 0), precision=CHEMISTRY_PRECISION
        ) - jnp.tanh(current)
        defect = current - starting_composition_field - CHEM_STEP * acceleration_factor * source
        current = (
            current
            - defect
            - jnp.tensordot(frozen_jacobian_inverse_addend, defect, axes=(1, 0), precision=CHEMISTRY_PRECISION)
        )
    return current


def absorbance_profile(field, molar_absorptivity_table, spokewise_sightline_length):
    mixed = jnp.tensordot(molar_absorptivity_table, field, axes=(1, 0), precision=HIGHEST)
    return jnp.dot(mixed, spokewise_sightline_length, precision=HIGHEST)


def butterfly_sum(part, axis):
    peers, stride = (lax.axis_size(axis), 1)
    if peers & (peers - 1):
        return lax.psum(part, axis)
    while stride < peers:
        pairs = [(j, j ^ stride) for j in range(peers)]
        part = part + lax.ppermute(part, axis, pairs)
        stride *= 2
    return part


def doubling_gather(part, axis):
    peers, stride = (lax.axis_size(axis), 1)
    if peers & (peers - 1):
        return lax.all_gather(part, axis, axis=1, tiled=True)
    position = lax.axis_index(axis)
    blocks = part[None]
    while stride < peers:
        pairs = [(j, j ^ stride) for j in range(peers)]
        other = lax.ppermute(blocks, axis, pairs)
        upper = (position // stride) % 2 == 1
        blocks = jnp.where(
            upper, jnp.concatenate([other, blocks], 0), jnp.concatenate([blocks, other], 0)
        )
        stride *= 2
    return jnp.transpose(blocks, (1, 0, 2)).reshape(part.shape[0], -1)


def gathered_profile(profile):
    return doubling_gather(butterfly_sum(profile, "radial"), "axial")


def local(
    composition_deviations,
    flow_speed_vector,
    thermal_field,
    linearized_kinetics_operator,
    frozen_jacobian_inverse_addend,
    rigid_block_indicator,
    molar_absorptivity_table,
    spokewise_sightline_length,
    sightline_lengthwise_index,
    observed_absorbance_traces,
):
    advected_composition_field = transport(composition_deviations, flow_speed_vector)
    combusted_composition_field = kinetics_advance(
        advected_composition_field,
        thermal_field,
        linearized_kinetics_operator,
        frozen_jacobian_inverse_addend,
    )
    flag_cells = jnp.repeat(
        jnp.repeat(rigid_block_indicator, TILE_ROWS, axis=0),
        advected_composition_field.shape[2],
        axis=1,
    )
    species_out = jnp.where(
        flag_cells[None] > 0, combusted_composition_field, advected_composition_field
    )
    path_scale = 1.0 / math.sqrt(advected_composition_field.shape[2] * lax.axis_size("radial"))
    profile = (
        absorbance_profile(species_out, molar_absorptivity_table, spokewise_sightline_length)
        * path_scale
    )
    whole_profile = gathered_profile(profile)
    device = lax.axis_index(("axial", "radial"))
    sample_count = observed_absorbance_traces.shape[1]
    own_rows = lax.dynamic_slice_in_dim(
        sightline_lengthwise_index, device * sample_count, sample_count, 1
    )
    cells = lax.broadcasted_iota(jnp.int32, (1, whole_profile.shape[1], 1), 1)
    values = jnp.sum(
        jnp.where(own_rows[:, None, :] == cells, whole_profile[:, :, None], 0.0), axis=1
    )
    return (species_out, values - observed_absorbance_traces)


def solution(mesh):
    in_specs = (
        P(None, "axial", "radial"),
        P(None, "axial", "radial"),
        P("axial", "radial"),
        P(),
        P(),
        P("axial", "radial"),
        P(),
        P("radial"),
        P(),
        P(None, ("axial", "radial")),
    )
    out_specs = (P(None, "axial", "radial"), P(None, ("axial", "radial")))
    return jax.shard_map(local, mesh=mesh, in_specs=in_specs, out_specs=out_specs, check_vma=False)
```

```python
import math

import jax
import jax.numpy as jnp
from jax import lax
from jax.sharding import PartitionSpec as P
from jax.experimental import pallas as pl
from jax.experimental.pallas import tpu as pltpu

TILE_ROWS = 2
ITERS = 3


TIME_STEP = 0.4
CHEM_STEP = 0.5
ARRHENIUS_BARRIER = 1.0
WENO_EPS = 1e-06
HIGHEST = lax.Precision.HIGHEST
CHEMISTRY_PRECISION = lax.Precision.HIGH


def edge_layers(shard, axis, dim, width):
    peers, length = (lax.axis_size(axis), shard.shape[dim])
    up = [(i, i + 1) for i in range(peers - 1)]
    down = [(j, i) for i, j in up]
    last = lax.slice_in_dim(shard, length - width, length, axis=dim)
    initial = lax.slice_in_dim(shard, 0, width, axis=dim)
    return lax.ppermute(last, axis, up), lax.ppermute(initial, axis, down)


SCALED_EPS = WENO_EPS * 12.0 / 13.0
SLOPE_WEIGHT = 3.0 / 13.0


def weno_side(minus_two, minus_one, centre, plus_one, plus_two):
    curve_zero = (minus_two + centre) - (minus_one + minus_one)
    curve_one = (minus_one + plus_one) - (centre + centre)
    curve_two = (centre + plus_two) - (plus_one + plus_one)
    slope_zero = curve_zero + 2.0 * (centre - minus_one)
    slope_one = minus_one - plus_one
    slope_two = curve_two + 2.0 * (centre - plus_one)
    guard_zero = (SCALED_EPS + curve_zero * curve_zero) + SLOPE_WEIGHT * (slope_zero * slope_zero)
    guard_one = (SCALED_EPS + curve_one * curve_one) + SLOPE_WEIGHT * (slope_one * slope_one)
    guard_two = (SCALED_EPS + curve_two * curve_two) + SLOPE_WEIGHT * (slope_two * slope_two)
    guard_zero = guard_zero * guard_zero
    guard_one = guard_one * guard_one
    guard_two = guard_two * guard_two
    cross_zero = guard_one * guard_two
    cross_one = 6.0 * (guard_zero * guard_two)
    cross_two = 3.0 * (guard_zero * guard_one)
    blended = cross_zero * (curve_zero + 3.0 * slope_zero)
    blended = blended + cross_one * (curve_one - 3.0 * slope_one)
    blended = blended + cross_two * (curve_two - 3.0 * slope_two)
    return centre + blended / (12.0 * (cross_zero + cross_one + cross_two))


HALO = 8
CHUNK = 8


def upwind_divergence(ext_ref, vel_ref, flux_ref, rows):
    faces = flux_ref.shape[0]
    for low in range(0, faces, CHUNK):

        def cut(offset):
            return ext_ref[pl.ds(HALO - 3 + offset + low, CHUNK), :]

        face_speed = 0.5 * (
            vel_ref[pl.ds(HALO - 1 + low, CHUNK), :] + vel_ref[pl.ds(HALO + low, CHUNK), :]
        )
        forward = face_speed >= 0.0
        stencil = [
            jnp.where(forward, cut(lower), cut(upper))
            for lower, upper in ((0, 5), (1, 4), (2, 3), (3, 2), (4, 1))
        ]
        flux_ref[pl.ds(low, CHUNK), :] = face_speed * weno_side(*stencil)
    return flux_ref[pl.ds(1, rows), :] - flux_ref[pl.ds(0, rows), :]


def transport_kernel(
    field_ref, speed_ref, top_ref, top_speed_ref, bottom_ref, bottom_speed_ref,
    left_ref, left_speed_ref, right_ref, right_speed_ref, out_ref,
    ext_ref, vel_ref, flux_ref,
):
    rows, cols = field_ref.shape[1], field_ref.shape[2]
    span = ext_ref.shape[0]
    tail = span - HALO - rows
    zeros = jnp.zeros((tail - HALO, cols), jnp.float32)
    field = field_ref[0]

    ext_ref[pl.ds(0, HALO), :] = top_ref[0]
    ext_ref[pl.ds(HALO, rows), :] = field
    ext_ref[pl.ds(HALO + rows, HALO), :] = bottom_ref[0]
    ext_ref[pl.ds(2 * HALO + rows, tail - HALO), :] = zeros
    vel_ref[pl.ds(0, HALO), :] = top_speed_ref[0]
    vel_ref[pl.ds(HALO, rows), :] = speed_ref[0]
    vel_ref[pl.ds(HALO + rows, HALO), :] = bottom_speed_ref[0]
    vel_ref[pl.ds(2 * HALO + rows, tail - HALO), :] = zeros
    along_axial = upwind_divergence(ext_ref, vel_ref, flux_ref, rows)

    ext_ref[pl.ds(0, HALO), :] = left_ref[0]
    ext_ref[pl.ds(HALO, cols), :] = field.T
    ext_ref[pl.ds(HALO + cols, HALO), :] = right_ref[0]
    vel_ref[pl.ds(0, HALO), :] = left_speed_ref[0]
    vel_ref[pl.ds(HALO, cols), :] = speed_ref[1].T
    vel_ref[pl.ds(HALO + cols, HALO), :] = right_speed_ref[0]
    along_radial = upwind_divergence(ext_ref, vel_ref, flux_ref, cols).T

    moved = field - TIME_STEP * (along_axial + along_radial)
    out_ref[:, pl.ds(pl.program_id(0), 1), :] = moved[:, None, :]


def edge_columns(field, start, width):
    cols = field.shape[2]
    pick = lax.broadcasted_iota(jnp.int32, (width, cols), 1) == (
        lax.broadcasted_iota(jnp.int32, (width, cols), 0) + start
    )
    return jnp.einsum("kr,sar->ska", pick.astype(field.dtype), field, precision=HIGHEST)


def transport(species, speed, width=3):
    species_count, rows, cols = species.shape
    assert rows == cols and rows % CHUNK == 0
    axial_edges = jnp.concatenate([species, speed[0:1]], axis=0)
    top, bottom = edge_layers(axial_edges, "axial", 1, width)
    radial_edges = jnp.concatenate([species, speed[1:2]], axis=0)
    peers = lax.axis_size("radial")
    up = [(i, i + 1) for i in range(peers - 1)]
    down = [(j, i) for i, j in up]
    left = lax.ppermute(edge_columns(radial_edges, cols - width, width), "radial", up)
    right = lax.ppermute(edge_columns(radial_edges, 0, width), "radial", down)
    before = ((0, 0), (HALO - width, 0), (0, 0))
    after = ((0, 0), (0, HALO - width), (0, 0))
    top, left = (jnp.pad(top, before), jnp.pad(left, before))
    bottom, right = (jnp.pad(bottom, after), jnp.pad(right, after))
    faces = rows + CHUNK
    span = HALO + faces + HALO
    plane = pl.BlockSpec((1, rows, cols), lambda s: (s, 0, 0))
    speeds = pl.BlockSpec((2, rows, cols), lambda s: (0, 0, 0))
    edge = pl.BlockSpec((1, HALO, cols), lambda s: (s, 0, 0))
    edge_speed = pl.BlockSpec((1, HALO, cols), lambda s: (species_count, 0, 0))
    moved_rows = pl.pallas_call(
        transport_kernel,
        grid=(species_count,),
        in_specs=[plane, speeds] + [edge, edge_speed] * 4,
        out_specs=pl.BlockSpec((rows, species_count, cols), lambda s: (0, 0, 0)),
        out_shape=jax.ShapeDtypeStruct((rows, species_count, cols), jnp.float32),
        scratch_shapes=[
            pltpu.VMEM((span, cols), jnp.float32),
            pltpu.VMEM((span, cols), jnp.float32),
            pltpu.VMEM((faces, cols), jnp.float32),
        ],
    )(species, speed, top, top, bottom, bottom, left, left, right, right)
    return jnp.transpose(moved_rows, (1, 0, 2))


def kinetics_advance(
    starting_composition_field,
    thermal_field,
    linearized_kinetics_operator,
    frozen_jacobian_inverse_addend,
):
    acceleration_factor = jnp.exp(-ARRHENIUS_BARRIER / thermal_field)
    current = starting_composition_field
    for newton_step in range(ITERS):
        source = jnp.tensordot(
            linearized_kinetics_operator, current, axes=(1, 0), precision=CHEMISTRY_PRECISION
        ) - jnp.tanh(current)
        defect = current - starting_composition_field - CHEM_STEP * acceleration_factor * source
        current = (
            current
            - defect
            - jnp.tensordot(frozen_jacobian_inverse_addend, defect, axes=(1, 0), precision=CHEMISTRY_PRECISION)
        )
    return current


def absorbance_profile(field, molar_absorptivity_table, spokewise_sightline_length):
    mixed = jnp.tensordot(molar_absorptivity_table, field, axes=(1, 0), precision=HIGHEST)
    return jnp.dot(mixed, spokewise_sightline_length, precision=HIGHEST)


def butterfly_sum(part, axis):
    peers, stride = (lax.axis_size(axis), 1)
    if peers & (peers - 1):
        return lax.psum(part, axis)
    while stride < peers:
        pairs = [(j, j ^ stride) for j in range(peers)]
        part = part + lax.ppermute(part, axis, pairs)
        stride *= 2
    return part


def doubling_gather(part, axis):
    peers, stride = (lax.axis_size(axis), 1)
    if peers & (peers - 1):
        return lax.all_gather(part, axis, axis=1, tiled=True)
    position = lax.axis_index(axis)
    blocks = part[None]
    while stride < peers:
        pairs = [(j, j ^ stride) for j in range(peers)]
        other = lax.ppermute(blocks, axis, pairs)
        upper = (position // stride) % 2 == 1
        blocks = jnp.where(
            upper, jnp.concatenate([other, blocks], 0), jnp.concatenate([blocks, other], 0)
        )
        stride *= 2
    return jnp.transpose(blocks, (1, 0, 2)).reshape(part.shape[0], -1)


def gathered_profile(profile):
    return doubling_gather(butterfly_sum(profile, "radial"), "axial")


def local(
    composition_deviations,
    flow_speed_vector,
    thermal_field,
    linearized_kinetics_operator,
    frozen_jacobian_inverse_addend,
    rigid_block_indicator,
    molar_absorptivity_table,
    spokewise_sightline_length,
    sightline_lengthwise_index,
    observed_absorbance_traces,
):
    advected_composition_field = transport(composition_deviations, flow_speed_vector)
    combusted_composition_field = kinetics_advance(
        advected_composition_field,
        thermal_field,
        linearized_kinetics_operator,
        frozen_jacobian_inverse_addend,
    )
    flag_cells = jnp.repeat(
        jnp.repeat(rigid_block_indicator, TILE_ROWS, axis=0),
        advected_composition_field.shape[2],
        axis=1,
    )
    species_out = jnp.where(
        flag_cells[None] > 0, combusted_composition_field, advected_composition_field
    )
    path_scale = 1.0 / math.sqrt(advected_composition_field.shape[2] * lax.axis_size("radial"))
    profile = (
        absorbance_profile(species_out, molar_absorptivity_table, spokewise_sightline_length)
        * path_scale
    )
    whole_profile = gathered_profile(profile)
    device = lax.axis_index(("axial", "radial"))
    sample_count = observed_absorbance_traces.shape[1]
    own_rows = lax.dynamic_slice_in_dim(
        sightline_lengthwise_index, device * sample_count, sample_count, 1
    )
    cells = lax.broadcasted_iota(jnp.int32, (1, whole_profile.shape[1], 1), 1)
    values = jnp.sum(
        jnp.where(own_rows[:, None, :] == cells, whole_profile[:, :, None], 0.0), axis=1
    )
    return (species_out, values - observed_absorbance_traces)


def solution(mesh):
    in_specs = (
        P(None, "axial", "radial"),
        P(None, "axial", "radial"),
        P("axial", "radial"),
        P(),
        P(),
        P("axial", "radial"),
        P(),
        P("radial"),
        P(),
        P(None, ("axial", "radial")),
    )
    out_specs = (P(None, "axial", "radial"), P(None, ("axial", "radial")))
    return jax.shard_map(local, mesh=mesh, in_specs=in_specs, out_specs=out_specs, check_vma=False)
```

```python
import math

import jax
import jax.numpy as jnp
from jax import lax
from jax.sharding import PartitionSpec as P
from jax.experimental import pallas as pl
from jax.experimental.pallas import tpu as pltpu

TILE_ROWS = 2
ITERS = 3


TIME_STEP = 0.4
CHEM_STEP = 0.5
ARRHENIUS_BARRIER = 1.0
WENO_EPS = 1e-06
HIGHEST = lax.Precision.HIGHEST
CHEMISTRY_PRECISION = lax.Precision.HIGH


def edge_layers(shard, axis, dim, width):
    peers, length = (lax.axis_size(axis), shard.shape[dim])
    up = [(i, i + 1) for i in range(peers - 1)]
    down = [(j, i) for i, j in up]
    last = lax.slice_in_dim(shard, length - width, length, axis=dim)
    initial = lax.slice_in_dim(shard, 0, width, axis=dim)
    return lax.ppermute(last, axis, up), lax.ppermute(initial, axis, down)


SCALED_EPS = WENO_EPS * 12.0 / 13.0
SLOPE_WEIGHT = 3.0 / 13.0


def weno_side(minus_two, minus_one, centre, plus_one, plus_two):
    curve_zero = (minus_two + centre) - (minus_one + minus_one)
    curve_one = (minus_one + plus_one) - (centre + centre)
    curve_two = (centre + plus_two) - (plus_one + plus_one)
    slope_zero = curve_zero + 2.0 * (centre - minus_one)
    slope_one = minus_one - plus_one
    slope_two = curve_two + 2.0 * (centre - plus_one)
    guard_zero = (SCALED_EPS + curve_zero * curve_zero) + SLOPE_WEIGHT * (slope_zero * slope_zero)
    guard_one = (SCALED_EPS + curve_one * curve_one) + SLOPE_WEIGHT * (slope_one * slope_one)
    guard_two = (SCALED_EPS + curve_two * curve_two) + SLOPE_WEIGHT * (slope_two * slope_two)
    guard_zero = guard_zero * guard_zero
    guard_one = guard_one * guard_one
    guard_two = guard_two * guard_two
    cross_zero = guard_one * guard_two
    cross_one = 6.0 * (guard_zero * guard_two)
    cross_two = 3.0 * (guard_zero * guard_one)
    blended = cross_zero * (curve_zero + 3.0 * slope_zero)
    blended = blended + cross_one * (curve_one - 3.0 * slope_one)
    blended = blended + cross_two * (curve_two - 3.0 * slope_two)
    return centre + blended / (12.0 * (cross_zero + cross_one + cross_two))


HALO = 8
CHUNK = 8


def upwind_divergence(ext_ref, vel_ref, flux_ref, rows):
    faces = flux_ref.shape[0]
    for low in range(0, faces, CHUNK):

        def cut(offset):
            return ext_ref[pl.ds(HALO - 3 + offset + low, CHUNK), :]

        face_speed = 0.5 * (
            vel_ref[pl.ds(HALO - 1 + low, CHUNK), :] + vel_ref[pl.ds(HALO + low, CHUNK), :]
        )
        forward = face_speed >= 0.0
        stencil = [
            jnp.where(forward, cut(lower), cut(upper))
            for lower, upper in ((0, 5), (1, 4), (2, 3), (3, 2), (4, 1))
        ]
        flux_ref[pl.ds(low, CHUNK), :] = face_speed * weno_side(*stencil)
    return flux_ref[pl.ds(1, rows), :] - flux_ref[pl.ds(0, rows), :]


def transport_kernel(
    field_ref, speed_ref, top_ref, top_speed_ref, bottom_ref, bottom_speed_ref,
    left_ref, left_speed_ref, right_ref, right_speed_ref, out_ref,
    ext_ref, vel_ref, flux_ref,
):
    rows, cols = field_ref.shape[1], field_ref.shape[2]
    width = top_ref.shape[1]
    span = ext_ref.shape[0]
    field = field_ref[0]

    for scratch in (ext_ref, vel_ref):
        scratch[pl.ds(0, HALO), :] = jnp.zeros((HALO, cols), jnp.float32)
        scratch[pl.ds(HALO + rows, span - HALO - rows), :] = jnp.zeros(
            (span - HALO - rows, cols), jnp.float32
        )
    ext_ref[pl.ds(HALO - width, width), :] = top_ref[0]
    ext_ref[pl.ds(HALO, rows), :] = field
    ext_ref[pl.ds(HALO + rows, width), :] = bottom_ref[0]
    vel_ref[pl.ds(HALO - width, width), :] = top_speed_ref[0]
    vel_ref[pl.ds(HALO, rows), :] = speed_ref[0]
    vel_ref[pl.ds(HALO + rows, width), :] = bottom_speed_ref[0]
    along_axial = upwind_divergence(ext_ref, vel_ref, flux_ref, rows)

    ext_ref[pl.ds(HALO - width, width), :] = left_ref[0]
    ext_ref[pl.ds(HALO, cols), :] = field.T
    ext_ref[pl.ds(HALO + cols, width), :] = right_ref[0]
    vel_ref[pl.ds(HALO - width, width), :] = left_speed_ref[0]
    vel_ref[pl.ds(HALO, cols), :] = speed_ref[1].T
    vel_ref[pl.ds(HALO + cols, width), :] = right_speed_ref[0]
    along_radial = upwind_divergence(ext_ref, vel_ref, flux_ref, cols).T

    moved = field - TIME_STEP * (along_axial + along_radial)
    out_ref[:, pl.ds(pl.program_id(0), 1), :] = moved[:, None, :]


def edge_columns(field, start, width):
    cols = field.shape[2]
    pick = lax.broadcasted_iota(jnp.int32, (width, cols), 1) == (
        lax.broadcasted_iota(jnp.int32, (width, cols), 0) + start
    )
    return jnp.einsum("kr,sar->ska", pick.astype(field.dtype), field, precision=HIGHEST)


def transport(species, speed, width=3):
    species_count, rows, cols = species.shape
    assert rows == cols and rows % CHUNK == 0
    axial_edges = jnp.concatenate([species, speed[0:1]], axis=0)
    top, bottom = edge_layers(axial_edges, "axial", 1, width)
    radial_edges = jnp.concatenate([species, speed[1:2]], axis=0)
    peers = lax.axis_size("radial")
    up = [(i, i + 1) for i in range(peers - 1)]
    down = [(j, i) for i, j in up]
    left = lax.ppermute(edge_columns(radial_edges, cols - width, width), "radial", up)
    right = lax.ppermute(edge_columns(radial_edges, 0, width), "radial", down)
    faces = rows + CHUNK
    span = HALO + faces + HALO
    plane = pl.BlockSpec((1, rows, cols), lambda s: (s, 0, 0))
    speeds = pl.BlockSpec((2, rows, cols), lambda s: (0, 0, 0))
    edge = pl.BlockSpec((1, width, cols), lambda s: (s, 0, 0))
    edge_speed = pl.BlockSpec((1, width, cols), lambda s: (species_count, 0, 0))
    moved_rows = pl.pallas_call(
        transport_kernel,
        grid=(species_count,),
        in_specs=[plane, speeds] + [edge, edge_speed] * 4,
        out_specs=pl.BlockSpec((rows, species_count, cols), lambda s: (0, 0, 0)),
        out_shape=jax.ShapeDtypeStruct((rows, species_count, cols), jnp.float32),
        scratch_shapes=[
            pltpu.VMEM((span, cols), jnp.float32),
            pltpu.VMEM((span, cols), jnp.float32),
            pltpu.VMEM((faces, cols), jnp.float32),
        ],
    )(species, speed, top, top, bottom, bottom, left, left, right, right)
    return jnp.transpose(moved_rows, (1, 0, 2))


def kinetics_advance(
    starting_composition_field,
    thermal_field,
    linearized_kinetics_operator,
    frozen_jacobian_inverse_addend,
):
    acceleration_factor = jnp.exp(-ARRHENIUS_BARRIER / thermal_field)
    current = starting_composition_field
    for newton_step in range(ITERS):
        source = jnp.tensordot(
            linearized_kinetics_operator, current, axes=(1, 0), precision=CHEMISTRY_PRECISION
        ) - jnp.tanh(current)
        defect = current - starting_composition_field - CHEM_STEP * acceleration_factor * source
        current = (
            current
            - defect
            - jnp.tensordot(frozen_jacobian_inverse_addend, defect, axes=(1, 0), precision=CHEMISTRY_PRECISION)
        )
    return current


def absorbance_profile(field, molar_absorptivity_table, spokewise_sightline_length):
    mixed = jnp.tensordot(molar_absorptivity_table, field, axes=(1, 0), precision=HIGHEST)
    return jnp.dot(mixed, spokewise_sightline_length, precision=HIGHEST)


def butterfly_sum(part, axis):
    peers, stride = (lax.axis_size(axis), 1)
    if peers & (peers - 1):
        return lax.psum(part, axis)
    while stride < peers:
        pairs = [(j, j ^ stride) for j in range(peers)]
        part = part + lax.ppermute(part, axis, pairs)
        stride *= 2
    return part


def doubling_gather(part, axis):
    peers, stride = (lax.axis_size(axis), 1)
    if peers & (peers - 1):
        return lax.all_gather(part, axis, axis=1, tiled=True)
    position = lax.axis_index(axis)
    blocks = part[None]
    while stride < peers:
        pairs = [(j, j ^ stride) for j in range(peers)]
        other = lax.ppermute(blocks, axis, pairs)
        upper = (position // stride) % 2 == 1
        blocks = jnp.where(
            upper, jnp.concatenate([other, blocks], 0), jnp.concatenate([blocks, other], 0)
        )
        stride *= 2
    return jnp.transpose(blocks, (1, 0, 2)).reshape(part.shape[0], -1)


def gathered_profile(profile):
    return doubling_gather(butterfly_sum(profile, "radial"), "axial")


def local(
    composition_deviations,
    flow_speed_vector,
    thermal_field,
    linearized_kinetics_operator,
    frozen_jacobian_inverse_addend,
    rigid_block_indicator,
    molar_absorptivity_table,
    spokewise_sightline_length,
    sightline_lengthwise_index,
    observed_absorbance_traces,
):
    advected_composition_field = transport(composition_deviations, flow_speed_vector)
    combusted_composition_field = kinetics_advance(
        advected_composition_field,
        thermal_field,
        linearized_kinetics_operator,
        frozen_jacobian_inverse_addend,
    )
    flag_cells = jnp.repeat(
        jnp.repeat(rigid_block_indicator, TILE_ROWS, axis=0),
        advected_composition_field.shape[2],
        axis=1,
    )
    species_out = jnp.where(
        flag_cells[None] > 0, combusted_composition_field, advected_composition_field
    )
    path_scale = 1.0 / math.sqrt(advected_composition_field.shape[2] * lax.axis_size("radial"))
    profile = (
        absorbance_profile(species_out, molar_absorptivity_table, spokewise_sightline_length)
        * path_scale
    )
    whole_profile = gathered_profile(profile)
    device = lax.axis_index(("axial", "radial"))
    sample_count = observed_absorbance_traces.shape[1]
    own_rows = lax.dynamic_slice_in_dim(
        sightline_lengthwise_index, device * sample_count, sample_count, 1
    )
    cells = lax.broadcasted_iota(jnp.int32, (1, whole_profile.shape[1], 1), 1)
    values = jnp.sum(
        jnp.where(own_rows[:, None, :] == cells, whole_profile[:, :, None], 0.0), axis=1
    )
    return (species_out, values - observed_absorbance_traces)


def solution(mesh):
    in_specs = (
        P(None, "axial", "radial"),
        P(None, "axial", "radial"),
        P("axial", "radial"),
        P(),
        P(),
        P("axial", "radial"),
        P(),
        P("radial"),
        P(),
        P(None, ("axial", "radial")),
    )
    out_specs = (P(None, "axial", "radial"), P(None, ("axial", "radial")))
    return jax.shard_map(local, mesh=mesh, in_specs=in_specs, out_specs=out_specs, check_vma=False)
```

```python
import math

import jax
import jax.numpy as jnp
from jax import lax
from jax.sharding import PartitionSpec as P
from jax.experimental import pallas as pl
from jax.experimental.pallas import tpu as pltpu

TILE_ROWS = 2
ITERS = 3


TIME_STEP = 0.4
CHEM_STEP = 0.5
ARRHENIUS_BARRIER = 1.0
WENO_EPS = 1e-06
HIGHEST = lax.Precision.HIGHEST
CHEMISTRY_PRECISION = lax.Precision.HIGH


def edge_layers(shard, axis, dim, width):
    peers, length = (lax.axis_size(axis), shard.shape[dim])
    up = [(i, i + 1) for i in range(peers - 1)]
    down = [(j, i) for i, j in up]
    last = lax.slice_in_dim(shard, length - width, length, axis=dim)
    initial = lax.slice_in_dim(shard, 0, width, axis=dim)
    return lax.ppermute(last, axis, up), lax.ppermute(initial, axis, down)


SCALED_EPS = WENO_EPS * 12.0 / 13.0
SLOPE_WEIGHT = 3.0 / 13.0


def weno_side(minus_two, minus_one, centre, plus_one, plus_two):
    curve_zero = (minus_two + centre) - (minus_one + minus_one)
    curve_one = (minus_one + plus_one) - (centre + centre)
    curve_two = (centre + plus_two) - (plus_one + plus_one)
    slope_zero = curve_zero + 2.0 * (centre - minus_one)
    slope_one = minus_one - plus_one
    slope_two = curve_two + 2.0 * (centre - plus_one)
    guard_zero = (SCALED_EPS + curve_zero * curve_zero) + SLOPE_WEIGHT * (slope_zero * slope_zero)
    guard_one = (SCALED_EPS + curve_one * curve_one) + SLOPE_WEIGHT * (slope_one * slope_one)
    guard_two = (SCALED_EPS + curve_two * curve_two) + SLOPE_WEIGHT * (slope_two * slope_two)
    guard_zero = guard_zero * guard_zero
    guard_one = guard_one * guard_one
    guard_two = guard_two * guard_two
    cross_zero = guard_one * guard_two
    cross_one = 6.0 * (guard_zero * guard_two)
    cross_two = 3.0 * (guard_zero * guard_one)
    blended = cross_zero * (curve_zero + 3.0 * slope_zero)
    blended = blended + cross_one * (curve_one - 3.0 * slope_one)
    blended = blended + cross_two * (curve_two - 3.0 * slope_two)
    return centre + blended / (12.0 * (cross_zero + cross_one + cross_two))


HALO = 8
CHUNK = 8


def upwind_divergence(ext_ref, vel_ref, flux_ref, rows):
    faces = flux_ref.shape[0]
    for low in range(0, faces, CHUNK):

        def cut(offset):
            return ext_ref[pl.ds(HALO - 3 + offset + low, CHUNK), :]

        face_speed = 0.5 * (
            vel_ref[pl.ds(HALO - 1 + low, CHUNK), :] + vel_ref[pl.ds(HALO + low, CHUNK), :]
        )
        forward = face_speed >= 0.0
        stencil = [
            jnp.where(forward, cut(lower), cut(upper))
            for lower, upper in ((0, 5), (1, 4), (2, 3), (3, 2), (4, 1))
        ]
        flux_ref[pl.ds(low, CHUNK), :] = face_speed * weno_side(*stencil)
    return flux_ref[pl.ds(1, rows), :] - flux_ref[pl.ds(0, rows), :]


def axial_kernel(field_ref, speed_ref, top_ref, top_speed_ref, bottom_ref, bottom_speed_ref,
                 out_ref, ext_ref, vel_ref, flux_ref):
    rows, cols = field_ref.shape[1], field_ref.shape[2]
    fill_scratch(ext_ref, top_ref[0], field_ref[0], bottom_ref[0])
    fill_scratch(vel_ref, top_speed_ref[0], speed_ref[0], bottom_speed_ref[0])
    out_ref[0] = upwind_divergence(ext_ref, vel_ref, flux_ref, rows)


def radial_kernel(field_ref, along_axial_ref, speed_ref, left_ref, left_speed_ref, right_ref,
                  right_speed_ref, out_ref, ext_ref, vel_ref, flux_ref):
    rows, cols = field_ref.shape[1], field_ref.shape[2]
    field = field_ref[0]
    fill_scratch(ext_ref, left_ref[0], field.T, right_ref[0])
    fill_scratch(vel_ref, left_speed_ref[0], speed_ref[0].T, right_speed_ref[0])
    along_radial = upwind_divergence(ext_ref, vel_ref, flux_ref, cols).T
    moved = field - TIME_STEP * (along_axial_ref[0] + along_radial)
    out_ref[:, pl.ds(pl.program_id(0), 1), :] = moved[:, None, :]


def fill_scratch(scratch, before, body, after):
    span, cols = scratch.shape
    width, rows = (before.shape[0], body.shape[0])
    scratch[pl.ds(0, HALO), :] = jnp.zeros((HALO, cols), jnp.float32)
    scratch[pl.ds(HALO + rows, span - HALO - rows), :] = jnp.zeros(
        (span - HALO - rows, cols), jnp.float32
    )
    scratch[pl.ds(HALO - width, width), :] = before
    scratch[pl.ds(HALO, rows), :] = body
    scratch[pl.ds(HALO + rows, width), :] = after


def edge_columns(field, start, width):
    cols = field.shape[2]
    pick = lax.broadcasted_iota(jnp.int32, (width, cols), 1) == (
        lax.broadcasted_iota(jnp.int32, (width, cols), 0) + start
    )
    return jnp.einsum("kr,sar->ska", pick.astype(field.dtype), field, precision=HIGHEST)


def transport(species, speed, width=3):
    species_count, rows, cols = species.shape
    assert rows == cols and rows % CHUNK == 0
    axial_edges = jnp.concatenate([species, speed[0:1]], axis=0)
    top, bottom = edge_layers(axial_edges, "axial", 1, width)
    radial_edges = jnp.concatenate([species, speed[1:2]], axis=0)
    peers = lax.axis_size("radial")
    up = [(i, i + 1) for i in range(peers - 1)]
    down = [(j, i) for i, j in up]
    left = lax.ppermute(edge_columns(radial_edges, cols - width, width), "radial", up)
    right = lax.ppermute(edge_columns(radial_edges, 0, width), "radial", down)
    faces = rows + CHUNK
    span = HALO + faces + HALO
    plane = pl.BlockSpec((1, rows, cols), lambda s: (s, 0, 0))
    edge = pl.BlockSpec((1, width, cols), lambda s: (s, 0, 0))
    edge_speed = pl.BlockSpec((1, width, cols), lambda s: (species_count, 0, 0))
    scratch = [
        pltpu.VMEM((span, cols), jnp.float32),
        pltpu.VMEM((span, cols), jnp.float32),
        pltpu.VMEM((faces, cols), jnp.float32),
    ]
    along_axial = pl.pallas_call(
        axial_kernel,
        grid=(species_count,),
        in_specs=[plane, pl.BlockSpec((1, rows, cols), lambda s: (0, 0, 0))] + [edge, edge_speed] * 2,
        out_specs=plane,
        out_shape=jax.ShapeDtypeStruct(species.shape, jnp.float32),
        scratch_shapes=scratch,
    )(species, speed, top, top, bottom, bottom)
    moved_rows = pl.pallas_call(
        radial_kernel,
        grid=(species_count,),
        in_specs=[plane, plane, pl.BlockSpec((1, rows, cols), lambda s: (1, 0, 0))]
        + [edge, edge_speed] * 2,
        out_specs=pl.BlockSpec((rows, species_count, cols), lambda s: (0, 0, 0)),
        out_shape=jax.ShapeDtypeStruct((rows, species_count, cols), jnp.float32),
        scratch_shapes=scratch,
    )(species, along_axial, speed, left, left, right, right)
    return jnp.transpose(moved_rows, (1, 0, 2))


def kinetics_advance(
    starting_composition_field,
    thermal_field,
    linearized_kinetics_operator,
    frozen_jacobian_inverse_addend,
):
    acceleration_factor = jnp.exp(-ARRHENIUS_BARRIER / thermal_field)
    current = starting_composition_field
    for newton_step in range(ITERS):
        source = jnp.tensordot(
            linearized_kinetics_operator, current, axes=(1, 0), precision=CHEMISTRY_PRECISION
        ) - jnp.tanh(current)
        defect = current - starting_composition_field - CHEM_STEP * acceleration_factor * source
        current = (
            current
            - defect
            - jnp.tensordot(frozen_jacobian_inverse_addend, defect, axes=(1, 0), precision=CHEMISTRY_PRECISION)
        )
    return current


def absorbance_profile(field, molar_absorptivity_table, spokewise_sightline_length):
    mixed = jnp.tensordot(molar_absorptivity_table, field, axes=(1, 0), precision=HIGHEST)
    return jnp.dot(mixed, spokewise_sightline_length, precision=HIGHEST)


def butterfly_sum(part, axis):
    peers, stride = (lax.axis_size(axis), 1)
    if peers & (peers - 1):
        return lax.psum(part, axis)
    while stride < peers:
        pairs = [(j, j ^ stride) for j in range(peers)]
        part = part + lax.ppermute(part, axis, pairs)
        stride *= 2
    return part


def doubling_gather(part, axis):
    peers, stride = (lax.axis_size(axis), 1)
    if peers & (peers - 1):
        return lax.all_gather(part, axis, axis=1, tiled=True)
    position = lax.axis_index(axis)
    blocks = part[None]
    while stride < peers:
        pairs = [(j, j ^ stride) for j in range(peers)]
        other = lax.ppermute(blocks, axis, pairs)
        upper = (position // stride) % 2 == 1
        blocks = jnp.where(
            upper, jnp.concatenate([other, blocks], 0), jnp.concatenate([blocks, other], 0)
        )
        stride *= 2
    return jnp.transpose(blocks, (1, 0, 2)).reshape(part.shape[0], -1)


def gathered_profile(profile):
    return doubling_gather(butterfly_sum(profile, "radial"), "axial")


def local(
    composition_deviations,
    flow_speed_vector,
    thermal_field,
    linearized_kinetics_operator,
    frozen_jacobian_inverse_addend,
    rigid_block_indicator,
    molar_absorptivity_table,
    spokewise_sightline_length,
    sightline_lengthwise_index,
    observed_absorbance_traces,
):
    advected_composition_field = transport(composition_deviations, flow_speed_vector)
    combusted_composition_field = kinetics_advance(
        advected_composition_field,
        thermal_field,
        linearized_kinetics_operator,
        frozen_jacobian_inverse_addend,
    )
    flag_cells = jnp.repeat(
        jnp.repeat(rigid_block_indicator, TILE_ROWS, axis=0),
        advected_composition_field.shape[2],
        axis=1,
    )
    species_out = jnp.where(
        flag_cells[None] > 0, combusted_composition_field, advected_composition_field
    )
    path_scale = 1.0 / math.sqrt(advected_composition_field.shape[2] * lax.axis_size("radial"))
    profile = (
        absorbance_profile(species_out, molar_absorptivity_table, spokewise_sightline_length)
        * path_scale
    )
    whole_profile = gathered_profile(profile)
    device = lax.axis_index(("axial", "radial"))
    sample_count = observed_absorbance_traces.shape[1]
    own_rows = lax.dynamic_slice_in_dim(
        sightline_lengthwise_index, device * sample_count, sample_count, 1
    )
    cells = lax.broadcasted_iota(jnp.int32, (1, whole_profile.shape[1], 1), 1)
    values = jnp.sum(
        jnp.where(own_rows[:, None, :] == cells, whole_profile[:, :, None], 0.0), axis=1
    )
    return (species_out, values - observed_absorbance_traces)


def solution(mesh):
    in_specs = (
        P(None, "axial", "radial"),
        P(None, "axial", "radial"),
        P("axial", "radial"),
        P(),
        P(),
        P("axial", "radial"),
        P(),
        P("radial"),
        P(),
        P(None, ("axial", "radial")),
    )
    out_specs = (P(None, "axial", "radial"), P(None, ("axial", "radial")))
    return jax.shard_map(local, mesh=mesh, in_specs=in_specs, out_specs=out_specs, check_vma=False)
```

```python
import math

import jax
import jax.numpy as jnp
from jax import lax
from jax.sharding import PartitionSpec as P
from jax.experimental import pallas as pl
from jax.experimental.pallas import tpu as pltpu

TILE_ROWS = 2
ITERS = 3


TIME_STEP = 0.4
CHEM_STEP = 0.5
ARRHENIUS_BARRIER = 1.0
WENO_EPS = 1e-06
HIGHEST = lax.Precision.HIGHEST
CHEMISTRY_PRECISION = lax.Precision.HIGH


def edge_layers(shard, axis, dim, width):
    peers, length = (lax.axis_size(axis), shard.shape[dim])
    up = [(i, i + 1) for i in range(peers - 1)]
    down = [(j, i) for i, j in up]
    last = lax.slice_in_dim(shard, length - width, length, axis=dim)
    initial = lax.slice_in_dim(shard, 0, width, axis=dim)
    return lax.ppermute(last, axis, up), lax.ppermute(initial, axis, down)


SCALED_EPS = WENO_EPS * 12.0 / 13.0
SLOPE_WEIGHT = 3.0 / 13.0


def weno_side(minus_two, minus_one, centre, plus_one, plus_two):
    curve_zero = (minus_two + centre) - (minus_one + minus_one)
    curve_one = (minus_one + plus_one) - (centre + centre)
    curve_two = (centre + plus_two) - (plus_one + plus_one)
    slope_zero = curve_zero + 2.0 * (centre - minus_one)
    slope_one = minus_one - plus_one
    slope_two = curve_two + 2.0 * (centre - plus_one)
    guard_zero = (SCALED_EPS + curve_zero * curve_zero) + SLOPE_WEIGHT * (slope_zero * slope_zero)
    guard_one = (SCALED_EPS + curve_one * curve_one) + SLOPE_WEIGHT * (slope_one * slope_one)
    guard_two = (SCALED_EPS + curve_two * curve_two) + SLOPE_WEIGHT * (slope_two * slope_two)
    guard_zero = guard_zero * guard_zero
    guard_one = guard_one * guard_one
    guard_two = guard_two * guard_two
    cross_zero = guard_one * guard_two
    cross_one = 6.0 * (guard_zero * guard_two)
    cross_two = 3.0 * (guard_zero * guard_one)
    blended = cross_zero * (curve_zero + 3.0 * slope_zero)
    blended = blended + cross_one * (curve_one - 3.0 * slope_one)
    blended = blended + cross_two * (curve_two - 3.0 * slope_two)
    return centre + blended / (12.0 * (cross_zero + cross_one + cross_two))


HALO = 8
SPECIES_GROUP = 19
CHUNK = 8


def upwind_divergence(ext_ref, vel_ref, flux_ref, rows):
    faces = flux_ref.shape[0]
    for low in range(0, faces, CHUNK):

        def cut(offset):
            return ext_ref[pl.ds(HALO - 3 + offset + low, CHUNK), :]

        face_speed = 0.5 * (
            vel_ref[pl.ds(HALO - 1 + low, CHUNK), :] + vel_ref[pl.ds(HALO + low, CHUNK), :]
        )
        forward = face_speed >= 0.0
        stencil = [
            jnp.where(forward, cut(lower), cut(upper))
            for lower, upper in ((0, 5), (1, 4), (2, 3), (3, 2), (4, 1))
        ]
        flux_ref[pl.ds(low, CHUNK), :] = face_speed * weno_side(*stencil)
    return flux_ref[pl.ds(1, rows), :] - flux_ref[pl.ds(0, rows), :]


def transport_kernel(
    field_ref, speed_ref, top_ref, top_speed_ref, bottom_ref, bottom_speed_ref,
    left_ref, left_speed_ref, right_ref, right_speed_ref, out_ref,
    ext_ref, vel_ref, flux_ref,
):
    rows, cols = field_ref.shape[1], field_ref.shape[2]
    group = field_ref.shape[0]

    def one_species(member, carry):
        field = field_ref[member]
        fill_scratch(ext_ref, top_ref[member], field, bottom_ref[member])
        fill_scratch(vel_ref, top_speed_ref[0], speed_ref[0], bottom_speed_ref[0])
        along_axial = upwind_divergence(ext_ref, vel_ref, flux_ref, rows)
        fill_scratch(ext_ref, left_ref[member], field.T, right_ref[member])
        fill_scratch(vel_ref, left_speed_ref[0], speed_ref[1].T, right_speed_ref[0])
        along_radial = upwind_divergence(ext_ref, vel_ref, flux_ref, cols).T
        moved = field - TIME_STEP * (along_axial + along_radial)
        out_ref[:, pl.ds(pl.program_id(0) * group + member, 1), :] = moved[:, None, :]
        return carry

    lax.fori_loop(0, group, one_species, 0)


def fill_scratch(scratch, before, body, after):
    span, cols = scratch.shape
    width, rows = (before.shape[0], body.shape[0])
    scratch[pl.ds(0, HALO), :] = jnp.zeros((HALO, cols), jnp.float32)
    scratch[pl.ds(HALO + rows, span - HALO - rows), :] = jnp.zeros(
        (span - HALO - rows, cols), jnp.float32
    )
    scratch[pl.ds(HALO - width, width), :] = before
    scratch[pl.ds(HALO, rows), :] = body
    scratch[pl.ds(HALO + rows, width), :] = after


def edge_columns(field, start, width):
    cols = field.shape[2]
    pick = lax.broadcasted_iota(jnp.int32, (width, cols), 1) == (
        lax.broadcasted_iota(jnp.int32, (width, cols), 0) + start
    )
    return jnp.einsum("kr,sar->ska", pick.astype(field.dtype), field, precision=HIGHEST)


def transport(species, speed, width=3):
    species_count, rows, cols = species.shape
    assert rows == cols and rows % CHUNK == 0
    axial_edges = jnp.concatenate([species, speed[0:1]], axis=0)
    top, bottom = edge_layers(axial_edges, "axial", 1, width)
    radial_edges = jnp.concatenate([species, speed[1:2]], axis=0)
    peers = lax.axis_size("radial")
    up = [(i, i + 1) for i in range(peers - 1)]
    down = [(j, i) for i, j in up]
    left = lax.ppermute(edge_columns(radial_edges, cols - width, width), "radial", up)
    right = lax.ppermute(edge_columns(radial_edges, 0, width), "radial", down)
    faces = rows + CHUNK
    span = HALO + faces + HALO
    group = max(g for g in range(1, SPECIES_GROUP + 1) if species_count % g == 0)
    plane = pl.BlockSpec((group, rows, cols), lambda s: (s, 0, 0))
    speeds = pl.BlockSpec((2, rows, cols), lambda s: (0, 0, 0))
    edge = pl.BlockSpec((group, width, cols), lambda s: (s, 0, 0))
    edge_speed = pl.BlockSpec((1, width, cols), lambda s: (species_count, 0, 0))
    moved_rows = pl.pallas_call(
        transport_kernel,
        grid=(species_count // group,),
        in_specs=[plane, speeds] + [edge, edge_speed] * 4,
        out_specs=pl.BlockSpec((rows, species_count, cols), lambda s: (0, 0, 0)),
        out_shape=jax.ShapeDtypeStruct((rows, species_count, cols), jnp.float32),
        scratch_shapes=[
            pltpu.VMEM((span, cols), jnp.float32),
            pltpu.VMEM((span, cols), jnp.float32),
            pltpu.VMEM((faces, cols), jnp.float32),
        ],
    )(species, speed, top, top, bottom, bottom, left, left, right, right)
    return jnp.transpose(moved_rows, (1, 0, 2))


def kinetics_advance(
    starting_composition_field,
    thermal_field,
    linearized_kinetics_operator,
    frozen_jacobian_inverse_addend,
):
    acceleration_factor = jnp.exp(-ARRHENIUS_BARRIER / thermal_field)
    current = starting_composition_field
    for newton_step in range(ITERS):
        source = jnp.tensordot(
            linearized_kinetics_operator, current, axes=(1, 0), precision=CHEMISTRY_PRECISION
        ) - jnp.tanh(current)
        defect = current - starting_composition_field - CHEM_STEP * acceleration_factor * source
        current = (
            current
            - defect
            - jnp.tensordot(frozen_jacobian_inverse_addend, defect, axes=(1, 0), precision=CHEMISTRY_PRECISION)
        )
    return current


def absorbance_profile(field, molar_absorptivity_table, spokewise_sightline_length):
    mixed = jnp.tensordot(molar_absorptivity_table, field, axes=(1, 0), precision=HIGHEST)
    return jnp.dot(mixed, spokewise_sightline_length, precision=HIGHEST)


def butterfly_sum(part, axis):
    peers, stride = (lax.axis_size(axis), 1)
    if peers & (peers - 1):
        return lax.psum(part, axis)
    while stride < peers:
        pairs = [(j, j ^ stride) for j in range(peers)]
        part = part + lax.ppermute(part, axis, pairs)
        stride *= 2
    return part


def doubling_gather(part, axis):
    peers, stride = (lax.axis_size(axis), 1)
    if peers & (peers - 1):
        return lax.all_gather(part, axis, axis=1, tiled=True)
    position = lax.axis_index(axis)
    blocks = part[None]
    while stride < peers:
        pairs = [(j, j ^ stride) for j in range(peers)]
        other = lax.ppermute(blocks, axis, pairs)
        upper = (position // stride) % 2 == 1
        blocks = jnp.where(
            upper, jnp.concatenate([other, blocks], 0), jnp.concatenate([blocks, other], 0)
        )
        stride *= 2
    return jnp.transpose(blocks, (1, 0, 2)).reshape(part.shape[0], -1)


def gathered_profile(profile):
    return doubling_gather(butterfly_sum(profile, "radial"), "axial")


def local(
    composition_deviations,
    flow_speed_vector,
    thermal_field,
    linearized_kinetics_operator,
    frozen_jacobian_inverse_addend,
    rigid_block_indicator,
    molar_absorptivity_table,
    spokewise_sightline_length,
    sightline_lengthwise_index,
    observed_absorbance_traces,
):
    advected_composition_field = transport(composition_deviations, flow_speed_vector)
    combusted_composition_field = kinetics_advance(
        advected_composition_field,
        thermal_field,
        linearized_kinetics_operator,
        frozen_jacobian_inverse_addend,
    )
    flag_cells = jnp.repeat(
        jnp.repeat(rigid_block_indicator, TILE_ROWS, axis=0),
        advected_composition_field.shape[2],
        axis=1,
    )
    species_out = jnp.where(
        flag_cells[None] > 0, combusted_composition_field, advected_composition_field
    )
    path_scale = 1.0 / math.sqrt(advected_composition_field.shape[2] * lax.axis_size("radial"))
    profile = (
        absorbance_profile(species_out, molar_absorptivity_table, spokewise_sightline_length)
        * path_scale
    )
    whole_profile = gathered_profile(profile)
    device = lax.axis_index(("axial", "radial"))
    sample_count = observed_absorbance_traces.shape[1]
    own_rows = lax.dynamic_slice_in_dim(
        sightline_lengthwise_index, device * sample_count, sample_count, 1
    )
    cells = lax.broadcasted_iota(jnp.int32, (1, whole_profile.shape[1], 1), 1)
    values = jnp.sum(
        jnp.where(own_rows[:, None, :] == cells, whole_profile[:, :, None], 0.0), axis=1
    )
    return (species_out, values - observed_absorbance_traces)


def solution(mesh):
    in_specs = (
        P(None, "axial", "radial"),
        P(None, "axial", "radial"),
        P("axial", "radial"),
        P(),
        P(),
        P("axial", "radial"),
        P(),
        P("radial"),
        P(),
        P(None, ("axial", "radial")),
    )
    out_specs = (P(None, "axial", "radial"), P(None, ("axial", "radial")))
    return jax.shard_map(local, mesh=mesh, in_specs=in_specs, out_specs=out_specs, check_vma=False)
```

```python
import math

import jax
import jax.numpy as jnp
from jax import lax
from jax.sharding import PartitionSpec as P
from jax.experimental import pallas as pl
from jax.experimental.pallas import tpu as pltpu

TILE_ROWS = 2
ITERS = 3


TIME_STEP = 0.4
CHEM_STEP = 0.5
ARRHENIUS_BARRIER = 1.0
WENO_EPS = 1e-06
HIGHEST = lax.Precision.HIGHEST
CHEMISTRY_PRECISION = lax.Precision.HIGH


def edge_layers(shard, axis, dim, width):
    peers, length = (lax.axis_size(axis), shard.shape[dim])
    up = [(i, i + 1) for i in range(peers - 1)]
    down = [(j, i) for i, j in up]
    last = lax.slice_in_dim(shard, length - width, length, axis=dim)
    initial = lax.slice_in_dim(shard, 0, width, axis=dim)
    return lax.ppermute(last, axis, up), lax.ppermute(initial, axis, down)


SCALED_EPS = WENO_EPS * 12.0 / 13.0
SLOPE_WEIGHT = 3.0 / 13.0


def weno_side(minus_two, minus_one, centre, plus_one, plus_two):
    curve_zero = (minus_two + centre) - (minus_one + minus_one)
    curve_one = (minus_one + plus_one) - (centre + centre)
    curve_two = (centre + plus_two) - (plus_one + plus_one)
    slope_zero = curve_zero + 2.0 * (centre - minus_one)
    slope_one = minus_one - plus_one
    slope_two = curve_two + 2.0 * (centre - plus_one)
    guard_zero = (SCALED_EPS + curve_zero * curve_zero) + SLOPE_WEIGHT * (slope_zero * slope_zero)
    guard_one = (SCALED_EPS + curve_one * curve_one) + SLOPE_WEIGHT * (slope_one * slope_one)
    guard_two = (SCALED_EPS + curve_two * curve_two) + SLOPE_WEIGHT * (slope_two * slope_two)
    guard_zero = guard_zero * guard_zero
    guard_one = guard_one * guard_one
    guard_two = guard_two * guard_two
    cross_zero = guard_one * guard_two
    cross_one = 6.0 * (guard_zero * guard_two)
    cross_two = 3.0 * (guard_zero * guard_one)
    blended = cross_zero * (curve_zero + 3.0 * slope_zero)
    blended = blended + cross_one * (curve_one - 3.0 * slope_one)
    blended = blended + cross_two * (curve_two - 3.0 * slope_two)
    return centre + blended / (12.0 * (cross_zero + cross_one + cross_two))


HALO = 8
SPECIES_GROUP = 19
CHUNK = 8


def upwind_divergence(ext_ref, vel_ref, flux_ref, rows):
    faces = flux_ref.shape[0]
    for low in range(0, faces, CHUNK):

        def cut(offset):
            return ext_ref[pl.ds(HALO - 3 + offset + low, CHUNK), :]

        face_speed = 0.5 * (
            vel_ref[pl.ds(HALO - 1 + low, CHUNK), :] + vel_ref[pl.ds(HALO + low, CHUNK), :]
        )
        forward = face_speed >= 0.0
        stencil = [
            jnp.where(forward, cut(lower), cut(upper))
            for lower, upper in ((0, 5), (1, 4), (2, 3), (3, 2), (4, 1))
        ]
        flux_ref[pl.ds(low, CHUNK), :] = face_speed * weno_side(*stencil)
    return flux_ref[pl.ds(1, rows), :] - flux_ref[pl.ds(0, rows), :]


def axial_kernel(field_ref, speed_ref, top_ref, top_speed_ref, bottom_ref, bottom_speed_ref,
                 out_ref, ext_ref, vel_ref, flux_ref):
    rows = field_ref.shape[1]
    fill_scratch(vel_ref, top_speed_ref[0], speed_ref[0], bottom_speed_ref[0])

    def one_species(member, carry):
        fill_scratch(ext_ref, top_ref[member], field_ref[member], bottom_ref[member])
        out_ref[member] = upwind_divergence(ext_ref, vel_ref, flux_ref, rows)
        return carry

    lax.fori_loop(0, field_ref.shape[0], one_species, 0)


def radial_kernel(field_ref, along_axial_ref, speed_ref, left_ref, left_speed_ref, right_ref,
                  right_speed_ref, out_ref, ext_ref, vel_ref, flux_ref):
    cols = field_ref.shape[2]
    group = field_ref.shape[0]
    fill_scratch(vel_ref, left_speed_ref[0], speed_ref[0].T, right_speed_ref[0])

    def one_species(member, carry):
        field = field_ref[member]
        fill_scratch(ext_ref, left_ref[member], field.T, right_ref[member])
        along_radial = upwind_divergence(ext_ref, vel_ref, flux_ref, cols).T
        moved = field - TIME_STEP * (along_axial_ref[member] + along_radial)
        out_ref[:, pl.ds(pl.program_id(0) * group + member, 1), :] = moved[:, None, :]
        return carry

    lax.fori_loop(0, group, one_species, 0)


def fill_scratch(scratch, before, body, after):
    span, cols = scratch.shape
    width, rows = (before.shape[0], body.shape[0])
    scratch[pl.ds(0, HALO), :] = jnp.zeros((HALO, cols), jnp.float32)
    scratch[pl.ds(HALO + rows, span - HALO - rows), :] = jnp.zeros(
        (span - HALO - rows, cols), jnp.float32
    )
    scratch[pl.ds(HALO - width, width), :] = before
    scratch[pl.ds(HALO, rows), :] = body
    scratch[pl.ds(HALO + rows, width), :] = after


def edge_columns(field, start, width):
    cols = field.shape[2]
    pick = lax.broadcasted_iota(jnp.int32, (width, cols), 1) == (
        lax.broadcasted_iota(jnp.int32, (width, cols), 0) + start
    )
    return jnp.einsum("kr,sar->ska", pick.astype(field.dtype), field, precision=HIGHEST)


def transport(species, speed, width=3):
    species_count, rows, cols = species.shape
    assert rows == cols and rows % CHUNK == 0
    axial_edges = jnp.concatenate([species, speed[0:1]], axis=0)
    top, bottom = edge_layers(axial_edges, "axial", 1, width)
    radial_edges = jnp.concatenate([species, speed[1:2]], axis=0)
    peers = lax.axis_size("radial")
    up = [(i, i + 1) for i in range(peers - 1)]
    down = [(j, i) for i, j in up]
    left = lax.ppermute(edge_columns(radial_edges, cols - width, width), "radial", up)
    right = lax.ppermute(edge_columns(radial_edges, 0, width), "radial", down)
    faces = rows + CHUNK
    span = HALO + faces + HALO
    group = max(g for g in range(1, SPECIES_GROUP + 1) if species_count % g == 0)
    plane = pl.BlockSpec((group, rows, cols), lambda s: (s, 0, 0))
    edge = pl.BlockSpec((group, width, cols), lambda s: (s, 0, 0))
    edge_speed = pl.BlockSpec((1, width, cols), lambda s: (species_count, 0, 0))
    scratch = [
        pltpu.VMEM((span, cols), jnp.float32),
        pltpu.VMEM((span, cols), jnp.float32),
        pltpu.VMEM((faces, cols), jnp.float32),
    ]
    along_axial = pl.pallas_call(
        axial_kernel,
        grid=(species_count // group,),
        in_specs=[plane, pl.BlockSpec((1, rows, cols), lambda s: (0, 0, 0))] + [edge, edge_speed] * 2,
        out_specs=plane,
        out_shape=jax.ShapeDtypeStruct(species.shape, jnp.float32),
        scratch_shapes=scratch,
    )(species, speed, top, top, bottom, bottom)
    moved_rows = pl.pallas_call(
        radial_kernel,
        grid=(species_count // group,),
        in_specs=[plane, plane, pl.BlockSpec((1, rows, cols), lambda s: (1, 0, 0))]
        + [edge, edge_speed] * 2,
        out_specs=pl.BlockSpec((rows, species_count, cols), lambda s: (0, 0, 0)),
        out_shape=jax.ShapeDtypeStruct((rows, species_count, cols), jnp.float32),
        scratch_shapes=scratch,
    )(species, along_axial, speed, left, left, right, right)
    return jnp.transpose(moved_rows, (1, 0, 2))


def kinetics_advance(
    starting_composition_field,
    thermal_field,
    linearized_kinetics_operator,
    frozen_jacobian_inverse_addend,
):
    acceleration_factor = jnp.exp(-ARRHENIUS_BARRIER / thermal_field)
    current = starting_composition_field
    for newton_step in range(ITERS):
        source = jnp.tensordot(
            linearized_kinetics_operator, current, axes=(1, 0), precision=CHEMISTRY_PRECISION
        ) - jnp.tanh(current)
        defect = current - starting_composition_field - CHEM_STEP * acceleration_factor * source
        current = (
            current
            - defect
            - jnp.tensordot(frozen_jacobian_inverse_addend, defect, axes=(1, 0), precision=CHEMISTRY_PRECISION)
        )
    return current


def absorbance_profile(field, molar_absorptivity_table, spokewise_sightline_length):
    mixed = jnp.tensordot(molar_absorptivity_table, field, axes=(1, 0), precision=HIGHEST)
    return jnp.dot(mixed, spokewise_sightline_length, precision=HIGHEST)


def butterfly_sum(part, axis):
    peers, stride = (lax.axis_size(axis), 1)
    if peers & (peers - 1):
        return lax.psum(part, axis)
    while stride < peers:
        pairs = [(j, j ^ stride) for j in range(peers)]
        part = part + lax.ppermute(part, axis, pairs)
        stride *= 2
    return part


def doubling_gather(part, axis):
    peers, stride = (lax.axis_size(axis), 1)
    if peers & (peers - 1):
        return lax.all_gather(part, axis, axis=1, tiled=True)
    position = lax.axis_index(axis)
    blocks = part[None]
    while stride < peers:
        pairs = [(j, j ^ stride) for j in range(peers)]
        other = lax.ppermute(blocks, axis, pairs)
        upper = (position // stride) % 2 == 1
        blocks = jnp.where(
            upper, jnp.concatenate([other, blocks], 0), jnp.concatenate([blocks, other], 0)
        )
        stride *= 2
    return jnp.transpose(blocks, (1, 0, 2)).reshape(part.shape[0], -1)


def gathered_profile(profile):
    return doubling_gather(butterfly_sum(profile, "radial"), "axial")


def local(
    composition_deviations,
    flow_speed_vector,
    thermal_field,
    linearized_kinetics_operator,
    frozen_jacobian_inverse_addend,
    rigid_block_indicator,
    molar_absorptivity_table,
    spokewise_sightline_length,
    sightline_lengthwise_index,
    observed_absorbance_traces,
):
    advected_composition_field = transport(composition_deviations, flow_speed_vector)
    combusted_composition_field = kinetics_advance(
        advected_composition_field,
        thermal_field,
        linearized_kinetics_operator,
        frozen_jacobian_inverse_addend,
    )
    flag_cells = jnp.repeat(
        jnp.repeat(rigid_block_indicator, TILE_ROWS, axis=0),
        advected_composition_field.shape[2],
        axis=1,
    )
    species_out = jnp.where(
        flag_cells[None] > 0, combusted_composition_field, advected_composition_field
    )
    path_scale = 1.0 / math.sqrt(advected_composition_field.shape[2] * lax.axis_size("radial"))
    profile = (
        absorbance_profile(species_out, molar_absorptivity_table, spokewise_sightline_length)
        * path_scale
    )
    whole_profile = gathered_profile(profile)
    device = lax.axis_index(("axial", "radial"))
    sample_count = observed_absorbance_traces.shape[1]
    own_rows = lax.dynamic_slice_in_dim(
        sightline_lengthwise_index, device * sample_count, sample_count, 1
    )
    cells = lax.broadcasted_iota(jnp.int32, (1, whole_profile.shape[1], 1), 1)
    values = jnp.sum(
        jnp.where(own_rows[:, None, :] == cells, whole_profile[:, :, None], 0.0), axis=1
    )
    return (species_out, values - observed_absorbance_traces)


def solution(mesh):
    in_specs = (
        P(None, "axial", "radial"),
        P(None, "axial", "radial"),
        P("axial", "radial"),
        P(),
        P(),
        P("axial", "radial"),
        P(),
        P("radial"),
        P(),
        P(None, ("axial", "radial")),
    )
    out_specs = (P(None, "axial", "radial"), P(None, ("axial", "radial")))
    return jax.shard_map(local, mesh=mesh, in_specs=in_specs, out_specs=out_specs, check_vma=False)
```

```python
import math

import jax
import jax.numpy as jnp
from jax import lax
from jax.sharding import PartitionSpec as P
from jax.experimental import pallas as pl
from jax.experimental.pallas import tpu as pltpu

TILE_ROWS = 2
ITERS = 3


TIME_STEP = 0.4
CHEM_STEP = 0.5
ARRHENIUS_BARRIER = 1.0
WENO_EPS = 1e-06
HIGHEST = lax.Precision.HIGHEST
CHEMISTRY_PRECISION = lax.Precision.HIGH


def edge_layers(shard, axis, dim, width):
    peers, length = (lax.axis_size(axis), shard.shape[dim])
    up = [(i, i + 1) for i in range(peers - 1)]
    down = [(j, i) for i, j in up]
    last = lax.slice_in_dim(shard, length - width, length, axis=dim)
    initial = lax.slice_in_dim(shard, 0, width, axis=dim)
    return lax.ppermute(last, axis, up), lax.ppermute(initial, axis, down)


SCALED_EPS = WENO_EPS * 12.0 / 13.0
SLOPE_WEIGHT = 3.0 / 13.0


def weno_side(minus_two, minus_one, centre, plus_one, plus_two):
    curve_zero = (minus_two + centre) - (minus_one + minus_one)
    curve_one = (minus_one + plus_one) - (centre + centre)
    curve_two = (centre + plus_two) - (plus_one + plus_one)
    slope_zero = curve_zero + 2.0 * (centre - minus_one)
    slope_one = minus_one - plus_one
    slope_two = curve_two + 2.0 * (centre - plus_one)
    guard_zero = (SCALED_EPS + curve_zero * curve_zero) + SLOPE_WEIGHT * (slope_zero * slope_zero)
    guard_one = (SCALED_EPS + curve_one * curve_one) + SLOPE_WEIGHT * (slope_one * slope_one)
    guard_two = (SCALED_EPS + curve_two * curve_two) + SLOPE_WEIGHT * (slope_two * slope_two)
    guard_zero = guard_zero * guard_zero
    guard_one = guard_one * guard_one
    guard_two = guard_two * guard_two
    cross_zero = guard_one * guard_two
    cross_one = 6.0 * (guard_zero * guard_two)
    cross_two = 3.0 * (guard_zero * guard_one)
    blended = cross_zero * (curve_zero + 3.0 * slope_zero)
    blended = blended + cross_one * (curve_one - 3.0 * slope_one)
    blended = blended + cross_two * (curve_two - 3.0 * slope_two)
    return centre + blended / (12.0 * (cross_zero + cross_one + cross_two))


HALO = 8
SPECIES_GROUP = 19
CHUNK = 8


def upwind_divergence(ext_ref, vel_ref, flux_ref, rows):
    faces = flux_ref.shape[0]
    for low in range(0, faces, CHUNK):

        def cut(offset):
            return ext_ref[pl.ds(HALO - 3 + offset + low, CHUNK), :]

        face_speed = 0.5 * (
            vel_ref[pl.ds(HALO - 1 + low, CHUNK), :] + vel_ref[pl.ds(HALO + low, CHUNK), :]
        )
        forward = face_speed >= 0.0
        stencil = [
            jnp.where(forward, cut(lower), cut(upper))
            for lower, upper in ((0, 5), (1, 4), (2, 3), (3, 2), (4, 1))
        ]
        flux_ref[pl.ds(low, CHUNK), :] = face_speed * weno_side(*stencil)
    return flux_ref[pl.ds(1, rows), :] - flux_ref[pl.ds(0, rows), :]


def transport_kernel(
    field_ref, speed_ref, top_ref, top_speed_ref, bottom_ref, bottom_speed_ref,
    left_ref, left_speed_ref, right_ref, right_speed_ref, out_ref,
    ext_ref, vel_ref, flux_ref,
):
    rows, cols = field_ref.shape[1], field_ref.shape[2]
    group = field_ref.shape[0]

    def one_species(member, carry):
        field = field_ref[member]
        fill_scratch(ext_ref, top_ref[member], field, bottom_ref[member])
        fill_scratch(vel_ref, top_speed_ref[0], speed_ref[0], bottom_speed_ref[0])
        along_axial = upwind_divergence(ext_ref, vel_ref, flux_ref, rows)
        fill_scratch(ext_ref, left_ref[member], field.T, right_ref[member])
        fill_scratch(vel_ref, left_speed_ref[0], speed_ref[1].T, right_speed_ref[0])
        along_radial = upwind_divergence(ext_ref, vel_ref, flux_ref, cols).T
        moved = field - TIME_STEP * (along_axial + along_radial)
        out_ref[:, pl.ds(pl.program_id(0) * group + member, 1), :] = moved[:, None, :]
        return carry

    lax.fori_loop(0, group, one_species, 0)


def fill_scratch(scratch, before, body, after):
    span, cols = scratch.shape
    width, rows = (before.shape[0], body.shape[0])
    scratch[pl.ds(0, HALO), :] = jnp.zeros((HALO, cols), jnp.float32)
    scratch[pl.ds(HALO + rows, span - HALO - rows), :] = jnp.zeros(
        (span - HALO - rows, cols), jnp.float32
    )
    scratch[pl.ds(HALO - width, width), :] = before
    scratch[pl.ds(HALO, rows), :] = body
    scratch[pl.ds(HALO + rows, width), :] = after


def edge_columns(field, width):
    cols = field.shape[2]
    row = lax.broadcasted_iota(jnp.int32, (2 * width, cols), 0)
    column = lax.broadcasted_iota(jnp.int32, (2 * width, cols), 1)
    pick = column == jnp.where(row < width, row + cols - width, row - width)
    picked = jnp.einsum("kr,sar->ska", pick.astype(field.dtype), field, precision=HIGHEST)
    return picked[:, :width], picked[:, width:]


def transport(species, speed, width=3):
    species_count, rows, cols = species.shape
    assert rows == cols and rows % CHUNK == 0
    axial_edges = jnp.concatenate([species, speed[0:1]], axis=0)
    top, bottom = edge_layers(axial_edges, "axial", 1, width)
    radial_edges = jnp.concatenate([species, speed[1:2]], axis=0)
    peers = lax.axis_size("radial")
    up = [(i, i + 1) for i in range(peers - 1)]
    down = [(j, i) for i, j in up]
    high_columns, low_columns = edge_columns(radial_edges, width)
    left = lax.ppermute(high_columns, "radial", up)
    right = lax.ppermute(low_columns, "radial", down)
    faces = rows + CHUNK
    span = HALO + faces + HALO
    group = max(g for g in range(1, SPECIES_GROUP + 1) if species_count % g == 0)
    plane = pl.BlockSpec((group, rows, cols), lambda s: (s, 0, 0))
    speeds = pl.BlockSpec((2, rows, cols), lambda s: (0, 0, 0))
    edge = pl.BlockSpec((group, width, cols), lambda s: (s, 0, 0))
    edge_speed = pl.BlockSpec((1, width, cols), lambda s: (species_count, 0, 0))
    moved_rows = pl.pallas_call(
        transport_kernel,
        grid=(species_count // group,),
        in_specs=[plane, speeds] + [edge, edge_speed] * 4,
        out_specs=pl.BlockSpec((rows, species_count, cols), lambda s: (0, 0, 0)),
        out_shape=jax.ShapeDtypeStruct((rows, species_count, cols), jnp.float32),
        scratch_shapes=[
            pltpu.VMEM((span, cols), jnp.float32),
            pltpu.VMEM((span, cols), jnp.float32),
            pltpu.VMEM((faces, cols), jnp.float32),
        ],
    )(species, speed, top, top, bottom, bottom, left, left, right, right)
    return jnp.transpose(moved_rows, (1, 0, 2))


def kinetics_advance(
    starting_composition_field,
    thermal_field,
    linearized_kinetics_operator,
    frozen_jacobian_inverse_addend,
):
    acceleration_factor = jnp.exp(-ARRHENIUS_BARRIER / thermal_field)
    current = starting_composition_field
    for newton_step in range(ITERS):
        source = jnp.tensordot(
            linearized_kinetics_operator, current, axes=(1, 0), precision=CHEMISTRY_PRECISION
        ) - jnp.tanh(current)
        defect = current - starting_composition_field - CHEM_STEP * acceleration_factor * source
        current = (
            current
            - defect
            - jnp.tensordot(frozen_jacobian_inverse_addend, defect, axes=(1, 0), precision=CHEMISTRY_PRECISION)
        )
    return current


def absorbance_profile(field, molar_absorptivity_table, spokewise_sightline_length):
    mixed = jnp.tensordot(molar_absorptivity_table, field, axes=(1, 0), precision=HIGHEST)
    return jnp.dot(mixed, spokewise_sightline_length, precision=HIGHEST)


def butterfly_sum(part, axis):
    peers, stride = (lax.axis_size(axis), 1)
    if peers & (peers - 1):
        return lax.psum(part, axis)
    while stride < peers:
        pairs = [(j, j ^ stride) for j in range(peers)]
        part = part + lax.ppermute(part, axis, pairs)
        stride *= 2
    return part


def doubling_gather(part, axis):
    peers, stride = (lax.axis_size(axis), 1)
    if peers & (peers - 1):
        return lax.all_gather(part, axis, axis=1, tiled=True)
    position = lax.axis_index(axis)
    blocks = part[None]
    while stride < peers:
        pairs = [(j, j ^ stride) for j in range(peers)]
        other = lax.ppermute(blocks, axis, pairs)
        upper = (position // stride) % 2 == 1
        blocks = jnp.where(
            upper, jnp.concatenate([other, blocks], 0), jnp.concatenate([blocks, other], 0)
        )
        stride *= 2
    return jnp.transpose(blocks, (1, 0, 2)).reshape(part.shape[0], -1)


def gathered_profile(profile):
    return doubling_gather(butterfly_sum(profile, "radial"), "axial")


def local(
    composition_deviations,
    flow_speed_vector,
    thermal_field,
    linearized_kinetics_operator,
    frozen_jacobian_inverse_addend,
    rigid_block_indicator,
    molar_absorptivity_table,
    spokewise_sightline_length,
    sightline_lengthwise_index,
    observed_absorbance_traces,
):
    advected_composition_field = transport(composition_deviations, flow_speed_vector)
    combusted_composition_field = kinetics_advance(
        advected_composition_field,
        thermal_field,
        linearized_kinetics_operator,
        frozen_jacobian_inverse_addend,
    )
    flag_cells = jnp.repeat(
        jnp.repeat(rigid_block_indicator, TILE_ROWS, axis=0),
        advected_composition_field.shape[2],
        axis=1,
    )
    species_out = jnp.where(
        flag_cells[None] > 0, combusted_composition_field, advected_composition_field
    )
    path_scale = 1.0 / math.sqrt(advected_composition_field.shape[2] * lax.axis_size("radial"))
    profile = (
        absorbance_profile(species_out, molar_absorptivity_table, spokewise_sightline_length)
        * path_scale
    )
    whole_profile = gathered_profile(profile)
    device = lax.axis_index(("axial", "radial"))
    sample_count = observed_absorbance_traces.shape[1]
    own_rows = lax.dynamic_slice_in_dim(
        sightline_lengthwise_index, device * sample_count, sample_count, 1
    )
    cells = lax.broadcasted_iota(jnp.int32, (1, whole_profile.shape[1], 1), 1)
    values = jnp.sum(
        jnp.where(own_rows[:, None, :] == cells, whole_profile[:, :, None], 0.0), axis=1
    )
    return (species_out, values - observed_absorbance_traces)


def solution(mesh):
    in_specs = (
        P(None, "axial", "radial"),
        P(None, "axial", "radial"),
        P("axial", "radial"),
        P(),
        P(),
        P("axial", "radial"),
        P(),
        P("radial"),
        P(),
        P(None, ("axial", "radial")),
    )
    out_specs = (P(None, "axial", "radial"), P(None, ("axial", "radial")))
    return jax.shard_map(local, mesh=mesh, in_specs=in_specs, out_specs=out_specs, check_vma=False)
```

```python
import math

import jax
import jax.numpy as jnp
from jax import lax
from jax.sharding import PartitionSpec as P
from jax.experimental import pallas as pl
from jax.experimental.pallas import tpu as pltpu

TILE_ROWS = 2
ITERS = 3


TIME_STEP = 0.4
CHEM_STEP = 0.5
ARRHENIUS_BARRIER = 1.0
WENO_EPS = 1e-06
HIGHEST = lax.Precision.HIGHEST
CHEMISTRY_PRECISION = lax.Precision.HIGH


def edge_layers(shard, axis, dim, width):
    peers, length = (lax.axis_size(axis), shard.shape[dim])
    up = [(i, i + 1) for i in range(peers - 1)]
    down = [(j, i) for i, j in up]
    last = lax.slice_in_dim(shard, length - width, length, axis=dim)
    initial = lax.slice_in_dim(shard, 0, width, axis=dim)
    return lax.ppermute(last, axis, up), lax.ppermute(initial, axis, down)


SCALED_EPS = WENO_EPS * 12.0 / 13.0
SLOPE_WEIGHT = 3.0 / 13.0


def weno_side(minus_two, minus_one, centre, plus_one, plus_two):
    curve_zero = (minus_two + centre) - (minus_one + minus_one)
    curve_one = (minus_one + plus_one) - (centre + centre)
    curve_two = (centre + plus_two) - (plus_one + plus_one)
    slope_zero = curve_zero + 2.0 * (centre - minus_one)
    slope_one = minus_one - plus_one
    slope_two = curve_two + 2.0 * (centre - plus_one)
    guard_zero = (SCALED_EPS + curve_zero * curve_zero) + SLOPE_WEIGHT * (slope_zero * slope_zero)
    guard_one = (SCALED_EPS + curve_one * curve_one) + SLOPE_WEIGHT * (slope_one * slope_one)
    guard_two = (SCALED_EPS + curve_two * curve_two) + SLOPE_WEIGHT * (slope_two * slope_two)
    guard_zero = guard_zero * guard_zero
    guard_one = guard_one * guard_one
    guard_two = guard_two * guard_two
    cross_zero = guard_one * guard_two
    cross_one = 6.0 * (guard_zero * guard_two)
    cross_two = 3.0 * (guard_zero * guard_one)
    blended = cross_zero * (curve_zero + 3.0 * slope_zero)
    blended = blended + cross_one * (curve_one - 3.0 * slope_one)
    blended = blended + cross_two * (curve_two - 3.0 * slope_two)
    return centre + blended / (12.0 * (cross_zero + cross_one + cross_two))


HALO = 8
SPECIES_GROUP = 19
CHUNK = 8


def upwind_divergence(ext_ref, vel_ref, flux_ref, rows):
    faces = flux_ref.shape[0]
    for low in range(0, faces, CHUNK):

        def cut(offset):
            return ext_ref[pl.ds(HALO - 3 + offset + low, CHUNK), :]

        face_speed = 0.5 * (
            vel_ref[pl.ds(HALO - 1 + low, CHUNK), :] + vel_ref[pl.ds(HALO + low, CHUNK), :]
        )
        forward = face_speed >= 0.0
        stencil = [
            jnp.where(forward, cut(lower), cut(upper))
            for lower, upper in ((0, 5), (1, 4), (2, 3), (3, 2), (4, 1))
        ]
        flux_ref[pl.ds(low, CHUNK), :] = face_speed * weno_side(*stencil)
    return flux_ref[pl.ds(1, rows), :] - flux_ref[pl.ds(0, rows), :]


def transport_kernel(
    field_ref, speed_ref, top_ref, top_speed_ref, bottom_ref, bottom_speed_ref,
    left_ref, left_speed_ref, right_ref, right_speed_ref, out_ref,
    ext_ref, vel_ref, flux_ref,
):
    rows, cols = field_ref.shape[1], field_ref.shape[2]
    group = field_ref.shape[0]

    def one_species(member, carry):
        field = field_ref[member]
        fill_scratch(ext_ref, top_ref[member], field, bottom_ref[member])
        fill_scratch(vel_ref, top_speed_ref[0], speed_ref[0], bottom_speed_ref[0])
        along_axial = upwind_divergence(ext_ref, vel_ref, flux_ref, rows)
        fill_scratch(ext_ref, left_ref[member], field.T, right_ref[member])
        fill_scratch(vel_ref, left_speed_ref[0], speed_ref[1].T, right_speed_ref[0])
        along_radial = upwind_divergence(ext_ref, vel_ref, flux_ref, cols).T
        moved = field - TIME_STEP * (along_axial + along_radial)
        out_ref[:, pl.ds(pl.program_id(0) * group + member, 1), :] = moved[:, None, :]
        return carry

    lax.fori_loop(0, group, one_species, 0)


def fill_scratch(scratch, before, body, after):
    span, cols = scratch.shape
    width, rows = (before.shape[0], body.shape[0])
    scratch[pl.ds(0, HALO), :] = jnp.zeros((HALO, cols), jnp.float32)
    scratch[pl.ds(HALO + rows, span - HALO - rows), :] = jnp.zeros(
        (span - HALO - rows, cols), jnp.float32
    )
    scratch[pl.ds(HALO - width, width), :] = before
    scratch[pl.ds(HALO, rows), :] = body
    scratch[pl.ds(HALO + rows, width), :] = after


def edge_columns(field, width):
    cols = field.shape[2]
    row = lax.broadcasted_iota(jnp.int32, (2 * width, cols), 0)
    column = lax.broadcasted_iota(jnp.int32, (2 * width, cols), 1)
    pick = column == jnp.where(row < width, row + cols - width, row - width)
    picked = jnp.einsum("kr,sar->ska", pick.astype(field.dtype), field, precision=HIGHEST)
    return picked[:, :width], picked[:, width:]


def transport(species, speed, width=3):
    species_count, rows, cols = species.shape
    assert rows == cols and rows % CHUNK == 0
    axial_edges = jnp.concatenate([species, speed[0:1]], axis=0)
    top, bottom = edge_layers(axial_edges, "axial", 1, width)
    radial_edges = jnp.concatenate([species, speed[1:2]], axis=0)
    peers = lax.axis_size("radial")
    up = [(i, i + 1) for i in range(peers - 1)]
    down = [(j, i) for i, j in up]
    high_columns, low_columns = edge_columns(radial_edges, width)
    left = lax.ppermute(high_columns, "radial", up)
    right = lax.ppermute(low_columns, "radial", down)
    faces = rows + CHUNK
    span = HALO + faces + HALO
    group = max(g for g in range(1, SPECIES_GROUP + 1) if species_count % g == 0)
    plane = pl.BlockSpec((group, rows, cols), lambda s: (s, 0, 0))
    speeds = pl.BlockSpec((2, rows, cols), lambda s: (0, 0, 0))
    edge = pl.BlockSpec((group, width, cols), lambda s: (s, 0, 0))
    edge_speed = pl.BlockSpec((1, width, cols), lambda s: (species_count, 0, 0))
    moved_rows = pl.pallas_call(
        transport_kernel,
        grid=(species_count // group,),
        in_specs=[plane, speeds] + [edge, edge_speed] * 4,
        out_specs=pl.BlockSpec((rows, species_count, cols), lambda s: (0, 0, 0)),
        out_shape=jax.ShapeDtypeStruct((rows, species_count, cols), jnp.float32),
        scratch_shapes=[
            pltpu.VMEM((span, cols), jnp.float32),
            pltpu.VMEM((span, cols), jnp.float32),
            pltpu.VMEM((faces, cols), jnp.float32),
        ],
    )(species, speed, top, top, bottom, bottom, left, left, right, right)
    return jnp.transpose(moved_rows, (1, 0, 2))


def kinetics_advance(
    starting_composition_field,
    thermal_field,
    linearized_kinetics_operator,
    frozen_jacobian_inverse_addend,
):
    acceleration_factor = jnp.exp(-ARRHENIUS_BARRIER / thermal_field)
    current = starting_composition_field
    for newton_step in range(ITERS):
        source = jnp.tensordot(
            linearized_kinetics_operator, current, axes=(1, 0), precision=CHEMISTRY_PRECISION
        ) - jnp.tanh(current)
        defect = current - starting_composition_field - CHEM_STEP * acceleration_factor * source
        current = (
            current
            - defect
            - jnp.tensordot(frozen_jacobian_inverse_addend, defect, axes=(1, 0), precision=CHEMISTRY_PRECISION)
        )
    return current


def absorbance_profile(field, molar_absorptivity_table, spokewise_sightline_length):
    mixed = jnp.tensordot(molar_absorptivity_table, field, axes=(1, 0), precision=HIGHEST)
    return jnp.dot(mixed, spokewise_sightline_length, precision=HIGHEST)


def butterfly_sum(part, axis):
    peers, stride = (lax.axis_size(axis), 1)
    if peers & (peers - 1):
        return lax.psum(part, axis)
    while stride < peers:
        pairs = [(j, j ^ stride) for j in range(peers)]
        part = part + lax.ppermute(part, axis, pairs)
        stride *= 2
    return part


def pick_samples(blocks, first, rows):
    count, lasers, block = blocks.shape
    flat = jnp.transpose(blocks, (1, 0, 2)).reshape(lasers, count * block)
    local = rows - first * block
    cells = lax.broadcasted_iota(jnp.int32, (1, count * block, 1), 1)
    return jnp.sum(jnp.where(local[:, None, :] == cells, flat[:, :, None], 0.0), axis=1)


def sampled_profile(part, rows, axis="axial"):
    column = butterfly_sum(part, "radial")
    peers, stride = (lax.axis_size(axis), 1)
    if peers & (peers - 1):
        return pick_samples(lax.all_gather(column, axis), 0, rows)
    position = lax.axis_index(axis)
    blocks = column[None]
    values = pick_samples(blocks, position, rows)
    while stride < peers:
        pairs = [(j, j ^ stride) for j in range(peers)]
        other = lax.ppermute(blocks, axis, pairs)
        values = values + pick_samples(other, (position // stride) * stride ^ stride, rows)
        upper = (position // stride) % 2 == 1
        if 2 * stride < peers:
            blocks = jnp.where(
                upper, jnp.concatenate([other, blocks], 0), jnp.concatenate([blocks, other], 0)
            )
        stride *= 2
    return values


def local(
    composition_deviations,
    flow_speed_vector,
    thermal_field,
    linearized_kinetics_operator,
    frozen_jacobian_inverse_addend,
    rigid_block_indicator,
    molar_absorptivity_table,
    spokewise_sightline_length,
    sightline_lengthwise_index,
    observed_absorbance_traces,
):
    advected_composition_field = transport(composition_deviations, flow_speed_vector)
    combusted_composition_field = kinetics_advance(
        advected_composition_field,
        thermal_field,
        linearized_kinetics_operator,
        frozen_jacobian_inverse_addend,
    )
    flag_cells = jnp.repeat(
        jnp.repeat(rigid_block_indicator, TILE_ROWS, axis=0),
        advected_composition_field.shape[2],
        axis=1,
    )
    species_out = jnp.where(
        flag_cells[None] > 0, combusted_composition_field, advected_composition_field
    )
    path_scale = 1.0 / math.sqrt(advected_composition_field.shape[2] * lax.axis_size("radial"))
    profile = (
        absorbance_profile(species_out, molar_absorptivity_table, spokewise_sightline_length)
        * path_scale
    )
    device = lax.axis_index(("axial", "radial"))
    sample_count = observed_absorbance_traces.shape[1]
    own_rows = lax.dynamic_slice_in_dim(
        sightline_lengthwise_index, device * sample_count, sample_count, 1
    )
    values = sampled_profile(profile, own_rows)
    return (species_out, values - observed_absorbance_traces)


def solution(mesh):
    in_specs = (
        P(None, "axial", "radial"),
        P(None, "axial", "radial"),
        P("axial", "radial"),
        P(),
        P(),
        P("axial", "radial"),
        P(),
        P("radial"),
        P(),
        P(None, ("axial", "radial")),
    )
    out_specs = (P(None, "axial", "radial"), P(None, ("axial", "radial")))
    return jax.shard_map(local, mesh=mesh, in_specs=in_specs, out_specs=out_specs, check_vma=False)
```

```python
import math

import jax
import jax.numpy as jnp
from jax import lax
from jax.sharding import PartitionSpec as P
from jax.experimental import pallas as pl
from jax.experimental.pallas import tpu as pltpu

TILE_ROWS = 2
ITERS = 3


TIME_STEP = 0.4
CHEM_STEP = 0.5
ARRHENIUS_BARRIER = 1.0
WENO_EPS = 1e-06
HIGHEST = lax.Precision.HIGHEST
CHEMISTRY_PRECISION = lax.Precision.HIGH


def edge_layers(shard, axis, dim, width):
    peers, length = (lax.axis_size(axis), shard.shape[dim])
    up = [(i, i + 1) for i in range(peers - 1)]
    down = [(j, i) for i, j in up]
    last = lax.slice_in_dim(shard, length - width, length, axis=dim)
    initial = lax.slice_in_dim(shard, 0, width, axis=dim)
    return lax.ppermute(last, axis, up), lax.ppermute(initial, axis, down)


SCALED_EPS = WENO_EPS * 12.0 / 13.0
SLOPE_WEIGHT = 3.0 / 13.0


def weno_side(minus_two, minus_one, centre, plus_one, plus_two):
    curve_zero = (minus_two + centre) - (minus_one + minus_one)
    curve_one = (minus_one + plus_one) - (centre + centre)
    curve_two = (centre + plus_two) - (plus_one + plus_one)
    slope_zero = curve_zero + 2.0 * (centre - minus_one)
    slope_one = minus_one - plus_one
    slope_two = curve_two + 2.0 * (centre - plus_one)
    guard_zero = (SCALED_EPS + curve_zero * curve_zero) + SLOPE_WEIGHT * (slope_zero * slope_zero)
    guard_one = (SCALED_EPS + curve_one * curve_one) + SLOPE_WEIGHT * (slope_one * slope_one)
    guard_two = (SCALED_EPS + curve_two * curve_two) + SLOPE_WEIGHT * (slope_two * slope_two)
    guard_zero = guard_zero * guard_zero
    guard_one = guard_one * guard_one
    guard_two = guard_two * guard_two
    cross_zero = guard_one * guard_two
    cross_one = 6.0 * (guard_zero * guard_two)
    cross_two = 3.0 * (guard_zero * guard_one)
    blended = cross_zero * (curve_zero + 3.0 * slope_zero)
    blended = blended + cross_one * (curve_one - 3.0 * slope_one)
    blended = blended + cross_two * (curve_two - 3.0 * slope_two)
    return centre + blended / (12.0 * (cross_zero + cross_one + cross_two))


HALO = 8
SPECIES_GROUP = 19
CHUNK = 8


def upwind_divergence(ext_ref, vel_ref, flux_ref, rows):
    faces = flux_ref.shape[0]
    for low in range(0, faces, CHUNK):

        def cut(offset):
            return ext_ref[pl.ds(HALO - 3 + offset + low, CHUNK), :]

        face_speed = 0.5 * (
            vel_ref[pl.ds(HALO - 1 + low, CHUNK), :] + vel_ref[pl.ds(HALO + low, CHUNK), :]
        )
        forward = face_speed >= 0.0
        stencil = [
            jnp.where(forward, cut(lower), cut(upper))
            for lower, upper in ((0, 5), (1, 4), (2, 3), (3, 2), (4, 1))
        ]
        flux_ref[pl.ds(low, CHUNK), :] = face_speed * weno_side(*stencil)
    return flux_ref[pl.ds(1, rows), :] - flux_ref[pl.ds(0, rows), :]


def transport_kernel(
    field_ref, speed_ref, top_ref, top_speed_ref, bottom_ref, bottom_speed_ref,
    left_ref, left_speed_ref, right_ref, right_speed_ref, out_ref,
    ext_ref, axial_speed_ref, radial_speed_ref, flux_ref,
):
    rows, cols = field_ref.shape[1], field_ref.shape[2]
    group = field_ref.shape[0]
    fill_scratch(axial_speed_ref, top_speed_ref[0], speed_ref[0], bottom_speed_ref[0])
    fill_scratch(radial_speed_ref, left_speed_ref[0], speed_ref[1].T, right_speed_ref[0])

    def one_species(member, carry):
        field = field_ref[member]
        fill_scratch(ext_ref, top_ref[member], field, bottom_ref[member])
        along_axial = upwind_divergence(ext_ref, axial_speed_ref, flux_ref, rows)
        fill_scratch(ext_ref, left_ref[member], field.T, right_ref[member])
        along_radial = upwind_divergence(ext_ref, radial_speed_ref, flux_ref, cols).T
        moved = field - TIME_STEP * (along_axial + along_radial)
        out_ref[:, pl.ds(pl.program_id(0) * group + member, 1), :] = moved[:, None, :]
        return carry

    lax.fori_loop(0, group, one_species, 0)


def fill_scratch(scratch, before, body, after):
    span, cols = scratch.shape
    width, rows = (before.shape[0], body.shape[0])
    scratch[pl.ds(0, HALO), :] = jnp.zeros((HALO, cols), jnp.float32)
    scratch[pl.ds(HALO + rows, span - HALO - rows), :] = jnp.zeros(
        (span - HALO - rows, cols), jnp.float32
    )
    scratch[pl.ds(HALO - width, width), :] = before
    scratch[pl.ds(HALO, rows), :] = body
    scratch[pl.ds(HALO + rows, width), :] = after


def edge_columns(field, width):
    cols = field.shape[2]
    row = lax.broadcasted_iota(jnp.int32, (2 * width, cols), 0)
    column = lax.broadcasted_iota(jnp.int32, (2 * width, cols), 1)
    pick = column == jnp.where(row < width, row + cols - width, row - width)
    picked = jnp.einsum("kr,sar->ska", pick.astype(field.dtype), field, precision=HIGHEST)
    return picked[:, :width], picked[:, width:]


def transport(species, speed, width=3):
    species_count, rows, cols = species.shape
    assert rows == cols and rows % CHUNK == 0
    axial_edges = jnp.concatenate([species, speed[0:1]], axis=0)
    top, bottom = edge_layers(axial_edges, "axial", 1, width)
    radial_edges = jnp.concatenate([species, speed[1:2]], axis=0)
    peers = lax.axis_size("radial")
    up = [(i, i + 1) for i in range(peers - 1)]
    down = [(j, i) for i, j in up]
    high_columns, low_columns = edge_columns(radial_edges, width)
    left = lax.ppermute(high_columns, "radial", up)
    right = lax.ppermute(low_columns, "radial", down)
    faces = rows + CHUNK
    span = HALO + faces + HALO
    group = max(g for g in range(1, SPECIES_GROUP + 1) if species_count % g == 0)
    plane = pl.BlockSpec((group, rows, cols), lambda s: (s, 0, 0))
    speeds = pl.BlockSpec((2, rows, cols), lambda s: (0, 0, 0))
    edge = pl.BlockSpec((group, width, cols), lambda s: (s, 0, 0))
    edge_speed = pl.BlockSpec((1, width, cols), lambda s: (species_count, 0, 0))
    moved_rows = pl.pallas_call(
        transport_kernel,
        grid=(species_count // group,),
        in_specs=[plane, speeds] + [edge, edge_speed] * 4,
        out_specs=pl.BlockSpec((rows, species_count, cols), lambda s: (0, 0, 0)),
        out_shape=jax.ShapeDtypeStruct((rows, species_count, cols), jnp.float32),
        scratch_shapes=[
            pltpu.VMEM((span, cols), jnp.float32),
            pltpu.VMEM((span, cols), jnp.float32),
            pltpu.VMEM((span, cols), jnp.float32),
            pltpu.VMEM((faces, cols), jnp.float32),
        ],
    )(species, speed, top, top, bottom, bottom, left, left, right, right)
    return jnp.transpose(moved_rows, (1, 0, 2))


def kinetics_advance(
    starting_composition_field,
    thermal_field,
    linearized_kinetics_operator,
    frozen_jacobian_inverse_addend,
):
    acceleration_factor = jnp.exp(-ARRHENIUS_BARRIER / thermal_field)
    current = starting_composition_field
    for newton_step in range(ITERS):
        source = jnp.tensordot(
            linearized_kinetics_operator, current, axes=(1, 0), precision=CHEMISTRY_PRECISION
        ) - jnp.tanh(current)
        defect = current - starting_composition_field - CHEM_STEP * acceleration_factor * source
        current = (
            current
            - defect
            - jnp.tensordot(frozen_jacobian_inverse_addend, defect, axes=(1, 0), precision=CHEMISTRY_PRECISION)
        )
    return current


def absorbance_profile(field, molar_absorptivity_table, spokewise_sightline_length):
    mixed = jnp.tensordot(molar_absorptivity_table, field, axes=(1, 0), precision=HIGHEST)
    return jnp.dot(mixed, spokewise_sightline_length, precision=HIGHEST)


def butterfly_sum(part, axis):
    peers, stride = (lax.axis_size(axis), 1)
    if peers & (peers - 1):
        return lax.psum(part, axis)
    while stride < peers:
        pairs = [(j, j ^ stride) for j in range(peers)]
        part = part + lax.ppermute(part, axis, pairs)
        stride *= 2
    return part


def pick_samples(blocks, first, rows):
    count, lasers, block = blocks.shape
    flat = jnp.transpose(blocks, (1, 0, 2)).reshape(lasers, count * block)
    local = rows - first * block
    cells = lax.broadcasted_iota(jnp.int32, (1, count * block, 1), 1)
    return jnp.sum(jnp.where(local[:, None, :] == cells, flat[:, :, None], 0.0), axis=1)


def sampled_profile(part, rows, axis="axial"):
    column = butterfly_sum(part, "radial")
    peers, stride = (lax.axis_size(axis), 1)
    if peers & (peers - 1):
        return pick_samples(lax.all_gather(column, axis), 0, rows)
    position = lax.axis_index(axis)
    blocks = column[None]
    values = pick_samples(blocks, position, rows)
    while stride < peers:
        pairs = [(j, j ^ stride) for j in range(peers)]
        other = lax.ppermute(blocks, axis, pairs)
        values = values + pick_samples(other, (position // stride) * stride ^ stride, rows)
        upper = (position // stride) % 2 == 1
        if 2 * stride < peers:
            blocks = jnp.where(
                upper, jnp.concatenate([other, blocks], 0), jnp.concatenate([blocks, other], 0)
            )
        stride *= 2
    return values


def local(
    composition_deviations,
    flow_speed_vector,
    thermal_field,
    linearized_kinetics_operator,
    frozen_jacobian_inverse_addend,
    rigid_block_indicator,
    molar_absorptivity_table,
    spokewise_sightline_length,
    sightline_lengthwise_index,
    observed_absorbance_traces,
):
    advected_composition_field = transport(composition_deviations, flow_speed_vector)
    combusted_composition_field = kinetics_advance(
        advected_composition_field,
        thermal_field,
        linearized_kinetics_operator,
        frozen_jacobian_inverse_addend,
    )
    flag_cells = jnp.repeat(
        jnp.repeat(rigid_block_indicator, TILE_ROWS, axis=0),
        advected_composition_field.shape[2],
        axis=1,
    )
    species_out = jnp.where(
        flag_cells[None] > 0, combusted_composition_field, advected_composition_field
    )
    path_scale = 1.0 / math.sqrt(advected_composition_field.shape[2] * lax.axis_size("radial"))
    profile = (
        absorbance_profile(species_out, molar_absorptivity_table, spokewise_sightline_length)
        * path_scale
    )
    device = lax.axis_index(("axial", "radial"))
    sample_count = observed_absorbance_traces.shape[1]
    own_rows = lax.dynamic_slice_in_dim(
        sightline_lengthwise_index, device * sample_count, sample_count, 1
    )
    values = sampled_profile(profile, own_rows)
    return (species_out, values - observed_absorbance_traces)


def solution(mesh):
    in_specs = (
        P(None, "axial", "radial"),
        P(None, "axial", "radial"),
        P("axial", "radial"),
        P(),
        P(),
        P("axial", "radial"),
        P(),
        P("radial"),
        P(),
        P(None, ("axial", "radial")),
    )
    out_specs = (P(None, "axial", "radial"), P(None, ("axial", "radial")))
    return jax.shard_map(local, mesh=mesh, in_specs=in_specs, out_specs=out_specs, check_vma=False)
```

```python
import math

import jax
import jax.numpy as jnp
from jax import lax
from jax.sharding import PartitionSpec as P
from jax.experimental import pallas as pl
from jax.experimental.pallas import tpu as pltpu

TILE_ROWS = 2
ITERS = 3


TIME_STEP = 0.4
CHEM_STEP = 0.5
ARRHENIUS_BARRIER = 1.0
WENO_EPS = 1e-06
HIGHEST = lax.Precision.HIGHEST
CHEMISTRY_PRECISION = lax.Precision.HIGH


def edge_layers(shard, axis, dim, width):
    peers, length = (lax.axis_size(axis), shard.shape[dim])
    up = [(i, i + 1) for i in range(peers - 1)]
    down = [(j, i) for i, j in up]
    last = lax.slice_in_dim(shard, length - width, length, axis=dim)
    initial = lax.slice_in_dim(shard, 0, width, axis=dim)
    return lax.ppermute(last, axis, up), lax.ppermute(initial, axis, down)


SCALED_EPS = WENO_EPS * 12.0 / 13.0
SLOPE_WEIGHT = 3.0 / 13.0


def weno_side(minus_two, minus_one, centre, plus_one, plus_two):
    curve_zero = (minus_two + centre) - (minus_one + minus_one)
    curve_one = (minus_one + plus_one) - (centre + centre)
    curve_two = (centre + plus_two) - (plus_one + plus_one)
    slope_zero = curve_zero + 2.0 * (centre - minus_one)
    slope_one = minus_one - plus_one
    slope_two = curve_two + 2.0 * (centre - plus_one)
    guard_zero = (SCALED_EPS + curve_zero * curve_zero) + SLOPE_WEIGHT * (slope_zero * slope_zero)
    guard_one = (SCALED_EPS + curve_one * curve_one) + SLOPE_WEIGHT * (slope_one * slope_one)
    guard_two = (SCALED_EPS + curve_two * curve_two) + SLOPE_WEIGHT * (slope_two * slope_two)
    guard_zero = guard_zero * guard_zero
    guard_one = guard_one * guard_one
    guard_two = guard_two * guard_two
    cross_zero = guard_one * guard_two
    cross_one = 6.0 * (guard_zero * guard_two)
    cross_two = 3.0 * (guard_zero * guard_one)
    blended = cross_zero * (curve_zero + 3.0 * slope_zero)
    blended = blended + cross_one * (curve_one - 3.0 * slope_one)
    blended = blended + cross_two * (curve_two - 3.0 * slope_two)
    return centre + blended / (12.0 * (cross_zero + cross_one + cross_two))


HALO = 8
SPECIES_GROUP = 38
CHUNK = 8


def upwind_divergence(ext_ref, vel_ref, flux_ref, rows):
    faces = flux_ref.shape[0]
    for low in range(0, faces, CHUNK):

        def cut(offset):
            return ext_ref[pl.ds(HALO - 3 + offset + low, CHUNK), :]

        face_speed = 0.5 * (
            vel_ref[pl.ds(HALO - 1 + low, CHUNK), :] + vel_ref[pl.ds(HALO + low, CHUNK), :]
        )
        forward = face_speed >= 0.0
        stencil = [
            jnp.where(forward, cut(lower), cut(upper))
            for lower, upper in ((0, 5), (1, 4), (2, 3), (3, 2), (4, 1))
        ]
        flux_ref[pl.ds(low, CHUNK), :] = face_speed * weno_side(*stencil)
    return flux_ref[pl.ds(1, rows), :] - flux_ref[pl.ds(0, rows), :]


def transport_kernel(
    field_ref, speed_ref, top_ref, top_speed_ref, bottom_ref, bottom_speed_ref,
    left_ref, left_speed_ref, right_ref, right_speed_ref, out_ref,
    ext_ref, axial_speed_ref, radial_speed_ref, flux_ref,
):
    rows, cols = field_ref.shape[1], field_ref.shape[2]
    group = field_ref.shape[0]
    fill_scratch(axial_speed_ref, top_speed_ref[0], speed_ref[0], bottom_speed_ref[0])
    fill_scratch(radial_speed_ref, left_speed_ref[0], speed_ref[1].T, right_speed_ref[0])

    def one_species(member, carry):
        field = field_ref[member]
        fill_scratch(ext_ref, top_ref[member], field, bottom_ref[member])
        along_axial = upwind_divergence(ext_ref, axial_speed_ref, flux_ref, rows)
        fill_scratch(ext_ref, left_ref[member], field.T, right_ref[member])
        along_radial = upwind_divergence(ext_ref, radial_speed_ref, flux_ref, cols).T
        moved = field - TIME_STEP * (along_axial + along_radial)
        out_ref[:, pl.ds(pl.program_id(0) * group + member, 1), :] = moved[:, None, :]
        return carry

    lax.fori_loop(0, group, one_species, 0)


def fill_scratch(scratch, before, body, after):
    span, cols = scratch.shape
    width, rows = (before.shape[0], body.shape[0])
    scratch[pl.ds(0, HALO), :] = jnp.zeros((HALO, cols), jnp.float32)
    scratch[pl.ds(HALO + rows, span - HALO - rows), :] = jnp.zeros(
        (span - HALO - rows, cols), jnp.float32
    )
    scratch[pl.ds(HALO - width, width), :] = before
    scratch[pl.ds(HALO, rows), :] = body
    scratch[pl.ds(HALO + rows, width), :] = after


def edge_columns(field, width):
    cols = field.shape[2]
    row = lax.broadcasted_iota(jnp.int32, (2 * width, cols), 0)
    column = lax.broadcasted_iota(jnp.int32, (2 * width, cols), 1)
    pick = column == jnp.where(row < width, row + cols - width, row - width)
    picked = jnp.einsum("kr,sar->ska", pick.astype(field.dtype), field, precision=HIGHEST)
    return picked[:, :width], picked[:, width:]


def transport(species, speed, width=3):
    species_count, rows, cols = species.shape
    assert rows == cols and rows % CHUNK == 0
    axial_edges = jnp.concatenate([species, speed[0:1]], axis=0)
    top, bottom = edge_layers(axial_edges, "axial", 1, width)
    radial_edges = jnp.concatenate([species, speed[1:2]], axis=0)
    peers = lax.axis_size("radial")
    up = [(i, i + 1) for i in range(peers - 1)]
    down = [(j, i) for i, j in up]
    high_columns, low_columns = edge_columns(radial_edges, width)
    left = lax.ppermute(high_columns, "radial", up)
    right = lax.ppermute(low_columns, "radial", down)
    faces = rows + CHUNK
    span = HALO + faces + HALO
    group = max(g for g in range(1, SPECIES_GROUP + 1) if species_count % g == 0)
    plane = pl.BlockSpec((group, rows, cols), lambda s: (s, 0, 0))
    speeds = pl.BlockSpec((2, rows, cols), lambda s: (0, 0, 0))
    edge = pl.BlockSpec((group, width, cols), lambda s: (s, 0, 0))
    edge_speed = pl.BlockSpec((1, width, cols), lambda s: (species_count, 0, 0))
    moved_rows = pl.pallas_call(
        transport_kernel,
        grid=(species_count // group,),
        in_specs=[plane, speeds] + [edge, edge_speed] * 4,
        out_specs=pl.BlockSpec((rows, species_count, cols), lambda s: (0, 0, 0)),
        out_shape=jax.ShapeDtypeStruct((rows, species_count, cols), jnp.float32),
        scratch_shapes=[
            pltpu.VMEM((span, cols), jnp.float32),
            pltpu.VMEM((span, cols), jnp.float32),
            pltpu.VMEM((span, cols), jnp.float32),
            pltpu.VMEM((faces, cols), jnp.float32),
        ],
    )(species, speed, top, top, bottom, bottom, left, left, right, right)
    return jnp.transpose(moved_rows, (1, 0, 2))


def kinetics_advance(
    starting_composition_field,
    thermal_field,
    linearized_kinetics_operator,
    frozen_jacobian_inverse_addend,
):
    acceleration_factor = jnp.exp(-ARRHENIUS_BARRIER / thermal_field)
    current = starting_composition_field
    for newton_step in range(ITERS):
        source = jnp.tensordot(
            linearized_kinetics_operator, current, axes=(1, 0), precision=CHEMISTRY_PRECISION
        ) - jnp.tanh(current)
        defect = current - starting_composition_field - CHEM_STEP * acceleration_factor * source
        current = (
            current
            - defect
            - jnp.tensordot(frozen_jacobian_inverse_addend, defect, axes=(1, 0), precision=CHEMISTRY_PRECISION)
        )
    return current


def absorbance_profile(field, molar_absorptivity_table, spokewise_sightline_length):
    mixed = jnp.tensordot(molar_absorptivity_table, field, axes=(1, 0), precision=HIGHEST)
    return jnp.dot(mixed, spokewise_sightline_length, precision=HIGHEST)


def butterfly_sum(part, axis):
    peers, stride = (lax.axis_size(axis), 1)
    if peers & (peers - 1):
        return lax.psum(part, axis)
    while stride < peers:
        pairs = [(j, j ^ stride) for j in range(peers)]
        part = part + lax.ppermute(part, axis, pairs)
        stride *= 2
    return part


def pick_samples(blocks, first, rows):
    count, lasers, block = blocks.shape
    flat = jnp.transpose(blocks, (1, 0, 2)).reshape(lasers, count * block)
    local = rows - first * block
    cells = lax.broadcasted_iota(jnp.int32, (1, count * block, 1), 1)
    return jnp.sum(jnp.where(local[:, None, :] == cells, flat[:, :, None], 0.0), axis=1)


def sampled_profile(part, rows, axis="axial"):
    column = butterfly_sum(part, "radial")
    peers, stride = (lax.axis_size(axis), 1)
    if peers & (peers - 1):
        return pick_samples(lax.all_gather(column, axis), 0, rows)
    position = lax.axis_index(axis)
    blocks = column[None]
    values = pick_samples(blocks, position, rows)
    while stride < peers:
        pairs = [(j, j ^ stride) for j in range(peers)]
        other = lax.ppermute(blocks, axis, pairs)
        values = values + pick_samples(other, (position // stride) * stride ^ stride, rows)
        upper = (position // stride) % 2 == 1
        if 2 * stride < peers:
            blocks = jnp.where(
                upper, jnp.concatenate([other, blocks], 0), jnp.concatenate([blocks, other], 0)
            )
        stride *= 2
    return values


def local(
    composition_deviations,
    flow_speed_vector,
    thermal_field,
    linearized_kinetics_operator,
    frozen_jacobian_inverse_addend,
    rigid_block_indicator,
    molar_absorptivity_table,
    spokewise_sightline_length,
    sightline_lengthwise_index,
    observed_absorbance_traces,
):
    advected_composition_field = transport(composition_deviations, flow_speed_vector)
    combusted_composition_field = kinetics_advance(
        advected_composition_field,
        thermal_field,
        linearized_kinetics_operator,
        frozen_jacobian_inverse_addend,
    )
    flag_cells = jnp.repeat(
        jnp.repeat(rigid_block_indicator, TILE_ROWS, axis=0),
        advected_composition_field.shape[2],
        axis=1,
    )
    species_out = jnp.where(
        flag_cells[None] > 0, combusted_composition_field, advected_composition_field
    )
    path_scale = 1.0 / math.sqrt(advected_composition_field.shape[2] * lax.axis_size("radial"))
    profile = (
        absorbance_profile(species_out, molar_absorptivity_table, spokewise_sightline_length)
        * path_scale
    )
    device = lax.axis_index(("axial", "radial"))
    sample_count = observed_absorbance_traces.shape[1]
    own_rows = lax.dynamic_slice_in_dim(
        sightline_lengthwise_index, device * sample_count, sample_count, 1
    )
    values = sampled_profile(profile, own_rows)
    return (species_out, values - observed_absorbance_traces)


def solution(mesh):
    in_specs = (
        P(None, "axial", "radial"),
        P(None, "axial", "radial"),
        P("axial", "radial"),
        P(),
        P(),
        P("axial", "radial"),
        P(),
        P("radial"),
        P(),
        P(None, ("axial", "radial")),
    )
    out_specs = (P(None, "axial", "radial"), P(None, ("axial", "radial")))
    return jax.shard_map(local, mesh=mesh, in_specs=in_specs, out_specs=out_specs, check_vma=False)
```

```python
import math

import jax
import jax.numpy as jnp
from jax import lax
from jax.sharding import PartitionSpec as P
from jax.experimental import pallas as pl
from jax.experimental.pallas import tpu as pltpu

TILE_ROWS = 2
ITERS = 3


TIME_STEP = 0.4
CHEM_STEP = 0.5
ARRHENIUS_BARRIER = 1.0
WENO_EPS = 1e-06
HIGHEST = lax.Precision.HIGHEST
CHEMISTRY_PRECISION = lax.Precision.HIGH


def edge_layers(shard, axis, dim, width):
    peers, length = (lax.axis_size(axis), shard.shape[dim])
    up = [(i, i + 1) for i in range(peers - 1)]
    down = [(j, i) for i, j in up]
    last = lax.slice_in_dim(shard, length - width, length, axis=dim)
    initial = lax.slice_in_dim(shard, 0, width, axis=dim)
    return lax.ppermute(last, axis, up), lax.ppermute(initial, axis, down)


SCALED_EPS = WENO_EPS * 12.0 / 13.0
SLOPE_WEIGHT = 3.0 / 13.0


def weno_side(minus_two, minus_one, centre, plus_one, plus_two):
    curve_zero = (minus_two + centre) - (minus_one + minus_one)
    curve_one = (minus_one + plus_one) - (centre + centre)
    curve_two = (centre + plus_two) - (plus_one + plus_one)
    slope_zero = curve_zero + 2.0 * (centre - minus_one)
    slope_one = minus_one - plus_one
    slope_two = curve_two + 2.0 * (centre - plus_one)
    guard_zero = (SCALED_EPS + curve_zero * curve_zero) + SLOPE_WEIGHT * (slope_zero * slope_zero)
    guard_one = (SCALED_EPS + curve_one * curve_one) + SLOPE_WEIGHT * (slope_one * slope_one)
    guard_two = (SCALED_EPS + curve_two * curve_two) + SLOPE_WEIGHT * (slope_two * slope_two)
    guard_zero = guard_zero * guard_zero
    guard_one = guard_one * guard_one
    guard_two = guard_two * guard_two
    cross_zero = guard_one * guard_two
    cross_one = 6.0 * (guard_zero * guard_two)
    cross_two = 3.0 * (guard_zero * guard_one)
    blended = cross_zero * (curve_zero + 3.0 * slope_zero)
    blended = blended + cross_one * (curve_one - 3.0 * slope_one)
    blended = blended + cross_two * (curve_two - 3.0 * slope_two)
    return centre + blended / (12.0 * (cross_zero + cross_one + cross_two))


HALO = 8
SPECIES_GROUP = 19
CHUNK = 8


def upwind_divergence(ext_ref, vel_ref, flux_ref, rows):
    faces = flux_ref.shape[0]
    for low in range(0, faces, CHUNK):

        def cut(offset):
            return ext_ref[pl.ds(HALO - 3 + offset + low, CHUNK), :]

        face_speed = 0.5 * (
            vel_ref[pl.ds(HALO - 1 + low, CHUNK), :] + vel_ref[pl.ds(HALO + low, CHUNK), :]
        )
        forward = face_speed >= 0.0
        stencil = [
            jnp.where(forward, cut(lower), cut(upper))
            for lower, upper in ((0, 5), (1, 4), (2, 3), (3, 2), (4, 1))
        ]
        flux_ref[pl.ds(low, CHUNK), :] = face_speed * weno_side(*stencil)
    return flux_ref[pl.ds(1, rows), :] - flux_ref[pl.ds(0, rows), :]


def transport_kernel(
    field_ref, speed_ref, top_ref, top_speed_ref, bottom_ref, bottom_speed_ref,
    left_ref, left_speed_ref, right_ref, right_speed_ref, out_ref,
    ext_ref, axial_speed_ref, radial_speed_ref, flux_ref,
):
    rows, cols = field_ref.shape[1], field_ref.shape[2]
    group = field_ref.shape[0]
    fill_scratch(axial_speed_ref, top_speed_ref[0], speed_ref[0], bottom_speed_ref[0])
    fill_scratch(radial_speed_ref, left_speed_ref[0], speed_ref[1].T, right_speed_ref[0])

    def one_species(member, carry):
        field = field_ref[member]
        fill_scratch(ext_ref, top_ref[member], field, bottom_ref[member])
        along_axial = upwind_divergence(ext_ref, axial_speed_ref, flux_ref, rows)
        fill_scratch(ext_ref, left_ref[member], field.T, right_ref[member])
        along_radial = upwind_divergence(ext_ref, radial_speed_ref, flux_ref, cols).T
        moved = field - TIME_STEP * (along_axial + along_radial)
        out_ref[:, pl.ds(pl.program_id(0) * group + member, 1), :] = moved[:, None, :]
        return carry

    lax.fori_loop(0, group, one_species, 0)


def fill_scratch(scratch, before, body, after):
    span, cols = scratch.shape
    width, rows = (before.shape[0], body.shape[0])
    scratch[pl.ds(0, HALO), :] = jnp.zeros((HALO, cols), jnp.float32)
    scratch[pl.ds(HALO + rows, span - HALO - rows), :] = jnp.zeros(
        (span - HALO - rows, cols), jnp.float32
    )
    scratch[pl.ds(HALO - width, width), :] = before
    scratch[pl.ds(HALO, rows), :] = body
    scratch[pl.ds(HALO + rows, width), :] = after


def edge_columns(field, width):
    cols = field.shape[2]
    row = lax.broadcasted_iota(jnp.int32, (2 * width, cols), 0)
    column = lax.broadcasted_iota(jnp.int32, (2 * width, cols), 1)
    pick = column == jnp.where(row < width, row + cols - width, row - width)
    picked = jnp.einsum("kr,sar->ska", pick.astype(field.dtype), field, precision=HIGHEST)
    return picked[:, :width], picked[:, width:]


def transport(species, speed, width=3):
    species_count, rows, cols = species.shape
    assert rows == cols and rows % CHUNK == 0
    axial_edges = jnp.concatenate([species, speed[0:1]], axis=0)
    top, bottom = edge_layers(axial_edges, "axial", 1, width)
    radial_edges = jnp.concatenate([species, speed[1:2]], axis=0)
    peers = lax.axis_size("radial")
    up = [(i, i + 1) for i in range(peers - 1)]
    down = [(j, i) for i, j in up]
    high_columns, low_columns = edge_columns(radial_edges, width)
    left = lax.ppermute(high_columns, "radial", up)
    right = lax.ppermute(low_columns, "radial", down)
    faces = rows + CHUNK
    span = HALO + faces + HALO
    group = max(g for g in range(1, SPECIES_GROUP + 1) if species_count % g == 0)
    plane = pl.BlockSpec((group, rows, cols), lambda s: (s, 0, 0))
    speeds = pl.BlockSpec((2, rows, cols), lambda s: (0, 0, 0))
    edge = pl.BlockSpec((group, width, cols), lambda s: (s, 0, 0))
    edge_speed = pl.BlockSpec((1, width, cols), lambda s: (species_count, 0, 0))
    moved_rows = pl.pallas_call(
        transport_kernel,
        grid=(species_count // group,),
        in_specs=[plane, speeds] + [edge, edge_speed] * 4,
        out_specs=pl.BlockSpec((rows, species_count, cols), lambda s: (0, 0, 0)),
        out_shape=jax.ShapeDtypeStruct((rows, species_count, cols), jnp.float32),
        scratch_shapes=[
            pltpu.VMEM((span, cols), jnp.float32),
            pltpu.VMEM((span, cols), jnp.float32),
            pltpu.VMEM((span, cols), jnp.float32),
            pltpu.VMEM((faces, cols), jnp.float32),
        ],
    )(species, speed, top, top, bottom, bottom, left, left, right, right)
    return jnp.transpose(moved_rows, (1, 0, 2))


def kinetics_advance(
    starting_composition_field,
    thermal_field,
    linearized_kinetics_operator,
    frozen_jacobian_inverse_addend,
):
    acceleration_factor = jnp.exp(-ARRHENIUS_BARRIER / thermal_field)
    current = starting_composition_field
    for newton_step in range(ITERS):
        source = jnp.tensordot(
            linearized_kinetics_operator, current, axes=(1, 0), precision=CHEMISTRY_PRECISION
        ) - jnp.tanh(current)
        step = CHEM_STEP * acceleration_factor * source
        defect = -step if newton_step == 0 else current - starting_composition_field - step
        current = (
            current
            - defect
            - jnp.tensordot(frozen_jacobian_inverse_addend, defect, axes=(1, 0), precision=CHEMISTRY_PRECISION)
        )
    return current


def absorbance_profile(field, molar_absorptivity_table, spokewise_sightline_length):
    mixed = jnp.tensordot(molar_absorptivity_table, field, axes=(1, 0), precision=HIGHEST)
    return jnp.dot(mixed, spokewise_sightline_length, precision=HIGHEST)


def butterfly_sum(part, axis):
    peers, stride = (lax.axis_size(axis), 1)
    if peers & (peers - 1):
        return lax.psum(part, axis)
    while stride < peers:
        pairs = [(j, j ^ stride) for j in range(peers)]
        part = part + lax.ppermute(part, axis, pairs)
        stride *= 2
    return part


def pick_samples(blocks, first, rows):
    count, lasers, block = blocks.shape
    flat = jnp.transpose(blocks, (1, 0, 2)).reshape(lasers, count * block)
    local = rows - first * block
    cells = lax.broadcasted_iota(jnp.int32, (1, count * block, 1), 1)
    return jnp.sum(jnp.where(local[:, None, :] == cells, flat[:, :, None], 0.0), axis=1)


def sampled_profile(part, rows, axis="axial"):
    column = butterfly_sum(part, "radial")
    peers, stride = (lax.axis_size(axis), 1)
    if peers & (peers - 1):
        return pick_samples(lax.all_gather(column, axis), 0, rows)
    position = lax.axis_index(axis)
    blocks = column[None]
    values = pick_samples(blocks, position, rows)
    while stride < peers:
        pairs = [(j, j ^ stride) for j in range(peers)]
        other = lax.ppermute(blocks, axis, pairs)
        values = values + pick_samples(other, (position // stride) * stride ^ stride, rows)
        upper = (position // stride) % 2 == 1
        if 2 * stride < peers:
            blocks = jnp.where(
                upper, jnp.concatenate([other, blocks], 0), jnp.concatenate([blocks, other], 0)
            )
        stride *= 2
    return values


def local(
    composition_deviations,
    flow_speed_vector,
    thermal_field,
    linearized_kinetics_operator,
    frozen_jacobian_inverse_addend,
    rigid_block_indicator,
    molar_absorptivity_table,
    spokewise_sightline_length,
    sightline_lengthwise_index,
    observed_absorbance_traces,
):
    advected_composition_field = transport(composition_deviations, flow_speed_vector)
    combusted_composition_field = kinetics_advance(
        advected_composition_field,
        thermal_field,
        linearized_kinetics_operator,
        frozen_jacobian_inverse_addend,
    )
    flag_cells = jnp.repeat(
        jnp.repeat(rigid_block_indicator, TILE_ROWS, axis=0),
        advected_composition_field.shape[2],
        axis=1,
    )
    species_out = jnp.where(
        flag_cells[None] > 0, combusted_composition_field, advected_composition_field
    )
    path_scale = 1.0 / math.sqrt(advected_composition_field.shape[2] * lax.axis_size("radial"))
    profile = (
        absorbance_profile(species_out, molar_absorptivity_table, spokewise_sightline_length)
        * path_scale
    )
    device = lax.axis_index(("axial", "radial"))
    sample_count = observed_absorbance_traces.shape[1]
    own_rows = lax.dynamic_slice_in_dim(
        sightline_lengthwise_index, device * sample_count, sample_count, 1
    )
    values = sampled_profile(profile, own_rows)
    return (species_out, values - observed_absorbance_traces)


def solution(mesh):
    in_specs = (
        P(None, "axial", "radial"),
        P(None, "axial", "radial"),
        P("axial", "radial"),
        P(),
        P(),
        P("axial", "radial"),
        P(),
        P("radial"),
        P(),
        P(None, ("axial", "radial")),
    )
    out_specs = (P(None, "axial", "radial"), P(None, ("axial", "radial")))
    return jax.shard_map(local, mesh=mesh, in_specs=in_specs, out_specs=out_specs, check_vma=False)
```

```python
import math

import jax
import jax.numpy as jnp
from jax import lax
from jax.sharding import PartitionSpec as P
from jax.experimental import pallas as pl
from jax.experimental.pallas import tpu as pltpu

TILE_ROWS = 2
ITERS = 3


TIME_STEP = 0.4
CHEM_STEP = 0.5
ARRHENIUS_BARRIER = 1.0
WENO_EPS = 1e-06
HIGHEST = lax.Precision.HIGHEST
CHEMISTRY_PRECISION = lax.Precision.HIGH


def edge_layers(shard, axis, dim, width):
    peers, length = (lax.axis_size(axis), shard.shape[dim])
    up = [(i, i + 1) for i in range(peers - 1)]
    down = [(j, i) for i, j in up]
    last = lax.slice_in_dim(shard, length - width, length, axis=dim)
    initial = lax.slice_in_dim(shard, 0, width, axis=dim)
    return lax.ppermute(last, axis, up), lax.ppermute(initial, axis, down)


SCALED_EPS = WENO_EPS * 12.0 / 13.0
SLOPE_WEIGHT = 3.0 / 13.0


def weno_side(minus_two, minus_one, centre, plus_one, plus_two):
    curve_zero = (minus_two + centre) - (minus_one + minus_one)
    curve_one = (minus_one + plus_one) - (centre + centre)
    curve_two = (centre + plus_two) - (plus_one + plus_one)
    slope_zero = curve_zero + 2.0 * (centre - minus_one)
    slope_one = minus_one - plus_one
    slope_two = curve_two + 2.0 * (centre - plus_one)
    guard_zero = (SCALED_EPS + curve_zero * curve_zero) + SLOPE_WEIGHT * (slope_zero * slope_zero)
    guard_one = (SCALED_EPS + curve_one * curve_one) + SLOPE_WEIGHT * (slope_one * slope_one)
    guard_two = (SCALED_EPS + curve_two * curve_two) + SLOPE_WEIGHT * (slope_two * slope_two)
    guard_zero = guard_zero * guard_zero
    guard_one = guard_one * guard_one
    guard_two = guard_two * guard_two
    cross_zero = guard_one * guard_two
    cross_one = 6.0 * (guard_zero * guard_two)
    cross_two = 3.0 * (guard_zero * guard_one)
    blended = cross_zero * (curve_zero + 3.0 * slope_zero)
    blended = blended + cross_one * (curve_one - 3.0 * slope_one)
    blended = blended + cross_two * (curve_two - 3.0 * slope_two)
    return centre + blended / (12.0 * (cross_zero + cross_one + cross_two))


HALO = 8
SPECIES_GROUP = 19
CHUNK = 8


def upwind_divergence(ext_ref, vel_ref, flux_ref, rows):
    faces = flux_ref.shape[0]
    for low in range(0, faces, CHUNK):

        def cut(offset):
            return ext_ref[pl.ds(HALO - 3 + offset + low, CHUNK), :]

        face_speed = 0.5 * (
            vel_ref[pl.ds(HALO - 1 + low, CHUNK), :] + vel_ref[pl.ds(HALO + low, CHUNK), :]
        )
        forward = face_speed >= 0.0
        stencil = [
            jnp.where(forward, cut(lower), cut(upper))
            for lower, upper in ((0, 5), (1, 4), (2, 3), (3, 2), (4, 1))
        ]
        flux_ref[pl.ds(low, CHUNK), :] = face_speed * weno_side(*stencil)
    return flux_ref[pl.ds(1, rows), :] - flux_ref[pl.ds(0, rows), :]


def transport_kernel(
    field_ref, speed_ref, top_ref, top_speed_ref, bottom_ref, bottom_speed_ref,
    left_ref, left_speed_ref, right_ref, right_speed_ref, out_ref,
    ext_ref, axial_speed_ref, radial_speed_ref, flux_ref,
):
    rows, cols = field_ref.shape[1], field_ref.shape[2]
    group = field_ref.shape[0]
    fill_scratch(axial_speed_ref, top_speed_ref[0], speed_ref[0], bottom_speed_ref[0])
    fill_scratch(radial_speed_ref, left_speed_ref[0], speed_ref[1].T, right_speed_ref[0])

    def one_species(member, carry):
        field = field_ref[member]
        fill_scratch(ext_ref, top_ref[member], field, bottom_ref[member])
        along_axial = upwind_divergence(ext_ref, axial_speed_ref, flux_ref, rows)
        fill_scratch(ext_ref, left_ref[member], field.T, right_ref[member])
        along_radial = upwind_divergence(ext_ref, radial_speed_ref, flux_ref, cols).T
        moved = field - TIME_STEP * (along_axial + along_radial)
        out_ref[:, pl.ds(pl.program_id(0) * group + member, 1), :] = moved[:, None, :]
        return carry

    lax.fori_loop(0, group, one_species, 0)


def fill_scratch(scratch, before, body, after):
    span, cols = scratch.shape
    width, rows = (before.shape[0], body.shape[0])
    scratch[pl.ds(0, HALO), :] = jnp.zeros((HALO, cols), jnp.float32)
    scratch[pl.ds(HALO + rows, span - HALO - rows), :] = jnp.zeros(
        (span - HALO - rows, cols), jnp.float32
    )
    scratch[pl.ds(HALO - width, width), :] = before
    scratch[pl.ds(HALO, rows), :] = body
    scratch[pl.ds(HALO + rows, width), :] = after


def edge_columns(field, width):
    cols = field.shape[2]
    row = lax.broadcasted_iota(jnp.int32, (2 * width, cols), 0)
    column = lax.broadcasted_iota(jnp.int32, (2 * width, cols), 1)
    pick = column == jnp.where(row < width, row + cols - width, row - width)
    picked = jnp.einsum("kr,sar->ska", pick.astype(field.dtype), field, precision=HIGHEST)
    return picked[:, :width], picked[:, width:]


def transport(species, speed, width=3):
    species_count, rows, cols = species.shape
    assert rows == cols and rows % CHUNK == 0
    axial_edges = jnp.concatenate([species, speed[0:1]], axis=0)
    top, bottom = edge_layers(axial_edges, "axial", 1, width)
    radial_edges = jnp.concatenate([species, speed[1:2]], axis=0)
    peers = lax.axis_size("radial")
    up = [(i, i + 1) for i in range(peers - 1)]
    down = [(j, i) for i, j in up]
    high_columns, low_columns = edge_columns(radial_edges, width)
    left = lax.ppermute(high_columns, "radial", up)
    right = lax.ppermute(low_columns, "radial", down)
    faces = rows + CHUNK
    span = HALO + faces + HALO
    group = max(g for g in range(1, SPECIES_GROUP + 1) if species_count % g == 0)
    plane = pl.BlockSpec((group, rows, cols), lambda s: (s, 0, 0))
    speeds = pl.BlockSpec((2, rows, cols), lambda s: (0, 0, 0))
    edge = pl.BlockSpec((group, width, cols), lambda s: (s, 0, 0))
    edge_speed = pl.BlockSpec((1, width, cols), lambda s: (species_count, 0, 0))
    moved_rows = pl.pallas_call(
        transport_kernel,
        grid=(species_count // group,),
        in_specs=[plane, speeds] + [edge, edge_speed] * 4,
        out_specs=pl.BlockSpec((rows, species_count, cols), lambda s: (0, 0, 0)),
        out_shape=jax.ShapeDtypeStruct((rows, species_count, cols), jnp.float32),
        scratch_shapes=[
            pltpu.VMEM((span, cols), jnp.float32),
            pltpu.VMEM((span, cols), jnp.float32),
            pltpu.VMEM((span, cols), jnp.float32),
            pltpu.VMEM((faces, cols), jnp.float32),
        ],
    )(species, speed, top, top, bottom, bottom, left, left, right, right)
    return jnp.transpose(moved_rows, (1, 0, 2))


def kinetics_advance(
    starting_composition_field,
    thermal_field,
    linearized_kinetics_operator,
    frozen_jacobian_inverse_addend,
):
    acceleration_factor = jnp.exp(-ARRHENIUS_BARRIER / thermal_field)
    current = starting_composition_field
    for newton_step in range(ITERS):
        source = jnp.tensordot(
            linearized_kinetics_operator, current, axes=(1, 0), precision=CHEMISTRY_PRECISION
        ) - jnp.tanh(current)
        step = CHEM_STEP * acceleration_factor * source
        defect = -step if newton_step == 0 else current - starting_composition_field - step
        current = (
            current
            - defect
            - jnp.tensordot(frozen_jacobian_inverse_addend, defect, axes=(1, 0), precision=CHEMISTRY_PRECISION)
        )
    return current


def absorbance_profile(field, molar_absorptivity_table, spokewise_sightline_length):
    mixed = jnp.tensordot(molar_absorptivity_table, field, axes=(1, 0), precision=CHEMISTRY_PRECISION)
    return jnp.dot(mixed, spokewise_sightline_length, precision=CHEMISTRY_PRECISION)


def butterfly_sum(part, axis):
    peers, stride = (lax.axis_size(axis), 1)
    if peers & (peers - 1):
        return lax.psum(part, axis)
    while stride < peers:
        pairs = [(j, j ^ stride) for j in range(peers)]
        part = part + lax.ppermute(part, axis, pairs)
        stride *= 2
    return part


def pick_samples(blocks, first, rows):
    count, lasers, block = blocks.shape
    flat = jnp.transpose(blocks, (1, 0, 2)).reshape(lasers, count * block)
    local = rows - first * block
    cells = lax.broadcasted_iota(jnp.int32, (1, count * block, 1), 1)
    return jnp.sum(jnp.where(local[:, None, :] == cells, flat[:, :, None], 0.0), axis=1)


def sampled_profile(part, rows, axis="axial"):
    column = butterfly_sum(part, "radial")
    peers, stride = (lax.axis_size(axis), 1)
    if peers & (peers - 1):
        return pick_samples(lax.all_gather(column, axis), 0, rows)
    position = lax.axis_index(axis)
    blocks = column[None]
    values = pick_samples(blocks, position, rows)
    while stride < peers:
        pairs = [(j, j ^ stride) for j in range(peers)]
        other = lax.ppermute(blocks, axis, pairs)
        values = values + pick_samples(other, (position // stride) * stride ^ stride, rows)
        upper = (position // stride) % 2 == 1
        if 2 * stride < peers:
            blocks = jnp.where(
                upper, jnp.concatenate([other, blocks], 0), jnp.concatenate([blocks, other], 0)
            )
        stride *= 2
    return values


def local(
    composition_deviations,
    flow_speed_vector,
    thermal_field,
    linearized_kinetics_operator,
    frozen_jacobian_inverse_addend,
    rigid_block_indicator,
    molar_absorptivity_table,
    spokewise_sightline_length,
    sightline_lengthwise_index,
    observed_absorbance_traces,
):
    advected_composition_field = transport(composition_deviations, flow_speed_vector)
    combusted_composition_field = kinetics_advance(
        advected_composition_field,
        thermal_field,
        linearized_kinetics_operator,
        frozen_jacobian_inverse_addend,
    )
    flag_cells = jnp.repeat(
        jnp.repeat(rigid_block_indicator, TILE_ROWS, axis=0),
        advected_composition_field.shape[2],
        axis=1,
    )
    species_out = jnp.where(
        flag_cells[None] > 0, combusted_composition_field, advected_composition_field
    )
    path_scale = 1.0 / math.sqrt(advected_composition_field.shape[2] * lax.axis_size("radial"))
    profile = (
        absorbance_profile(species_out, molar_absorptivity_table, spokewise_sightline_length)
        * path_scale
    )
    device = lax.axis_index(("axial", "radial"))
    sample_count = observed_absorbance_traces.shape[1]
    own_rows = lax.dynamic_slice_in_dim(
        sightline_lengthwise_index, device * sample_count, sample_count, 1
    )
    values = sampled_profile(profile, own_rows)
    return (species_out, values - observed_absorbance_traces)


def solution(mesh):
    in_specs = (
        P(None, "axial", "radial"),
        P(None, "axial", "radial"),
        P("axial", "radial"),
        P(),
        P(),
        P("axial", "radial"),
        P(),
        P("radial"),
        P(),
        P(None, ("axial", "radial")),
    )
    out_specs = (P(None, "axial", "radial"), P(None, ("axial", "radial")))
    return jax.shard_map(local, mesh=mesh, in_specs=in_specs, out_specs=out_specs, check_vma=False)
```

```python
import math

import jax
import jax.numpy as jnp
from jax import lax
from jax.sharding import PartitionSpec as P
from jax.experimental import pallas as pl
from jax.experimental.pallas import tpu as pltpu

TILE_ROWS = 2
ITERS = 3


TIME_STEP = 0.4
CHEM_STEP = 0.5
ARRHENIUS_BARRIER = 1.0
WENO_EPS = 1e-06
HIGHEST = lax.Precision.HIGHEST
CHEMISTRY_PRECISION = lax.Precision.HIGH


def edge_layers(shard, axis, dim, width):
    peers, length = (lax.axis_size(axis), shard.shape[dim])
    up = [(i, i + 1) for i in range(peers - 1)]
    down = [(j, i) for i, j in up]
    last = lax.slice_in_dim(shard, length - width, length, axis=dim)
    initial = lax.slice_in_dim(shard, 0, width, axis=dim)
    return lax.ppermute(last, axis, up), lax.ppermute(initial, axis, down)


SCALED_EPS = WENO_EPS * 12.0 / 13.0
SLOPE_WEIGHT = 3.0 / 13.0


def weno_side(minus_two, minus_one, centre, plus_one, plus_two):
    curve_zero = (minus_two + centre) - (minus_one + minus_one)
    curve_one = (minus_one + plus_one) - (centre + centre)
    curve_two = (centre + plus_two) - (plus_one + plus_one)
    slope_zero = curve_zero + 2.0 * (centre - minus_one)
    slope_one = minus_one - plus_one
    slope_two = curve_two + 2.0 * (centre - plus_one)
    guard_zero = (SCALED_EPS + curve_zero * curve_zero) + SLOPE_WEIGHT * (slope_zero * slope_zero)
    guard_one = (SCALED_EPS + curve_one * curve_one) + SLOPE_WEIGHT * (slope_one * slope_one)
    guard_two = (SCALED_EPS + curve_two * curve_two) + SLOPE_WEIGHT * (slope_two * slope_two)
    guard_zero = guard_zero * guard_zero
    guard_one = guard_one * guard_one
    guard_two = guard_two * guard_two
    cross_zero = guard_one * guard_two
    cross_one = 6.0 * (guard_zero * guard_two)
    cross_two = 3.0 * (guard_zero * guard_one)
    blended = cross_zero * (curve_zero + 3.0 * slope_zero)
    blended = blended + cross_one * (curve_one - 3.0 * slope_one)
    blended = blended + cross_two * (curve_two - 3.0 * slope_two)
    return centre + blended / (12.0 * (cross_zero + cross_one + cross_two))


HALO = 8
SPECIES_GROUP = 19
CHUNK = 16


def upwind_divergence(ext_ref, vel_ref, flux_ref, rows):
    faces = flux_ref.shape[0]
    for low in range(0, faces, CHUNK):

        def cut(offset):
            return ext_ref[pl.ds(HALO - 3 + offset + low, CHUNK), :]

        face_speed = 0.5 * (
            vel_ref[pl.ds(HALO - 1 + low, CHUNK), :] + vel_ref[pl.ds(HALO + low, CHUNK), :]
        )
        forward = face_speed >= 0.0
        stencil = [
            jnp.where(forward, cut(lower), cut(upper))
            for lower, upper in ((0, 5), (1, 4), (2, 3), (3, 2), (4, 1))
        ]
        flux_ref[pl.ds(low, CHUNK), :] = face_speed * weno_side(*stencil)
    return flux_ref[pl.ds(1, rows), :] - flux_ref[pl.ds(0, rows), :]


def transport_kernel(
    field_ref, speed_ref, top_ref, top_speed_ref, bottom_ref, bottom_speed_ref,
    left_ref, left_speed_ref, right_ref, right_speed_ref, out_ref,
    ext_ref, axial_speed_ref, radial_speed_ref, flux_ref,
):
    rows, cols = field_ref.shape[1], field_ref.shape[2]
    group = field_ref.shape[0]
    fill_scratch(axial_speed_ref, top_speed_ref[0], speed_ref[0], bottom_speed_ref[0])
    fill_scratch(radial_speed_ref, left_speed_ref[0], speed_ref[1].T, right_speed_ref[0])

    def one_species(member, carry):
        field = field_ref[member]
        fill_scratch(ext_ref, top_ref[member], field, bottom_ref[member])
        along_axial = upwind_divergence(ext_ref, axial_speed_ref, flux_ref, rows)
        fill_scratch(ext_ref, left_ref[member], field.T, right_ref[member])
        along_radial = upwind_divergence(ext_ref, radial_speed_ref, flux_ref, cols).T
        moved = field - TIME_STEP * (along_axial + along_radial)
        out_ref[:, pl.ds(pl.program_id(0) * group + member, 1), :] = moved[:, None, :]
        return carry

    lax.fori_loop(0, group, one_species, 0)


def fill_scratch(scratch, before, body, after):
    span, cols = scratch.shape
    width, rows = (before.shape[0], body.shape[0])
    scratch[pl.ds(0, HALO), :] = jnp.zeros((HALO, cols), jnp.float32)
    scratch[pl.ds(HALO + rows, span - HALO - rows), :] = jnp.zeros(
        (span - HALO - rows, cols), jnp.float32
    )
    scratch[pl.ds(HALO - width, width), :] = before
    scratch[pl.ds(HALO, rows), :] = body
    scratch[pl.ds(HALO + rows, width), :] = after


def edge_columns(field, width):
    cols = field.shape[2]
    row = lax.broadcasted_iota(jnp.int32, (2 * width, cols), 0)
    column = lax.broadcasted_iota(jnp.int32, (2 * width, cols), 1)
    pick = column == jnp.where(row < width, row + cols - width, row - width)
    picked = jnp.einsum("kr,sar->ska", pick.astype(field.dtype), field, precision=HIGHEST)
    return picked[:, :width], picked[:, width:]


def transport(species, speed, width=3):
    species_count, rows, cols = species.shape
    assert rows == cols and rows % CHUNK == 0
    axial_edges = jnp.concatenate([species, speed[0:1]], axis=0)
    top, bottom = edge_layers(axial_edges, "axial", 1, width)
    radial_edges = jnp.concatenate([species, speed[1:2]], axis=0)
    peers = lax.axis_size("radial")
    up = [(i, i + 1) for i in range(peers - 1)]
    down = [(j, i) for i, j in up]
    high_columns, low_columns = edge_columns(radial_edges, width)
    left = lax.ppermute(high_columns, "radial", up)
    right = lax.ppermute(low_columns, "radial", down)
    faces = rows + CHUNK
    span = HALO + faces + HALO
    group = max(g for g in range(1, SPECIES_GROUP + 1) if species_count % g == 0)
    plane = pl.BlockSpec((group, rows, cols), lambda s: (s, 0, 0))
    speeds = pl.BlockSpec((2, rows, cols), lambda s: (0, 0, 0))
    edge = pl.BlockSpec((group, width, cols), lambda s: (s, 0, 0))
    edge_speed = pl.BlockSpec((1, width, cols), lambda s: (species_count, 0, 0))
    moved_rows = pl.pallas_call(
        transport_kernel,
        grid=(species_count // group,),
        in_specs=[plane, speeds] + [edge, edge_speed] * 4,
        out_specs=pl.BlockSpec((rows, species_count, cols), lambda s: (0, 0, 0)),
        out_shape=jax.ShapeDtypeStruct((rows, species_count, cols), jnp.float32),
        scratch_shapes=[
            pltpu.VMEM((span, cols), jnp.float32),
            pltpu.VMEM((span, cols), jnp.float32),
            pltpu.VMEM((span, cols), jnp.float32),
            pltpu.VMEM((faces, cols), jnp.float32),
        ],
    )(species, speed, top, top, bottom, bottom, left, left, right, right)
    return jnp.transpose(moved_rows, (1, 0, 2))


def kinetics_advance(
    starting_composition_field,
    thermal_field,
    linearized_kinetics_operator,
    frozen_jacobian_inverse_addend,
):
    acceleration_factor = jnp.exp(-ARRHENIUS_BARRIER / thermal_field)
    current = starting_composition_field
    for newton_step in range(ITERS):
        source = jnp.tensordot(
            linearized_kinetics_operator, current, axes=(1, 0), precision=CHEMISTRY_PRECISION
        ) - jnp.tanh(current)
        step = CHEM_STEP * acceleration_factor * source
        defect = -step if newton_step == 0 else current - starting_composition_field - step
        current = (
            current
            - defect
            - jnp.tensordot(frozen_jacobian_inverse_addend, defect, axes=(1, 0), precision=CHEMISTRY_PRECISION)
        )
    return current


def absorbance_profile(field, molar_absorptivity_table, spokewise_sightline_length):
    mixed = jnp.tensordot(molar_absorptivity_table, field, axes=(1, 0), precision=HIGHEST)
    return jnp.dot(mixed, spokewise_sightline_length, precision=HIGHEST)


def butterfly_sum(part, axis):
    peers, stride = (lax.axis_size(axis), 1)
    if peers & (peers - 1):
        return lax.psum(part, axis)
    while stride < peers:
        pairs = [(j, j ^ stride) for j in range(peers)]
        part = part + lax.ppermute(part, axis, pairs)
        stride *= 2
    return part


def pick_samples(blocks, first, rows):
    count, lasers, block = blocks.shape
    flat = jnp.transpose(blocks, (1, 0, 2)).reshape(lasers, count * block)
    local = rows - first * block
    cells = lax.broadcasted_iota(jnp.int32, (1, count * block, 1), 1)
    return jnp.sum(jnp.where(local[:, None, :] == cells, flat[:, :, None], 0.0), axis=1)


def sampled_profile(part, rows, axis="axial"):
    column = butterfly_sum(part, "radial")
    peers, stride = (lax.axis_size(axis), 1)
    if peers & (peers - 1):
        return pick_samples(lax.all_gather(column, axis), 0, rows)
    position = lax.axis_index(axis)
    blocks = column[None]
    values = pick_samples(blocks, position, rows)
    while stride < peers:
        pairs = [(j, j ^ stride) for j in range(peers)]
        other = lax.ppermute(blocks, axis, pairs)
        values = values + pick_samples(other, (position // stride) * stride ^ stride, rows)
        upper = (position // stride) % 2 == 1
        if 2 * stride < peers:
            blocks = jnp.where(
                upper, jnp.concatenate([other, blocks], 0), jnp.concatenate([blocks, other], 0)
            )
        stride *= 2
    return values


def local(
    composition_deviations,
    flow_speed_vector,
    thermal_field,
    linearized_kinetics_operator,
    frozen_jacobian_inverse_addend,
    rigid_block_indicator,
    molar_absorptivity_table,
    spokewise_sightline_length,
    sightline_lengthwise_index,
    observed_absorbance_traces,
):
    advected_composition_field = transport(composition_deviations, flow_speed_vector)
    combusted_composition_field = kinetics_advance(
        advected_composition_field,
        thermal_field,
        linearized_kinetics_operator,
        frozen_jacobian_inverse_addend,
    )
    flag_cells = jnp.repeat(
        jnp.repeat(rigid_block_indicator, TILE_ROWS, axis=0),
        advected_composition_field.shape[2],
        axis=1,
    )
    species_out = jnp.where(
        flag_cells[None] > 0, combusted_composition_field, advected_composition_field
    )
    path_scale = 1.0 / math.sqrt(advected_composition_field.shape[2] * lax.axis_size("radial"))
    profile = (
        absorbance_profile(species_out, molar_absorptivity_table, spokewise_sightline_length)
        * path_scale
    )
    device = lax.axis_index(("axial", "radial"))
    sample_count = observed_absorbance_traces.shape[1]
    own_rows = lax.dynamic_slice_in_dim(
        sightline_lengthwise_index, device * sample_count, sample_count, 1
    )
    values = sampled_profile(profile, own_rows)
    return (species_out, values - observed_absorbance_traces)


def solution(mesh):
    in_specs = (
        P(None, "axial", "radial"),
        P(None, "axial", "radial"),
        P("axial", "radial"),
        P(),
        P(),
        P("axial", "radial"),
        P(),
        P("radial"),
        P(),
        P(None, ("axial", "radial")),
    )
    out_specs = (P(None, "axial", "radial"), P(None, ("axial", "radial")))
    return jax.shard_map(local, mesh=mesh, in_specs=in_specs, out_specs=out_specs, check_vma=False)
```
